32 devices in a mesh: expert: 8 (over z, y), shard: 4 (over x, core).
Axes of the slice: x: 2, y: 2, z: 4, core: 2. Of those that a mesh axis runs over, the one named last changes fastest.
Arguments:
- tokens: float32 [25216, 512], P(('expert', 'shard')), may hold values from -6 to 6
- routes: int32 [25216, 2], P(('expert', 'shard')), may hold values from 0 to 7, all different within a row; in each aligned block of 394 rows (0 to 393, 394 to 787, ...) at most 192 rows name the same one
- priority: int32 [25216], P(('expert', 'shard')), may hold values from 0 to 393, as said below
- norm_gain: bfloat16 [2, 2, 512], P(None, None, 'shard'), may hold values from 0.5 to 1.5
- norm_bias: bfloat16 [2, 2, 512], P(None, None, 'shard'), may hold values from -1 to 1
- w_qkv: bfloat16 [2, 512, 1536], P(None, 'shard'), may hold values from -0.25 to 0.25
- w_proj: bfloat16 [2, 512, 512], P(None, 'shard'), may hold values from -2 to 2
- w_router: bfloat16 [2, 512, 8], P(None, 'shard'), may hold values from -0.1875 to 0.1875
- exp_in: bfloat16 [2, 8, 512, 2048], P(None, 'expert', 'shard'), may hold values from -0.25 to 0.25
- exp_out: bfloat16 [2, 8, 2048, 512], P(None, 'expert', 'shard'), may hold values from -0.875 to 0.875
- cotangent: float32 [25216, 512], P(('expert', 'shard')), may hold values from -6 to 6
Outputs:
- activations: float32 [25216, 512], P(('expert', 'shard'))
- d_tokens: float32 [25216, 512], P(('expert', 'shard'))
- grad_gain: float32 [2, 2, 512], P(None, None, 'shard')
- grad_bias: float32 [2, 2, 512], P(None, None, 'shard')
- grad_qkv: float32 [2, 512, 1536], P(None, 'shard')
- grad_proj: float32 [2, 512, 512], P(None, 'shard')
- grad_router: float32 [2, 512, 8], P(None, 'shard')
- grad_exp_in: float32 [2, 8, 512, 2048], P(None, 'expert', 'shard')
- grad_exp_out: float32 [2, 8, 2048, 512], P(None, 'expert', 'shard')
The draws below stay inside these ranges and needn't reach their ends.
Inputs may be any that keep to these rules, and one draw needn't show every extreme that they name: `routes`: each row names 2 different experts; in each aligned block of 394 rows no expert is named by more than 192 rows. `priority`: in each aligned block of 394 rows the values are a permutation of 0 to 393.
All inputs are finite; a program needn't handle non-finite values.
Results may differ from the reference program's by a relative error of at most 0.025.
Values may be sent and summed in bfloat16 or wider, within the bound.
No kernel may reach another device: no remote copies, remote signals or barrier semaphores. Data moves between devices by JAX's collectives and lax.ppermute only.
A program may use at most 256 MiB of HBM per device.

```python
import math
import jax
import jax.numpy as jnp
import numpy as np
from jax import lax

D = 512
HEADS = 8
HEAD = 64
HIDDEN_SIZE = 2048
EXPERTS = 8
SEQ = 197
SEQ_MB = 2
MICRO = 2
LAYERS = 2
TOP = 2
TOK_MB = 394
TOKENS = 25216
CAP = 128
MOST = 192


def draw_priority(key, part):
    blocks = TOKENS // TOK_MB
    block_keys = jax.random.split(key, blocks)
    ranks = jax.vmap(lambda one_key: jax.random.permutation(one_key, TOK_MB))(block_keys)
    return ranks.reshape(blocks * TOK_MB).astype(jnp.int32)


def block_levels(own_key, dims, shards, least, high):
    gain, own = 1.0, jax.random.fold_in(own_key, 6)
    for axis_at, blocks in shards:
        heights = jnp.exp(jax.random.uniform(jax.random.fold_in(own, axis_at), (blocks,), jnp.float32, least / len(shards), high / len(shards)))
        gain = gain * jnp.repeat(heights, dims[axis_at] // blocks).reshape([-1 if axis == axis_at else 1 for axis in range(len(dims))])
    return gain


def assign_block(key, own, number, rows, amount, top, reach, skew):
    sequence = jax.random.permutation(key, amount)
    heavy_load, usual = load_shares(amount, rows * top, reach, skew, True), load_shares(amount, rows * top, reach, skew, False)
    places = jnp.arange(amount)

    def named(sizes, rotation):
        used = int((sizes > 0).sum())
        fixed = max(1, used // 4)
        passed = fixed + (places - fixed + rotation * (used - fixed)) % max(1, amount - fixed)
        return jnp.zeros((amount,), jnp.int32).at[sequence[jnp.where(places < fixed, places, passed)]].set(jnp.asarray(sizes, jnp.int32))

    sizes = jnp.where(number % 4 == 0, named(heavy_load, number // 4), named(usual, number - number // 4 - 1))
    mixed = jax.random.permutation(jax.random.fold_in(own, 3), amount)
    source_of, sink = mixed[0:amount // 2 * 2:2], mixed[1:amount // 2 * 2:2]
    room = jnp.minimum(sizes[source_of] - 1, reach - sizes[sink]) // 2
    room = jnp.where((source_of == sequence[0]) | (sink == sequence[0]) | (sizes[sink] == 0), 0, jnp.maximum(room, 0))
    passed = jax.random.randint(jax.random.fold_in(own, 4), (amount // 2,), 0, 1 << 20) % (room + 1)
    sizes = sizes.at[source_of].add(-passed).at[sink].add(passed)
    members = jnp.searchsorted(jnp.cumsum(sizes), jnp.arange(rows * top), side="right").astype(jnp.int32)
    grid = members.reshape(top, rows).T
    grid = grid[jax.random.permutation(jax.random.fold_in(own, 1), rows)]
    rotation = jax.random.randint(jax.random.fold_in(own, 2), (rows, 1), 0, top)
    return jnp.take_along_axis(grid, (jnp.arange(top)[None, :] + rotation) % top, axis=1)


def load_shares(count, total, limit, lean, full):
    portions = [(1 << 20) // math.isqrt(standing ** lean) + 1 for standing in range(1, count + 1)]
    largest = limit if full else min(limit, max(-(-total // count), total * portions[0] // sum(portions)))
    least = 1 if total - largest >= count - 1 else 0
    holding, rest = [largest] + [least] * (count - 1), total - largest - least * (count - 1)
    while rest > 0:
        free = [i for i in range(1, count) if holding[i] < largest] or [i for i in range(1, count) if holding[i] < limit]
        mass, remaining = sum([portions[i] for i in free]), rest
        for i in free:
            more = min(limit - holding[i], max(1, remaining * portions[i] // mass), rest)
            holding[i] = holding[i] + more
            rest = rest - more
    return np.array(holding)


def scatter_about(rng, extent, width, most, pieces=(), kind=jnp.bfloat16):
    level = block_levels(rng, extent, pieces, -0.22, 0.18) if pieces else 1.0
    values = jax.random.normal(rng, extent, jnp.float32) * width * level
    return jnp.minimum(jnp.maximum(values, -most), most).astype(kind)


def setup_inputs(seed: int = 0) -> dict:
    key_list = jax.random.split(jax.random.key(seed), 12)
    tokens = scatter_about(key_list[0], (TOKENS, D), 1.0, 6.0, ((0, 32),), jnp.float32)
    routes_keys = jax.random.split(jax.random.fold_in(key_list[1], 1), TOKENS // TOK_MB)
    routes_turns = jax.random.permutation(jax.random.fold_in(key_list[1], 3), TOKENS // TOK_MB)
    routes = jax.vmap(lambda own, number: assign_block(jax.random.fold_in(key_list[1], 2), own, number, TOK_MB, EXPERTS, TOP, MOST, 2))(routes_keys, routes_turns).reshape((TOKENS, TOP))
    priority = draw_priority(jax.random.fold_in(key_list[11], 71), 0)
    norm_gain = jnp.clip(1.0 + 0.1 * jax.random.normal(key_list[3], (LAYERS, 2, D), jnp.float32), 0.5, 1.5).astype(jnp.bfloat16)
    norm_bias = scatter_about(key_list[4], (LAYERS, 2, D), 0.2, 1.0, ((2, 4),))
    w_qkv = scatter_about(key_list[5], (LAYERS, D, 3 * D), D ** -0.5, 0.25, ((1, 4),))
    w_proj = scatter_about(key_list[6], (LAYERS, D, D), (D * 4 // SEQ) ** -0.5, 2.0, ((1, 4),))
    w_router = scatter_about(key_list[7], (LAYERS, D, EXPERTS), (2 * D) ** -0.5, 0.1875, ((1, 4),))
    exp_in = scatter_about(key_list[8], (LAYERS, EXPERTS, D, HIDDEN_SIZE), D ** -0.5, 0.25, ((1, 8), (2, 4)))
    exp_out = scatter_about(key_list[9], (LAYERS, EXPERTS, HIDDEN_SIZE, D), (max(HIDDEN_SIZE * 8 // (5 * EXPERTS * EXPERTS), 1)) ** -0.5, 0.875, ((1, 8), (2, 4)))
    cotangent = scatter_about(key_list[10], (TOKENS, D), 1.0, 6.0, ((0, 32),), jnp.float32)
    return dict(tokens=tokens, routes=routes, priority=priority, norm_gain=norm_gain, norm_bias=norm_bias, w_qkv=w_qkv, w_proj=w_proj, w_router=w_router, exp_in=exp_in, exp_out=exp_out, cotangent=cotangent)


@jax.custom_vjp
def low(v):
    return lax.optimization_barrier(v.astype(jnp.bfloat16)).astype(jnp.float32)

@jax.custom_vjp
def low_back(v):
    return v

def low_keep(v):
    return (low(v), None)

def low_pass(kept, grad):
    return (grad,)

def back_keep(v):
    return (v, None)

def back_low(kept, grad):
    return (low(grad),)
low.defvjp(low_keep, low_pass)
low_back.defvjp(back_keep, back_low)
norm_eps = 1e-06

def dot_high(left, right):
    return jnp.dot(left, right, precision=lax.Precision.HIGHEST, preferred_element_type=jnp.float32)

def layer_norm(values, norm_scale, norm_shift):
    centre = values - lax.optimization_barrier(jnp.mean(values, axis=-1, keepdims=True))
    spread = lax.optimization_barrier(jnp.mean(centre * centre, axis=-1, keepdims=True))
    return centre * lax.rsqrt(spread + norm_eps) * norm_scale + norm_shift

def slot_tables(route_ids, prio_rank, experts, capacity):
    tok_count = route_ids.shape[0]
    order_key = jnp.concatenate([prio_rank, prio_rank + tok_count]).astype(jnp.int32)
    pair_expert = jnp.concatenate([route_ids[:, 0], route_ids[:, 1]]).astype(jnp.int32)
    same_expert = pair_expert[:, None] == pair_expert[None, :]
    earlier = order_key[None, :] < order_key[:, None]
    position = lax.optimization_barrier(jnp.sum((same_expert & earlier).astype(jnp.int32), axis=1)).astype(jnp.int32)
    kept_mask = position < capacity
    flat_slot = jnp.where(kept_mask, pair_expert * capacity + position, experts * capacity).astype(jnp.int32)
    pair_ids = jnp.arange(2 * tok_count, dtype=jnp.int32)
    slot_pair = jnp.full((experts * capacity + 1,), 2 * tok_count, jnp.int32).at[flat_slot].set(pair_ids)
    slot_pair = slot_pair[:experts * capacity]
    slot_token = jnp.where(slot_pair < 2 * tok_count, slot_pair % tok_count, tok_count).astype(jnp.int32)
    return (flat_slot, slot_pair, slot_token, kept_mask)

def attend(seq_group):
    score_scale = HEAD ** (-0.5)
    query_heads = seq_group[:, :, 0]
    key_heads = seq_group[:, :, 1]
    value_heads = seq_group[:, :, 2]
    scores = low_back(jnp.einsum('sqhd,skhd->shqk', query_heads, key_heads, precision=lax.Precision.HIGHEST) * score_scale)
    soft_scores = low(jax.nn.softmax(scores, axis=-1))
    return jnp.einsum('shqk,skhd->sqhd', soft_scores, value_heads, precision=lax.Precision.HIGHEST)

def expert_mlp(operands):
    row_block, weight_in, weight_out = operands
    hidden_pre = low_back(dot_high(row_block, weight_in))
    hidden_act = low(jax.nn.gelu(hidden_pre, approximate=True))
    return low_back(low(dot_high(hidden_act, weight_out)))

def take_rows(row_table, index):
    return row_table[index]

def reference(tokens, routes, priority, norm_gain, norm_bias, w_qkv, w_proj, w_router, exp_in, exp_out, cotangent):
    blocks = TOKENS // TOK_MB
    table_fn = lambda route_block, prio_block: slot_tables(route_block, prio_block, EXPERTS, CAP)
    flat_slot, slot_pair, slot_token, kept_mask = jax.vmap(table_fn)(routes.reshape(blocks, TOK_MB, TOP), priority.reshape(blocks, TOK_MB))
    kept_gate = kept_mask.astype(jnp.float32).reshape(blocks, TOP, TOK_MB)
    route_hot = (routes[:, :, None] == jnp.arange(EXPERTS, dtype=jnp.int32)[None, None, :]).astype(jnp.float32)

    def block(residual, layer_index, norm_gains, norm_shifts, qkv_w, proj_w, router_w, in_w, out_w):
        tok_count = residual.shape[0]
        normed = low(layer_norm(residual, norm_gains[layer_index, 0], norm_shifts[layer_index, 0]))
        qkv_rows = low_back(low(dot_high(normed, qkv_w[layer_index])))
        group_count = tok_count // (SEQ * SEQ_MB * MICRO)
        grouped = qkv_rows.reshape(group_count, SEQ_MB * MICRO, SEQ, 3, HEADS, HEAD)
        mixed_heads = lax.map(jax.checkpoint(attend), grouped).reshape(tok_count, D)
        mixed_heads = low_back(low(mixed_heads))
        middle = residual + low_back(dot_high(mixed_heads, proj_w[layer_index]))
        normed_two = low(layer_norm(middle, norm_gains[layer_index, 1], norm_shifts[layer_index, 1]))
        gate_probs = jax.nn.softmax(low_back(dot_high(normed_two, router_w[layer_index])), axis=-1)
        padded = jnp.concatenate([normed_two.reshape(blocks, TOK_MB, D), jnp.zeros((blocks, 1, D), jnp.float32)], axis=1)
        dispatched = jax.vmap(take_rows)(padded, slot_token)
        received = dispatched.reshape(blocks, EXPERTS, CAP, D).transpose(1, 0, 2, 3).reshape(EXPERTS, blocks * CAP, D)
        received = low_back(received)
        results = lax.map(jax.checkpoint(expert_mlp), (received, in_w[layer_index], out_w[layer_index]))
        back_rows = results.reshape(EXPERTS, blocks, CAP, D).transpose(1, 0, 2, 3).reshape(blocks, EXPERTS * CAP, D)
        back_rows = jnp.concatenate([back_rows, jnp.zeros((blocks, 1, D), jnp.float32)], axis=1)
        pair_rows = jax.vmap(take_rows)(back_rows, flat_slot).reshape(blocks, TOP, TOK_MB, D)
        chosen = lax.optimization_barrier(jnp.sum(route_hot * gate_probs[:, None, :], axis=-1))
        weight_pair = kept_gate * chosen.reshape(blocks, TOK_MB, TOP).transpose(0, 2, 1)
        combined = lax.optimization_barrier(jnp.sum(weight_pair[:, :, :, None] * pair_rows, axis=1))
        return middle + combined.reshape(tok_count, D)

    def forward(norm_gains, norm_shifts, qkv_w, proj_w, router_w, in_w, out_w, residual):
        for layer_index in range(LAYERS):
            residual = block(residual, layer_index, norm_gains, norm_shifts, qkv_w, proj_w, router_w, in_w, out_w)
        return residual
    result, pullback = jax.vjp(forward, norm_gain.astype(jnp.float32), norm_bias.astype(jnp.float32), w_qkv.astype(jnp.float32), w_proj.astype(jnp.float32), w_router.astype(jnp.float32), exp_in.astype(jnp.float32), exp_out.astype(jnp.float32), tokens)
    gradients = pullback(cotangent)
    return (result, gradients[7], gradients[0], gradients[1], gradients[2], gradients[3], gradients[4], gradients[5], gradients[6])
```

```python
import jax
import jax.numpy as jnp
from jax import lax
from jax.sharding import PartitionSpec as P

D = 512
HEADS = 8
HEAD = 64
HIDDEN_SIZE = 2048
EXP_DEV = 1
SEQ = 197
MICRO = 2
LAYERS = 2
TOP = 2
TOK_MB = 394


norm_eps = 1e-06


def layer_norm(values, norm_scale, norm_shift):
    centre = values - jnp.mean(values, axis=-1, keepdims=True)
    spread = jnp.mean(centre * centre, axis=-1, keepdims=True)
    return centre * lax.rsqrt(spread + norm_eps) * norm_scale + norm_shift


def gelu_tanh(values):
    return jax.nn.gelu(values, approximate=True)


def dot_first(left, right):
    return lax.dot_general(
        left, right, (((0,), (0,)), ((), ())), preferred_element_type=jnp.float32
    )


def dot_last(left, right):
    return lax.dot_general(
        left, right, (((1,), (1,)), ((), ())), preferred_element_type=jnp.float32
    )


def slot_tables(route_ids, prio_rank, experts, capacity):
    tok_count = route_ids.shape[0]
    order_key = jnp.concatenate([prio_rank, prio_rank + tok_count])
    pair_expert = jnp.concatenate([route_ids[:, 0], route_ids[:, 1]])
    same_expert = pair_expert[:, None] == pair_expert[None, :]
    earlier = order_key[None, :] < order_key[:, None]
    position = jnp.sum((same_expert & earlier).astype(jnp.int32), axis=1)
    kept_mask = position < capacity
    flat_slot = jnp.where(kept_mask, pair_expert * capacity + position, experts * capacity)
    pair_ids = jnp.arange(2 * tok_count, dtype=jnp.int32)
    slot_pair = (
        jnp.full((experts * capacity + 1,), 2 * tok_count, jnp.int32).at[flat_slot].set(pair_ids)
    )
    slot_pair = slot_pair[: experts * capacity]
    slot_token = jnp.where(slot_pair < 2 * tok_count, slot_pair % tok_count, tok_count)
    return (flat_slot, slot_pair, slot_token, kept_mask)


def block_tables(route_ids, prio_rank, experts, capacity):
    blocks, tok_count = prio_rank.shape
    flat_slot, slot_pair, slot_token, kept_mask = jax.vmap(
        lambda r, p: slot_tables(r, p, experts, capacity)
    )(route_ids, prio_rank)
    block_ids = jnp.arange(blocks, dtype=jnp.int32)
    send_index = (block_ids[:, None] * (tok_count + 1) + slot_token).reshape(
        blocks, experts, capacity
    ).transpose(1, 0, 2)
    pair_index = (block_ids[:, None] * (2 * tok_count + 1) + slot_pair).reshape(
        blocks, experts, capacity
    ).transpose(1, 0, 2)
    slot_e = flat_slot // capacity
    slot_c = flat_slot % capacity
    back_index = jnp.where(
        kept_mask,
        (slot_e * blocks + block_ids[:, None]) * capacity + slot_c,
        experts * blocks * capacity,
    )
    return send_index, pair_index, back_index, kept_mask


def forward_layer(residual, route_hot, tables, weights, experts, capacity):
    norm_gains, norm_shifts, qkv_w, proj_w, router_w, in_w, out_w = weights
    send_index, pair_index, back_index, kept_mask = tables
    tok_count = residual.shape[0]
    blocks = back_index.shape[0]
    tok_block = tok_count // blocks
    seq_count = tok_count // SEQ
    score_scale = HEAD ** (-0.5)
    norm_scale = norm_gains.astype(jnp.float32)
    norm_shift = norm_shifts.astype(jnp.float32)
    normed = layer_norm(residual, norm_scale[0], norm_shift[0]).astype(jnp.bfloat16)
    qkv_rows = jnp.dot(normed, qkv_w, preferred_element_type=jnp.float32).astype(jnp.bfloat16)
    heads = qkv_rows.reshape(seq_count, SEQ, 3, HEADS, HEAD)
    scores = (
        jnp.einsum(
            "sqhd,skhd->shqk", heads[:, :, 0], heads[:, :, 1], preferred_element_type=jnp.float32
        )
        * score_scale
    )
    row_top = jnp.max(scores, axis=-1, keepdims=True)
    scores_exp = jnp.exp(scores - row_top)
    row_total = jnp.sum(scores_exp, axis=-1, keepdims=True)
    soft_scores = scores_exp / row_total
    log_total = row_top + jnp.log(row_total)
    mixed_heads = jnp.einsum(
        "shqk,skhd->sqhd",
        soft_scores.astype(jnp.bfloat16),
        heads[:, :, 2],
        preferred_element_type=jnp.float32,
    )
    mixed_heads = mixed_heads.astype(jnp.bfloat16).reshape(tok_count, D)
    middle = residual + jnp.dot(mixed_heads, proj_w, preferred_element_type=jnp.float32)
    normed_two = layer_norm(middle, norm_scale[1], norm_shift[1]).astype(jnp.bfloat16)
    gate_probs = jax.nn.softmax(
        jnp.dot(normed_two, router_w, preferred_element_type=jnp.float32), axis=-1
    )
    padded = jnp.concatenate(
        [normed_two.reshape(blocks, tok_block, D), jnp.zeros((blocks, 1, D), jnp.bfloat16)],
        axis=1,
    ).reshape(blocks * (tok_block + 1), D)
    sending = padded[send_index]
    received = lax.all_to_all(sending, "expert", split_axis=0, concat_axis=0, tiled=True)
    row_block = received.reshape(experts * blocks * capacity, D)
    hidden_pre = jnp.dot(row_block, in_w[0], preferred_element_type=jnp.float32)
    hidden_act = gelu_tanh(hidden_pre).astype(jnp.bfloat16)
    expert_rows = jnp.dot(hidden_act, out_w[0], preferred_element_type=jnp.float32).astype(
        jnp.bfloat16
    )
    returned = lax.all_to_all(
        expert_rows.reshape(experts, blocks, capacity, D),
        "expert",
        split_axis=0,
        concat_axis=0,
        tiled=True,
    )
    back_rows = jnp.concatenate(
        [returned.reshape(experts * blocks * capacity, D), jnp.zeros((1, D), jnp.bfloat16)]
    )
    pair_rows = (
        back_rows[back_index].astype(jnp.float32).reshape(blocks, TOP, tok_block, D)
    )
    probs_block = gate_probs.reshape(blocks, tok_block, experts)
    chosen = jnp.sum(route_hot * probs_block[:, :, None, :], axis=-1)
    kept_gate = kept_mask.astype(jnp.float32).reshape(blocks, TOP, tok_block)
    weight_pair = kept_gate * chosen.transpose(0, 2, 1)
    combined = jnp.sum(weight_pair[..., None] * pair_rows, axis=1)
    output = middle + combined.reshape(tok_count, D)
    saved_state = (
        residual,
        normed,
        heads,
        log_total,
        mixed_heads,
        middle,
        normed_two,
        gate_probs,
        kept_gate,
        weight_pair,
        pair_rows,
        row_block,
        hidden_pre,
    )
    return (output, saved_state)


def backward_layer(d_output, saved_state, route_hot, tables, weights, experts, capacity):
    (
        residual,
        normed,
        heads,
        log_total,
        mixed_heads,
        middle,
        normed_two,
        gate_probs,
        kept_gate,
        weight_pair,
        pair_rows,
        row_block,
        hidden_pre,
    ) = saved_state
    send_index, pair_index, back_index, kept_mask = tables
    norm_gains, norm_shifts, qkv_w, proj_w, router_w, in_w, out_w = weights
    tok_count = residual.shape[0]
    blocks = back_index.shape[0]
    tok_block = tok_count // blocks
    seq_count = tok_count // SEQ
    score_scale = HEAD ** (-0.5)
    norm_scale = norm_gains.astype(jnp.float32)
    norm_shift = norm_shifts.astype(jnp.float32)
    d_block = d_output.reshape(blocks, 1, tok_block, D)
    d_gate_pair = kept_gate * jnp.sum(d_block * pair_rows, axis=-1)
    d_gates = jnp.sum(route_hot * d_gate_pair.transpose(0, 2, 1)[..., None], axis=2)
    d_gates = d_gates.reshape(tok_count, experts)
    d_logits = (
        gate_probs * (d_gates - jnp.sum(gate_probs * d_gates, axis=-1, keepdims=True))
    ).astype(jnp.bfloat16)
    g_router = dot_first(normed_two, d_logits)
    d_normed_two = dot_last(d_logits, router_w)
    d_pairs = (weight_pair[..., None] * d_block).astype(jnp.bfloat16).reshape(
        blocks, TOP * tok_block, D
    )
    d_pairs = jnp.concatenate(
        [d_pairs, jnp.zeros((blocks, 1, D), jnp.bfloat16)], axis=1
    ).reshape(blocks * (TOP * tok_block + 1), D)
    d_slots = d_pairs[pair_index]
    d_expert_out = lax.all_to_all(d_slots, "expert", split_axis=0, concat_axis=0, tiled=True)
    flat_out = d_expert_out.reshape(experts * blocks * capacity, D)
    hidden_act = gelu_tanh(hidden_pre).astype(jnp.bfloat16)
    g_out = dot_first(hidden_act, flat_out)
    d_act = dot_last(flat_out, out_w[0])
    d_pre = jax.vjp(gelu_tanh, hidden_pre)[1](d_act)[0].astype(jnp.bfloat16)
    g_in = dot_first(row_block, d_pre)
    d_rows = dot_last(d_pre, in_w[0]).astype(jnp.bfloat16).reshape(experts, blocks, capacity, D)
    d_back = lax.all_to_all(d_rows, "expert", split_axis=0, concat_axis=0, tiled=True)
    d_pair_in = jnp.concatenate(
        [d_back.reshape(experts * blocks * capacity, D), jnp.zeros((1, D), jnp.bfloat16)]
    )[back_index]
    d_pair_in = d_pair_in.astype(jnp.float32).reshape(blocks, TOP, tok_block, D)
    d_normed_two = d_normed_two + jnp.sum(d_pair_in, axis=1).reshape(tok_count, D)
    pulled_two = jax.vjp(layer_norm, middle, norm_scale[1], norm_shift[1])[1](d_normed_two)
    d_middle = d_output + pulled_two[0]
    d_branch = d_middle.astype(jnp.bfloat16)
    g_proj = dot_first(mixed_heads, d_branch)
    d_mixed = dot_last(d_branch, proj_w).astype(jnp.bfloat16).reshape(seq_count, SEQ, HEADS, HEAD)
    query_heads = heads[:, :, 0]
    key_heads = heads[:, :, 1]
    value_heads = heads[:, :, 2]
    scores = (
        jnp.einsum("sqhd,skhd->shqk", query_heads, key_heads, preferred_element_type=jnp.float32)
        * score_scale
    )
    soft_scores = jnp.exp(scores - log_total)
    d_soft = jnp.einsum("sqhd,skhd->shqk", d_mixed, value_heads, preferred_element_type=jnp.float32)
    d_values = jnp.einsum(
        "shqk,sqhd->skhd",
        soft_scores.astype(jnp.bfloat16),
        d_mixed,
        preferred_element_type=jnp.float32,
    )
    d_scores = (
        soft_scores * (d_soft - jnp.sum(soft_scores * d_soft, axis=-1, keepdims=True))
    ).astype(jnp.bfloat16)
    d_query = (
        jnp.einsum("shqk,skhd->sqhd", d_scores, key_heads, preferred_element_type=jnp.float32)
        * score_scale
    )
    d_keys = (
        jnp.einsum("shqk,sqhd->skhd", d_scores, query_heads, preferred_element_type=jnp.float32)
        * score_scale
    )
    d_qkv = (
        jnp.stack([d_query, d_keys, d_values], axis=2)
        .reshape(tok_count, 3 * D)
        .astype(jnp.bfloat16)
    )
    g_qkv = dot_first(normed, d_qkv)
    d_normed = dot_last(d_qkv, qkv_w)
    pulled_one = jax.vjp(layer_norm, residual, norm_scale[0], norm_shift[0])[1](d_normed)
    d_residual = d_middle + pulled_one[0]
    g_gain = jnp.stack([pulled_one[1], pulled_two[1]])
    g_shift = jnp.stack([pulled_one[2], pulled_two[2]])
    return (d_residual, (g_gain, g_shift, g_qkv, g_proj, g_router, g_in[None], g_out[None]))


SCATTER_DIMS = (1, 1, 0, 0, 0, 1, 1)


def reduce_layer(layer_grads):
    scattered = [
        lax.psum_scatter(
            grad.astype(jnp.bfloat16), "shard", scatter_dimension=dim, tiled=True
        ).astype(jnp.float32)
        for grad, dim in zip(layer_grads, SCATTER_DIMS)
    ]
    replicated = [
        lax.psum(part.astype(jnp.bfloat16), "expert").astype(jnp.float32)
        for part in scattered[:5]
    ]
    return replicated + scattered[5:]


def local(
    tokens,
    routes,
    priority,
    norm_gain,
    norm_bias,
    w_qkv,
    w_proj,
    w_router,
    exp_in,
    exp_out,
    cotangent,
):
    experts = lax.axis_size("expert") * EXP_DEV
    capacity = max(8, (5 * TOK_MB // (2 * experts) + 7) // 8 * 8)
    tok_count = tokens.shape[0]
    blocks = tok_count // TOK_MB
    route_ids = routes.reshape(blocks, TOK_MB, TOP)
    prio_rank = priority.reshape(blocks, TOK_MB)
    tables = block_tables(route_ids, prio_rank, experts, capacity)
    route_hot = (
        route_ids[..., None] == jnp.arange(experts, dtype=jnp.int32)
    ).astype(jnp.float32)
    all_weights = []
    for layer_index in range(LAYERS):
        all_weights.append(
            (
                lax.all_gather(norm_gain[layer_index], "shard", axis=1, tiled=True),
                lax.all_gather(norm_bias[layer_index], "shard", axis=1, tiled=True),
                lax.all_gather(w_qkv[layer_index], "shard", axis=0, tiled=True),
                lax.all_gather(w_proj[layer_index], "shard", axis=0, tiled=True),
                lax.all_gather(w_router[layer_index], "shard", axis=0, tiled=True),
                lax.all_gather(exp_in[layer_index], "shard", axis=1, tiled=True),
                lax.all_gather(exp_out[layer_index], "shard", axis=1, tiled=True),
            )
        )
    residual = tokens
    saved_list = []
    for layer_index in range(LAYERS):
        residual, saved_state = forward_layer(
            residual, route_hot, tables, all_weights[layer_index], experts, capacity
        )
        saved_list.append(saved_state)
    activations = residual
    d_residual = cotangent
    reduced = [None] * LAYERS
    for layer_index in reversed(range(LAYERS)):
        d_residual, layer_grads = backward_layer(
            d_residual,
            saved_list[layer_index],
            route_hot,
            tables,
            all_weights[layer_index],
            experts,
            capacity,
        )
        reduced[layer_index] = reduce_layer(layer_grads)
    outs = [jnp.stack([reduced[l][k] for l in range(LAYERS)]) for k in range(7)]
    return (activations, d_residual, *outs)


def solution(mesh):
    return jax.shard_map(
        local,
        mesh=mesh,
        in_specs=(
            P(("expert", "shard"), None),
            P(("expert", "shard"), None),
            P(("expert", "shard")),
            P(None, None, "shard"),
            P(None, None, "shard"),
            P(None, "shard", None),
            P(None, "shard", None),
            P(None, "shard", None),
            P(None, "expert", "shard", None),
            P(None, "expert", "shard", None),
            P(("expert", "shard"), None),
        ),
        out_specs=(
            P(("expert", "shard"), None),
            P(("expert", "shard"), None),
            P(None, None, "shard"),
            P(None, None, "shard"),
            P(None, "shard", None),
            P(None, "shard", None),
            P(None, "shard", None),
            P(None, "expert", "shard", None),
            P(None, "expert", "shard", None),
        ),
        check_vma=False,
    )
```

```python
import jax
import jax.numpy as jnp
from jax import lax
from jax.sharding import PartitionSpec as P

D = 512
HEADS = 8
HEAD = 64
HIDDEN_SIZE = 2048
EXP_DEV = 1
SEQ = 197
MICRO = 2
LAYERS = 2
TOP = 2
TOK_MB = 394


norm_eps = 1e-06


def layer_norm(values, norm_scale, norm_shift):
    centre = values - jnp.mean(values, axis=-1, keepdims=True)
    spread = jnp.mean(centre * centre, axis=-1, keepdims=True)
    return centre * lax.rsqrt(spread + norm_eps) * norm_scale + norm_shift


def gelu_tanh(values):
    return jax.nn.gelu(values, approximate=True)


def dot_first(left, right):
    return lax.dot_general(
        left, right, (((0,), (0,)), ((), ())), preferred_element_type=jnp.float32
    )


def dot_last(left, right):
    return lax.dot_general(
        left, right, (((1,), (1,)), ((), ())), preferred_element_type=jnp.float32
    )


def slot_tables(route_ids, prio_rank, experts, capacity):
    tok_count = route_ids.shape[0]
    order_key = jnp.concatenate([prio_rank, prio_rank + tok_count])
    pair_expert = jnp.concatenate([route_ids[:, 0], route_ids[:, 1]])
    same_expert = pair_expert[:, None] == pair_expert[None, :]
    earlier = order_key[None, :] < order_key[:, None]
    position = jnp.sum((same_expert & earlier).astype(jnp.int32), axis=1)
    kept_mask = position < capacity
    flat_slot = jnp.where(kept_mask, pair_expert * capacity + position, experts * capacity)
    pair_ids = jnp.arange(2 * tok_count, dtype=jnp.int32)
    slot_pair = (
        jnp.full((experts * capacity + 1,), 2 * tok_count, jnp.int32).at[flat_slot].set(pair_ids)
    )
    slot_pair = slot_pair[: experts * capacity]
    slot_token = jnp.where(slot_pair < 2 * tok_count, slot_pair % tok_count, tok_count)
    return (flat_slot, slot_pair, slot_token, kept_mask)


def block_tables(route_ids, prio_rank, experts, capacity):
    blocks, tok_count = prio_rank.shape
    flat_slot, slot_pair, slot_token, kept_mask = jax.vmap(
        lambda r, p: slot_tables(r, p, experts, capacity)
    )(route_ids, prio_rank)
    block_ids = jnp.arange(blocks, dtype=jnp.int32)
    send_index = (block_ids[:, None] * (tok_count + 1) + slot_token).reshape(
        blocks, experts, capacity
    ).transpose(1, 0, 2)
    pair_index = (block_ids[:, None] * (2 * tok_count + 1) + slot_pair).reshape(
        blocks, experts, capacity
    ).transpose(1, 0, 2)
    slot_e = flat_slot // capacity
    slot_c = flat_slot % capacity
    back_index = jnp.where(
        kept_mask,
        (slot_e * blocks + block_ids[:, None]) * capacity + slot_c,
        experts * blocks * capacity,
    )
    return send_index, pair_index, back_index, kept_mask


def forward_layer(residual, route_hot, tables, weights, experts, capacity):
    norm_gains, norm_shifts, qkv_w, proj_w, router_w, in_w, out_w = weights
    send_index, pair_index, back_index, kept_mask = tables
    tok_count = residual.shape[0]
    blocks = back_index.shape[0]
    tok_block = tok_count // blocks
    seq_count = tok_count // SEQ
    score_scale = HEAD ** (-0.5)
    norm_scale = norm_gains.astype(jnp.float32)
    norm_shift = norm_shifts.astype(jnp.float32)
    normed = layer_norm(residual, norm_scale[0], norm_shift[0]).astype(jnp.bfloat16)
    qkv_rows = jnp.dot(normed, qkv_w, preferred_element_type=jnp.float32).astype(jnp.bfloat16)
    heads = qkv_rows.reshape(seq_count, SEQ, 3, HEADS, HEAD)
    scores = (
        jnp.einsum(
            "sqhd,skhd->shqk", heads[:, :, 0], heads[:, :, 1], preferred_element_type=jnp.float32
        )
        * score_scale
    )
    row_top = jnp.max(scores, axis=-1, keepdims=True)
    scores_exp = jnp.exp(scores - row_top)
    row_total = jnp.sum(scores_exp, axis=-1, keepdims=True)
    soft_scores = scores_exp / row_total
    log_total = row_top + jnp.log(row_total)
    mixed_heads = jnp.einsum(
        "shqk,skhd->sqhd",
        soft_scores.astype(jnp.bfloat16),
        heads[:, :, 2],
        preferred_element_type=jnp.float32,
    )
    mixed_heads = mixed_heads.astype(jnp.bfloat16).reshape(tok_count, D)
    middle = residual + jnp.dot(mixed_heads, proj_w, preferred_element_type=jnp.float32)
    normed_two = layer_norm(middle, norm_scale[1], norm_shift[1]).astype(jnp.bfloat16)
    gate_probs = jax.nn.softmax(
        jnp.dot(normed_two, router_w, preferred_element_type=jnp.float32), axis=-1
    )
    padded = jnp.concatenate(
        [normed_two.reshape(blocks, tok_block, D), jnp.zeros((blocks, 1, D), jnp.bfloat16)],
        axis=1,
    ).reshape(blocks * (tok_block + 1), D)
    sending = padded[send_index]
    received = lax.all_to_all(sending, "expert", split_axis=0, concat_axis=0, tiled=True)
    row_block = received.reshape(experts * blocks * capacity, D)
    hidden_pre = jnp.dot(row_block, in_w[0], preferred_element_type=jnp.float32)
    hidden_act = gelu_tanh(hidden_pre).astype(jnp.bfloat16)
    expert_rows = jnp.dot(hidden_act, out_w[0], preferred_element_type=jnp.float32).astype(
        jnp.bfloat16
    )
    returned = lax.all_to_all(
        expert_rows.reshape(experts, blocks, capacity, D),
        "expert",
        split_axis=0,
        concat_axis=0,
        tiled=True,
    )
    back_rows = jnp.concatenate(
        [returned.reshape(experts * blocks * capacity, D), jnp.zeros((1, D), jnp.bfloat16)]
    )
    pair_rows = (
        back_rows[back_index].astype(jnp.float32).reshape(blocks, TOP, tok_block, D)
    )
    probs_block = gate_probs.reshape(blocks, tok_block, experts)
    chosen = jnp.sum(route_hot * probs_block[:, :, None, :], axis=-1)
    kept_gate = kept_mask.astype(jnp.float32).reshape(blocks, TOP, tok_block)
    weight_pair = kept_gate * chosen.transpose(0, 2, 1)
    combined = jnp.sum(weight_pair[..., None] * pair_rows, axis=1)
    output = middle + combined.reshape(tok_count, D)
    saved_state = (
        residual,
        normed,
        heads,
        log_total,
        mixed_heads,
        middle,
        normed_two,
        gate_probs,
        kept_gate,
        weight_pair,
        pair_rows,
        row_block,
        hidden_pre,
    )
    return (output, saved_state)


def backward_layer(d_output, saved_state, route_hot, tables, weights, experts, capacity):
    (
        residual,
        normed,
        heads,
        log_total,
        mixed_heads,
        middle,
        normed_two,
        gate_probs,
        kept_gate,
        weight_pair,
        pair_rows,
        row_block,
        hidden_pre,
    ) = saved_state
    send_index, pair_index, back_index, kept_mask = tables
    norm_gains, norm_shifts, qkv_w, proj_w, router_w, in_w, out_w = weights
    tok_count = residual.shape[0]
    blocks = back_index.shape[0]
    tok_block = tok_count // blocks
    seq_count = tok_count // SEQ
    score_scale = HEAD ** (-0.5)
    norm_scale = norm_gains.astype(jnp.float32)
    norm_shift = norm_shifts.astype(jnp.float32)
    d_block = d_output.reshape(blocks, 1, tok_block, D)
    d_gate_pair = kept_gate * jnp.sum(d_block * pair_rows, axis=-1)
    d_gates = jnp.sum(route_hot * d_gate_pair.transpose(0, 2, 1)[..., None], axis=2)
    d_gates = d_gates.reshape(tok_count, experts)
    d_logits = (
        gate_probs * (d_gates - jnp.sum(gate_probs * d_gates, axis=-1, keepdims=True))
    ).astype(jnp.bfloat16)
    g_router = dot_first(normed_two, d_logits)
    d_normed_two = dot_last(d_logits, router_w)
    d_pairs = (weight_pair[..., None] * d_block).astype(jnp.bfloat16).reshape(
        blocks, TOP * tok_block, D
    )
    d_pairs = jnp.concatenate(
        [d_pairs, jnp.zeros((blocks, 1, D), jnp.bfloat16)], axis=1
    ).reshape(blocks * (TOP * tok_block + 1), D)
    d_slots = d_pairs[pair_index]
    d_expert_out = lax.all_to_all(d_slots, "expert", split_axis=0, concat_axis=0, tiled=True)
    flat_out = d_expert_out.reshape(experts * blocks * capacity, D)
    hidden_act = gelu_tanh(hidden_pre).astype(jnp.bfloat16)
    g_out = dot_first(hidden_act, flat_out)
    d_act = dot_last(flat_out, out_w[0])
    d_pre = jax.vjp(gelu_tanh, hidden_pre)[1](d_act)[0].astype(jnp.bfloat16)
    g_in = dot_first(row_block, d_pre)
    d_rows = dot_last(d_pre, in_w[0]).astype(jnp.bfloat16).reshape(experts, blocks, capacity, D)
    d_back = lax.all_to_all(d_rows, "expert", split_axis=0, concat_axis=0, tiled=True)
    d_pair_in = jnp.concatenate(
        [d_back.reshape(experts * blocks * capacity, D), jnp.zeros((1, D), jnp.bfloat16)]
    )[back_index]
    d_pair_in = d_pair_in.astype(jnp.float32).reshape(blocks, TOP, tok_block, D)
    d_normed_two = d_normed_two + jnp.sum(d_pair_in, axis=1).reshape(tok_count, D)
    pulled_two = jax.vjp(layer_norm, middle, norm_scale[1], norm_shift[1])[1](d_normed_two)
    d_middle = d_output + pulled_two[0]
    d_branch = d_middle.astype(jnp.bfloat16)
    g_proj = dot_first(mixed_heads, d_branch)
    d_mixed = dot_last(d_branch, proj_w).astype(jnp.bfloat16).reshape(seq_count, SEQ, HEADS, HEAD)
    query_heads = heads[:, :, 0]
    key_heads = heads[:, :, 1]
    value_heads = heads[:, :, 2]
    scores = (
        jnp.einsum("sqhd,skhd->shqk", query_heads, key_heads, preferred_element_type=jnp.float32)
        * score_scale
    )
    soft_scores = jnp.exp(scores - log_total)
    d_soft = jnp.einsum("sqhd,skhd->shqk", d_mixed, value_heads, preferred_element_type=jnp.float32)
    d_values = jnp.einsum(
        "shqk,sqhd->skhd",
        soft_scores.astype(jnp.bfloat16),
        d_mixed,
        preferred_element_type=jnp.float32,
    )
    d_scores = (
        soft_scores * (d_soft - jnp.sum(soft_scores * d_soft, axis=-1, keepdims=True))
    ).astype(jnp.bfloat16)
    d_query = (
        jnp.einsum("shqk,skhd->sqhd", d_scores, key_heads, preferred_element_type=jnp.float32)
        * score_scale
    )
    d_keys = (
        jnp.einsum("shqk,sqhd->skhd", d_scores, query_heads, preferred_element_type=jnp.float32)
        * score_scale
    )
    d_qkv = (
        jnp.stack([d_query, d_keys, d_values], axis=2)
        .reshape(tok_count, 3 * D)
        .astype(jnp.bfloat16)
    )
    g_qkv = dot_first(normed, d_qkv)
    d_normed = dot_last(d_qkv, qkv_w)
    pulled_one = jax.vjp(layer_norm, residual, norm_scale[0], norm_shift[0])[1](d_normed)
    d_residual = d_middle + pulled_one[0]
    g_gain = jnp.stack([pulled_one[1], pulled_two[1]])
    g_shift = jnp.stack([pulled_one[2], pulled_two[2]])
    return (d_residual, (g_gain, g_shift, g_qkv, g_proj, g_router, g_in[None], g_out[None]))


def halving_scatter(grad, axis_name):
    size = lax.axis_size(axis_name)
    me = lax.axis_index(axis_name)
    chunk = grad.shape[0] // size
    rest = grad.shape[1:]
    total = grad.astype(jnp.float32).reshape(size, chunk, *rest)
    bit = 1
    while bit < size:
        pairs = total.reshape(total.shape[0] // 2, 2, chunk, *rest)
        mine = (me // bit) % 2
        keep = lax.dynamic_index_in_dim(pairs, mine, axis=1, keepdims=False)
        give = lax.dynamic_index_in_dim(pairs, 1 - mine, axis=1, keepdims=False)
        got = lax.ppermute(
            give.astype(jnp.bfloat16), axis_name, [(i, i ^ bit) for i in range(size)]
        )
        total = keep + got.astype(jnp.float32)
        bit *= 2
    return total.reshape(chunk, *rest)


def doubling_sum(part, axis_name):
    size = lax.axis_size(axis_name)
    total = part.astype(jnp.float32)
    bit = 1
    while bit < size:
        own = lax.reduce_precision(total, exponent_bits=8, mantissa_bits=7)
        got = lax.ppermute(
            own.astype(jnp.bfloat16), axis_name, [(i, i ^ bit) for i in range(size)]
        )
        total = own + got.astype(jnp.float32)
        bit *= 2
    return total


def reduce_layer(layer_grads):
    g_gain, g_shift, g_qkv, g_proj, g_router, g_in, g_out = layer_grads
    qkv_cols = g_qkv.shape[1]
    proj_cols = g_proj.shape[1]
    small = jnp.concatenate([g_gain.T, g_shift.T, g_router], axis=1)
    shared = jnp.concatenate([g_qkv, g_proj, small], axis=1)
    shared = doubling_sum(halving_scatter(shared, "shard"), "expert")
    tail = shared[:, qkv_cols + proj_cols :]
    return [
        tail[:, 0:2].T,
        tail[:, 2:4].T,
        shared[:, :qkv_cols],
        shared[:, qkv_cols : qkv_cols + proj_cols],
        tail[:, 4:],
        halving_scatter(g_in[0], "shard")[None],
        halving_scatter(g_out[0], "shard")[None],
    ]


def local(
    tokens,
    routes,
    priority,
    norm_gain,
    norm_bias,
    w_qkv,
    w_proj,
    w_router,
    exp_in,
    exp_out,
    cotangent,
):
    experts = lax.axis_size("expert") * EXP_DEV
    capacity = max(8, (5 * TOK_MB // (2 * experts) + 7) // 8 * 8)
    tok_count = tokens.shape[0]
    blocks = tok_count // TOK_MB
    streams = []
    for block in range(blocks):
        rows = slice(block * TOK_MB, (block + 1) * TOK_MB)
        route_ids = routes[rows].reshape(1, TOK_MB, TOP)
        prio_rank = priority[rows].reshape(1, TOK_MB)
        tables = block_tables(route_ids, prio_rank, experts, capacity)
        route_hot = (
            route_ids[..., None] == jnp.arange(experts, dtype=jnp.int32)
        ).astype(jnp.float32)
        streams.append((rows, tables, route_hot))
    all_weights = []
    for layer_index in range(LAYERS):
        all_weights.append(
            (
                lax.all_gather(norm_gain[layer_index], "shard", axis=1, tiled=True),
                lax.all_gather(norm_bias[layer_index], "shard", axis=1, tiled=True),
                lax.all_gather(w_qkv[layer_index], "shard", axis=0, tiled=True),
                lax.all_gather(w_proj[layer_index], "shard", axis=0, tiled=True),
                lax.all_gather(w_router[layer_index], "shard", axis=0, tiled=True),
                lax.all_gather(exp_in[layer_index], "shard", axis=1, tiled=True),
                lax.all_gather(exp_out[layer_index], "shard", axis=1, tiled=True),
            )
        )
    residuals = [tokens[rows] for rows, _, _ in streams]
    saved = [[None] * LAYERS for _ in streams]
    for layer_index in range(LAYERS):
        for block, (rows, tables, route_hot) in enumerate(streams):
            residuals[block], saved[block][layer_index] = forward_layer(
                residuals[block], route_hot, tables, all_weights[layer_index], experts, capacity
            )
    activations = jnp.concatenate(residuals, axis=0)
    d_residuals = [cotangent[rows] for rows, _, _ in streams]
    reduced = [None] * LAYERS
    for layer_index in reversed(range(LAYERS)):
        layer_sum = None
        for block, (rows, tables, route_hot) in enumerate(streams):
            d_residuals[block], layer_grads = backward_layer(
                d_residuals[block],
                saved[block][layer_index],
                route_hot,
                tables,
                all_weights[layer_index],
                experts,
                capacity,
            )
            if layer_sum is None:
                layer_sum = layer_grads
            else:
                layer_sum = tuple(old + new for old, new in zip(layer_sum, layer_grads))
        reduced[layer_index] = reduce_layer(layer_sum)
    outs = [jnp.stack([reduced[l][k] for l in range(LAYERS)]) for k in range(7)]
    d_tokens = jnp.concatenate(d_residuals, axis=0)
    return (activations, d_tokens, *outs)


def solution(mesh):
    return jax.shard_map(
        local,
        mesh=mesh,
        in_specs=(
            P(("expert", "shard"), None),
            P(("expert", "shard"), None),
            P(("expert", "shard")),
            P(None, None, "shard"),
            P(None, None, "shard"),
            P(None, "shard", None),
            P(None, "shard", None),
            P(None, "shard", None),
            P(None, "expert", "shard", None),
            P(None, "expert", "shard", None),
            P(("expert", "shard"), None),
        ),
        out_specs=(
            P(("expert", "shard"), None),
            P(("expert", "shard"), None),
            P(None, None, "shard"),
            P(None, None, "shard"),
            P(None, "shard", None),
            P(None, "shard", None),
            P(None, "shard", None),
            P(None, "expert", "shard", None),
            P(None, "expert", "shard", None),
        ),
        check_vma=False,
    )
```

```python
import jax
import jax.numpy as jnp
from jax import lax
from jax.sharding import PartitionSpec as P

D = 512
HEADS = 8
HEAD = 64
HIDDEN_SIZE = 2048
EXP_DEV = 1
SEQ = 197
MICRO = 2
LAYERS = 2
TOP = 2
TOK_MB = 394


norm_eps = 1e-06


def layer_norm(values, norm_scale, norm_shift):
    centre = values - jnp.mean(values, axis=-1, keepdims=True)
    spread = jnp.mean(centre * centre, axis=-1, keepdims=True)
    return centre * lax.rsqrt(spread + norm_eps) * norm_scale + norm_shift


def gelu_tanh(values):
    return jax.nn.gelu(values, approximate=True)


def dot_first(left, right):
    return lax.dot_general(
        left, right, (((0,), (0,)), ((), ())), preferred_element_type=jnp.float32
    )


def dot_last(left, right):
    return lax.dot_general(
        left, right, (((1,), (1,)), ((), ())), preferred_element_type=jnp.float32
    )


def slot_onehot(route_ids, prio_rank, experts, capacity):
    tok_count = route_ids.shape[0]
    order_key = jnp.concatenate([prio_rank, prio_rank + tok_count])
    pair_expert = jnp.concatenate([route_ids[:, 0], route_ids[:, 1]])
    expert_hot = (pair_expert[:, None] == jnp.arange(experts, dtype=jnp.int32)[None, :]).astype(
        jnp.bfloat16
    )
    earlier = (order_key[:, None] < order_key[None, :]).astype(jnp.bfloat16)
    counts = dot_first(expert_hot, earlier)
    position = jnp.sum(counts.T * expert_hot.astype(jnp.float32), axis=1).astype(jnp.int32)
    kept_mask = position < capacity
    flat_slot = jnp.where(kept_mask, pair_expert * capacity + position, experts * capacity)
    pair_hot = (
        flat_slot[:, None] == jnp.arange(experts * capacity, dtype=jnp.int32)[None, :]
    ).astype(jnp.bfloat16)
    token_hot = pair_hot[:tok_count] + pair_hot[tok_count:]
    return pair_hot, token_hot, kept_mask


def forward_layer(residual, route_hot, tables, weights, experts, capacity):
    norm_gains, norm_shifts, qkv_w, proj_w, router_w, in_w, out_w = weights
    pair_hot, token_hot, kept_mask = tables
    tok_count = residual.shape[0]
    seq_count = tok_count // SEQ
    score_scale = HEAD ** (-0.5)
    norm_scale = norm_gains.astype(jnp.float32)
    norm_shift = norm_shifts.astype(jnp.float32)
    normed = layer_norm(residual, norm_scale[0], norm_shift[0]).astype(jnp.bfloat16)
    qkv_rows = jnp.dot(normed, qkv_w, preferred_element_type=jnp.float32).astype(jnp.bfloat16)
    heads = qkv_rows.reshape(seq_count, SEQ, 3, HEADS, HEAD)
    scores = (
        jnp.einsum(
            "sqhd,skhd->shqk", heads[:, :, 0], heads[:, :, 1], preferred_element_type=jnp.float32
        )
        * score_scale
    )
    row_top = jnp.max(scores, axis=-1, keepdims=True)
    scores_exp = jnp.exp(scores - row_top)
    row_total = jnp.sum(scores_exp, axis=-1, keepdims=True)
    soft_scores = scores_exp / row_total
    log_total = row_top + jnp.log(row_total)
    mixed_heads = jnp.einsum(
        "shqk,skhd->sqhd",
        soft_scores.astype(jnp.bfloat16),
        heads[:, :, 2],
        preferred_element_type=jnp.float32,
    )
    mixed_heads = mixed_heads.astype(jnp.bfloat16).reshape(tok_count, D)
    middle = residual + jnp.dot(mixed_heads, proj_w, preferred_element_type=jnp.float32)
    normed_two = layer_norm(middle, norm_scale[1], norm_shift[1]).astype(jnp.bfloat16)
    gate_probs = jax.nn.softmax(
        jnp.dot(normed_two, router_w, preferred_element_type=jnp.float32), axis=-1
    )
    sending = dot_first(token_hot, normed_two).astype(jnp.bfloat16)
    received = lax.all_to_all(
        sending.reshape(experts, capacity, D), "expert", split_axis=0, concat_axis=0, tiled=True
    )
    row_block = received.reshape(experts * capacity, D)
    hidden_pre = jnp.dot(row_block, in_w[0], preferred_element_type=jnp.float32)
    hidden_act = gelu_tanh(hidden_pre).astype(jnp.bfloat16)
    expert_rows = jnp.dot(hidden_act, out_w[0], preferred_element_type=jnp.float32).astype(
        jnp.bfloat16
    )
    returned = lax.all_to_all(
        expert_rows.reshape(experts, capacity, D),
        "expert",
        split_axis=0,
        concat_axis=0,
        tiled=True,
    )
    pair_rows = jnp.dot(
        pair_hot, returned.reshape(experts * capacity, D), preferred_element_type=jnp.float32
    ).reshape(TOP, tok_count, D)
    chosen = jnp.sum(route_hot * gate_probs[:, None, :], axis=-1)
    kept_gate = kept_mask.astype(jnp.float32).reshape(TOP, tok_count)
    weight_pair = kept_gate * chosen.T
    combined = jnp.sum(weight_pair[..., None] * pair_rows, axis=0)
    output = middle + combined
    saved_state = (
        residual,
        normed,
        heads,
        log_total,
        mixed_heads,
        middle,
        normed_two,
        gate_probs,
        kept_gate,
        weight_pair,
        pair_rows,
        row_block,
        hidden_pre,
    )
    return (output, saved_state)


def backward_layer(d_output, saved_state, route_hot, tables, weights, experts, capacity):
    (
        residual,
        normed,
        heads,
        log_total,
        mixed_heads,
        middle,
        normed_two,
        gate_probs,
        kept_gate,
        weight_pair,
        pair_rows,
        row_block,
        hidden_pre,
    ) = saved_state
    pair_hot, token_hot, kept_mask = tables
    norm_gains, norm_shifts, qkv_w, proj_w, router_w, in_w, out_w = weights
    tok_count = residual.shape[0]
    seq_count = tok_count // SEQ
    score_scale = HEAD ** (-0.5)
    norm_scale = norm_gains.astype(jnp.float32)
    norm_shift = norm_shifts.astype(jnp.float32)
    d_gate_pair = kept_gate * jnp.sum(d_output[None] * pair_rows, axis=-1)
    d_gates = jnp.sum(route_hot * d_gate_pair.T[:, :, None], axis=1)
    d_logits = (
        gate_probs * (d_gates - jnp.sum(gate_probs * d_gates, axis=-1, keepdims=True))
    ).astype(jnp.bfloat16)
    g_router = dot_first(normed_two, d_logits)
    d_normed_two = dot_last(d_logits, router_w)
    d_pairs = (
        (weight_pair[:, :, None] * d_output[None]).astype(jnp.bfloat16).reshape(TOP * tok_count, D)
    )
    d_slots = dot_first(pair_hot, d_pairs).astype(jnp.bfloat16).reshape(experts, capacity, D)
    d_expert_out = lax.all_to_all(d_slots, "expert", split_axis=0, concat_axis=0, tiled=True)
    flat_out = d_expert_out.reshape(experts * capacity, D)
    hidden_act = gelu_tanh(hidden_pre).astype(jnp.bfloat16)
    g_out = dot_first(hidden_act, flat_out)
    d_act = dot_last(flat_out, out_w[0])
    d_pre = jax.vjp(gelu_tanh, hidden_pre)[1](d_act)[0].astype(jnp.bfloat16)
    g_in = dot_first(row_block, d_pre)
    d_rows = dot_last(d_pre, in_w[0]).astype(jnp.bfloat16).reshape(experts, capacity, D)
    d_back = lax.all_to_all(d_rows, "expert", split_axis=0, concat_axis=0, tiled=True)
    d_pair_in = jnp.dot(
        pair_hot, d_back.reshape(experts * capacity, D), preferred_element_type=jnp.float32
    ).reshape(TOP, tok_count, D)
    d_normed_two = d_normed_two + jnp.sum(d_pair_in, axis=0)
    pulled_two = jax.vjp(layer_norm, middle, norm_scale[1], norm_shift[1])[1](d_normed_two)
    d_middle = d_output + pulled_two[0]
    d_branch = d_middle.astype(jnp.bfloat16)
    g_proj = dot_first(mixed_heads, d_branch)
    d_mixed = dot_last(d_branch, proj_w).astype(jnp.bfloat16).reshape(seq_count, SEQ, HEADS, HEAD)
    query_heads = heads[:, :, 0]
    key_heads = heads[:, :, 1]
    value_heads = heads[:, :, 2]
    scores = (
        jnp.einsum("sqhd,skhd->shqk", query_heads, key_heads, preferred_element_type=jnp.float32)
        * score_scale
    )
    soft_scores = jnp.exp(scores - log_total)
    d_soft = jnp.einsum("sqhd,skhd->shqk", d_mixed, value_heads, preferred_element_type=jnp.float32)
    d_values = jnp.einsum(
        "shqk,sqhd->skhd",
        soft_scores.astype(jnp.bfloat16),
        d_mixed,
        preferred_element_type=jnp.float32,
    )
    d_scores = (
        soft_scores * (d_soft - jnp.sum(soft_scores * d_soft, axis=-1, keepdims=True))
    ).astype(jnp.bfloat16)
    d_query = (
        jnp.einsum("shqk,skhd->sqhd", d_scores, key_heads, preferred_element_type=jnp.float32)
        * score_scale
    )
    d_keys = (
        jnp.einsum("shqk,sqhd->skhd", d_scores, query_heads, preferred_element_type=jnp.float32)
        * score_scale
    )
    d_qkv = (
        jnp.stack([d_query, d_keys, d_values], axis=2)
        .reshape(tok_count, 3 * D)
        .astype(jnp.bfloat16)
    )
    g_qkv = dot_first(normed, d_qkv)
    d_normed = dot_last(d_qkv, qkv_w)
    pulled_one = jax.vjp(layer_norm, residual, norm_scale[0], norm_shift[0])[1](d_normed)
    d_residual = d_middle + pulled_one[0]
    g_gain = jnp.stack([pulled_one[1], pulled_two[1]])
    g_shift = jnp.stack([pulled_one[2], pulled_two[2]])
    return (d_residual, (g_gain, g_shift, g_qkv, g_proj, g_router, g_in[None], g_out[None]))


def halving_scatter(grad, axis_name):
    size = lax.axis_size(axis_name)
    me = lax.axis_index(axis_name)
    chunk = grad.shape[0] // size
    rest = grad.shape[1:]
    total = grad.astype(jnp.float32).reshape(size, chunk, *rest)
    bit = 1
    while bit < size:
        pairs = total.reshape(total.shape[0] // 2, 2, chunk, *rest)
        mine = (me // bit) % 2
        keep = lax.dynamic_index_in_dim(pairs, mine, axis=1, keepdims=False)
        give = lax.dynamic_index_in_dim(pairs, 1 - mine, axis=1, keepdims=False)
        got = lax.ppermute(
            give.astype(jnp.bfloat16), axis_name, [(i, i ^ bit) for i in range(size)]
        )
        total = keep + got.astype(jnp.float32)
        bit *= 2
    return total.reshape(chunk, *rest)


def doubling_sum(part, axis_name):
    size = lax.axis_size(axis_name)
    total = part.astype(jnp.float32)
    bit = 1
    while bit < size:
        own = lax.reduce_precision(total, exponent_bits=8, mantissa_bits=7)
        got = lax.ppermute(
            own.astype(jnp.bfloat16), axis_name, [(i, i ^ bit) for i in range(size)]
        )
        total = own + got.astype(jnp.float32)
        bit *= 2
    return total


def reduce_layer(layer_grads):
    g_gain, g_shift, g_qkv, g_proj, g_router, g_in, g_out = layer_grads
    qkv_cols = g_qkv.shape[1]
    proj_cols = g_proj.shape[1]
    small = jnp.concatenate([g_gain.T, g_shift.T, g_router], axis=1)
    shared = jnp.concatenate([g_qkv, g_proj, small], axis=1)
    shared = doubling_sum(halving_scatter(shared, "shard"), "expert")
    tail = shared[:, qkv_cols + proj_cols :]
    return [
        tail[:, 0:2].T,
        tail[:, 2:4].T,
        shared[:, :qkv_cols],
        shared[:, qkv_cols : qkv_cols + proj_cols],
        tail[:, 4:],
        halving_scatter(g_in[0], "shard")[None],
        halving_scatter(g_out[0], "shard")[None],
    ]


def local(
    tokens,
    routes,
    priority,
    norm_gain,
    norm_bias,
    w_qkv,
    w_proj,
    w_router,
    exp_in,
    exp_out,
    cotangent,
):
    experts = lax.axis_size("expert") * EXP_DEV
    capacity = max(8, (5 * TOK_MB // (2 * experts) + 7) // 8 * 8)
    tok_count = tokens.shape[0]
    blocks = tok_count // TOK_MB
    streams = []
    for block in range(blocks):
        rows = slice(block * TOK_MB, (block + 1) * TOK_MB)
        route_ids = routes[rows]
        tables = slot_onehot(route_ids, priority[rows], experts, capacity)
        route_hot = (
            route_ids[..., None] == jnp.arange(experts, dtype=jnp.int32)
        ).astype(jnp.float32)
        streams.append((rows, tables, route_hot))
    layer_count = norm_gain.shape[0]
    small = jnp.concatenate(
        [
            norm_gain.reshape(layer_count * 2, -1).T,
            norm_bias.reshape(layer_count * 2, -1).T,
            w_router.transpose(1, 0, 2).reshape(w_router.shape[1], -1),
        ],
        axis=1,
    )
    small = lax.all_gather(small, "shard", axis=0, tiled=True)
    qkv_cols = w_qkv.shape[2]
    all_weights = []
    for layer_index in range(LAYERS):
        attn = lax.all_gather(
            jnp.concatenate([w_qkv[layer_index], w_proj[layer_index]], axis=1),
            "shard",
            axis=0,
            tiled=True,
        )
        shift_at = 2 * layer_count + 2 * layer_index
        router_at = 4 * layer_count + experts * layer_index
        all_weights.append(
            (
                small[:, 2 * layer_index : 2 * layer_index + 2].T,
                small[:, shift_at : shift_at + 2].T,
                attn[:, :qkv_cols],
                attn[:, qkv_cols:],
                small[:, router_at : router_at + experts],
                lax.all_gather(exp_in[layer_index], "shard", axis=1, tiled=True),
                lax.all_gather(exp_out[layer_index], "shard", axis=1, tiled=True),
            )
        )
    residuals = [tokens[rows] for rows, _, _ in streams]
    saved = [[None] * LAYERS for _ in streams]
    for layer_index in range(LAYERS):
        for block, (rows, tables, route_hot) in enumerate(streams):
            residuals[block], saved[block][layer_index] = forward_layer(
                residuals[block], route_hot, tables, all_weights[layer_index], experts, capacity
            )
    activations = jnp.concatenate(residuals, axis=0)
    d_residuals = [cotangent[rows] for rows, _, _ in streams]
    reduced = [None] * LAYERS
    for layer_index in reversed(range(LAYERS)):
        layer_sum = None
        for block, (rows, tables, route_hot) in enumerate(streams):
            d_residuals[block], layer_grads = backward_layer(
                d_residuals[block],
                saved[block][layer_index],
                route_hot,
                tables,
                all_weights[layer_index],
                experts,
                capacity,
            )
            if layer_sum is None:
                layer_sum = layer_grads
            else:
                layer_sum = tuple(old + new for old, new in zip(layer_sum, layer_grads))
        reduced[layer_index] = reduce_layer(layer_sum)
    outs = [jnp.stack([reduced[l][k] for l in range(LAYERS)]) for k in range(7)]
    d_tokens = jnp.concatenate(d_residuals, axis=0)
    return (activations, d_tokens, *outs)


def solution(mesh):
    return jax.shard_map(
        local,
        mesh=mesh,
        in_specs=(
            P(("expert", "shard"), None),
            P(("expert", "shard"), None),
            P(("expert", "shard")),
            P(None, None, "shard"),
            P(None, None, "shard"),
            P(None, "shard", None),
            P(None, "shard", None),
            P(None, "shard", None),
            P(None, "expert", "shard", None),
            P(None, "expert", "shard", None),
            P(("expert", "shard"), None),
        ),
        out_specs=(
            P(("expert", "shard"), None),
            P(("expert", "shard"), None),
            P(None, None, "shard"),
            P(None, None, "shard"),
            P(None, "shard", None),
            P(None, "shard", None),
            P(None, "shard", None),
            P(None, "expert", "shard", None),
            P(None, "expert", "shard", None),
        ),
        check_vma=False,
    )
```

```python
import jax
import jax.numpy as jnp
from jax import lax
from jax.sharding import PartitionSpec as P

D = 512
HEADS = 8
HEAD = 64
HIDDEN_SIZE = 2048
EXP_DEV = 1
SEQ = 197
MICRO = 2
LAYERS = 2
TOP = 2
TOK_MB = 394


norm_eps = 1e-06


def layer_norm(values, norm_scale, norm_shift):
    centre = values - jnp.mean(values, axis=-1, keepdims=True)
    spread = jnp.mean(centre * centre, axis=-1, keepdims=True)
    return centre * lax.rsqrt(spread + norm_eps) * norm_scale + norm_shift


def gelu_tanh(values):
    return jax.nn.gelu(values, approximate=True)


def dot_first(left, right):
    return lax.dot_general(
        left, right, (((0,), (0,)), ((), ())), preferred_element_type=jnp.float32
    )


def dot_last(left, right):
    return lax.dot_general(
        left, right, (((1,), (1,)), ((), ())), preferred_element_type=jnp.float32
    )


def slot_onehot(route_ids, prio_rank, experts, capacity):
    tok_count = route_ids.shape[0]
    order_key = jnp.concatenate([prio_rank, prio_rank + tok_count])
    pair_expert = jnp.concatenate([route_ids[:, 0], route_ids[:, 1]])
    expert_hot = (pair_expert[:, None] == jnp.arange(experts, dtype=jnp.int32)[None, :]).astype(
        jnp.bfloat16
    )
    earlier = (order_key[:, None] < order_key[None, :]).astype(jnp.bfloat16)
    counts = dot_first(expert_hot, earlier)
    position = jnp.sum(counts.T * expert_hot.astype(jnp.float32), axis=1).astype(jnp.int32)
    kept_mask = position < capacity
    own = lax.axis_index("expert")
    flat_slot = jnp.where(
        kept_mask, (pair_expert ^ own) * capacity + position, experts * capacity
    )
    pair_hot = (
        flat_slot[:, None] == jnp.arange(experts * capacity, dtype=jnp.int32)[None, :]
    ).astype(jnp.bfloat16)
    token_hot = pair_hot[:tok_count] + pair_hot[tok_count:]
    return pair_hot, token_hot, kept_mask


def exchange(blocks, axis_name):
    size = blocks.shape[0]
    moved = [blocks[0]] + [
        lax.ppermute(blocks[k], axis_name, [(i, i ^ k) for i in range(size)])
        for k in range(1, size)
    ]
    return jnp.stack(moved)


def forward_layer(residual, route_hot, tables, weights, experts, capacity):
    norm_gains, norm_shifts, qkv_w, proj_w, router_w, in_w, out_w = weights
    pair_hot, token_hot, kept_mask = tables
    tok_count = residual.shape[0]
    seq_count = tok_count // SEQ
    score_scale = HEAD ** (-0.5)
    norm_scale = norm_gains.astype(jnp.float32)
    norm_shift = norm_shifts.astype(jnp.float32)
    normed = layer_norm(residual, norm_scale[0], norm_shift[0]).astype(jnp.bfloat16)
    qkv_rows = jnp.dot(normed, qkv_w, preferred_element_type=jnp.float32).astype(jnp.bfloat16)
    heads = qkv_rows.reshape(seq_count, SEQ, 3, HEADS, HEAD)
    scores = (
        jnp.einsum(
            "sqhd,skhd->shqk", heads[:, :, 0], heads[:, :, 1], preferred_element_type=jnp.float32
        )
        * score_scale
    )
    row_top = jnp.max(scores, axis=-1, keepdims=True)
    scores_exp = jnp.exp(scores - row_top)
    row_total = jnp.sum(scores_exp, axis=-1, keepdims=True)
    soft_scores = scores_exp / row_total
    log_total = row_top + jnp.log(row_total)
    mixed_heads = jnp.einsum(
        "shqk,skhd->sqhd",
        soft_scores.astype(jnp.bfloat16),
        heads[:, :, 2],
        preferred_element_type=jnp.float32,
    )
    mixed_heads = mixed_heads.astype(jnp.bfloat16).reshape(tok_count, D)
    middle = residual + jnp.dot(mixed_heads, proj_w, preferred_element_type=jnp.float32)
    normed_two = layer_norm(middle, norm_scale[1], norm_shift[1]).astype(jnp.bfloat16)
    gate_probs = jax.nn.softmax(
        jnp.dot(normed_two, router_w, preferred_element_type=jnp.float32), axis=-1
    )
    sending = dot_first(token_hot, normed_two).astype(jnp.bfloat16)
    received = exchange(sending.reshape(experts, capacity, D), "expert")
    row_block = received.reshape(experts * capacity, D)
    hidden_pre = jnp.dot(row_block, in_w[0], preferred_element_type=jnp.float32)
    hidden_act = gelu_tanh(hidden_pre).astype(jnp.bfloat16)
    expert_rows = jnp.dot(hidden_act, out_w[0], preferred_element_type=jnp.float32).astype(
        jnp.bfloat16
    )
    returned = exchange(expert_rows.reshape(experts, capacity, D), "expert")
    pair_rows = jnp.dot(
        pair_hot, returned.reshape(experts * capacity, D), preferred_element_type=jnp.float32
    ).reshape(TOP, tok_count, D)
    chosen = jnp.sum(route_hot * gate_probs[:, None, :], axis=-1)
    kept_gate = kept_mask.astype(jnp.float32).reshape(TOP, tok_count)
    weight_pair = kept_gate * chosen.T
    combined = jnp.sum(weight_pair[..., None] * pair_rows, axis=0)
    output = middle + combined
    saved_state = (
        residual,
        normed,
        heads,
        log_total,
        mixed_heads,
        middle,
        normed_two,
        gate_probs,
        kept_gate,
        weight_pair,
        pair_rows,
        row_block,
        hidden_pre,
    )
    return (output, saved_state)


def backward_layer(d_output, saved_state, route_hot, tables, weights, experts, capacity):
    (
        residual,
        normed,
        heads,
        log_total,
        mixed_heads,
        middle,
        normed_two,
        gate_probs,
        kept_gate,
        weight_pair,
        pair_rows,
        row_block,
        hidden_pre,
    ) = saved_state
    pair_hot, token_hot, kept_mask = tables
    norm_gains, norm_shifts, qkv_w, proj_w, router_w, in_w, out_w = weights
    tok_count = residual.shape[0]
    seq_count = tok_count // SEQ
    score_scale = HEAD ** (-0.5)
    norm_scale = norm_gains.astype(jnp.float32)
    norm_shift = norm_shifts.astype(jnp.float32)
    d_gate_pair = kept_gate * jnp.sum(d_output[None] * pair_rows, axis=-1)
    d_gates = jnp.sum(route_hot * d_gate_pair.T[:, :, None], axis=1)
    d_logits = (
        gate_probs * (d_gates - jnp.sum(gate_probs * d_gates, axis=-1, keepdims=True))
    ).astype(jnp.bfloat16)
    g_router = dot_first(normed_two, d_logits)
    d_normed_two = dot_last(d_logits, router_w)
    d_pairs = (
        (weight_pair[:, :, None] * d_output[None]).astype(jnp.bfloat16).reshape(TOP * tok_count, D)
    )
    d_slots = dot_first(pair_hot, d_pairs).astype(jnp.bfloat16).reshape(experts, capacity, D)
    d_expert_out = exchange(d_slots, "expert")
    flat_out = d_expert_out.reshape(experts * capacity, D)
    hidden_act = gelu_tanh(hidden_pre).astype(jnp.bfloat16)
    g_out = dot_first(hidden_act, flat_out)
    d_act = dot_last(flat_out, out_w[0])
    d_pre = jax.vjp(gelu_tanh, hidden_pre)[1](d_act)[0].astype(jnp.bfloat16)
    g_in = dot_first(row_block, d_pre)
    d_rows = dot_last(d_pre, in_w[0]).astype(jnp.bfloat16).reshape(experts, capacity, D)
    d_back = exchange(d_rows, "expert")
    d_pair_in = jnp.dot(
        pair_hot, d_back.reshape(experts * capacity, D), preferred_element_type=jnp.float32
    ).reshape(TOP, tok_count, D)
    d_normed_two = d_normed_two + jnp.sum(d_pair_in, axis=0)
    pulled_two = jax.vjp(layer_norm, middle, norm_scale[1], norm_shift[1])[1](d_normed_two)
    d_middle = d_output + pulled_two[0]
    d_branch = d_middle.astype(jnp.bfloat16)
    g_proj = dot_first(mixed_heads, d_branch)
    d_mixed = dot_last(d_branch, proj_w).astype(jnp.bfloat16).reshape(seq_count, SEQ, HEADS, HEAD)
    query_heads = heads[:, :, 0]
    key_heads = heads[:, :, 1]
    value_heads = heads[:, :, 2]
    scores = (
        jnp.einsum("sqhd,skhd->shqk", query_heads, key_heads, preferred_element_type=jnp.float32)
        * score_scale
    )
    soft_scores = jnp.exp(scores - log_total)
    d_soft = jnp.einsum("sqhd,skhd->shqk", d_mixed, value_heads, preferred_element_type=jnp.float32)
    d_values = jnp.einsum(
        "shqk,sqhd->skhd",
        soft_scores.astype(jnp.bfloat16),
        d_mixed,
        preferred_element_type=jnp.float32,
    )
    d_scores = (
        soft_scores * (d_soft - jnp.sum(soft_scores * d_soft, axis=-1, keepdims=True))
    ).astype(jnp.bfloat16)
    d_query = (
        jnp.einsum("shqk,skhd->sqhd", d_scores, key_heads, preferred_element_type=jnp.float32)
        * score_scale
    )
    d_keys = (
        jnp.einsum("shqk,sqhd->skhd", d_scores, query_heads, preferred_element_type=jnp.float32)
        * score_scale
    )
    d_qkv = (
        jnp.stack([d_query, d_keys, d_values], axis=2)
        .reshape(tok_count, 3 * D)
        .astype(jnp.bfloat16)
    )
    g_qkv = dot_first(normed, d_qkv)
    d_normed = dot_last(d_qkv, qkv_w)
    pulled_one = jax.vjp(layer_norm, residual, norm_scale[0], norm_shift[0])[1](d_normed)
    d_residual = d_middle + pulled_one[0]
    g_gain = jnp.stack([pulled_one[1], pulled_two[1]])
    g_shift = jnp.stack([pulled_one[2], pulled_two[2]])
    return (d_residual, (g_gain, g_shift, g_qkv, g_proj, g_router, g_in[None], g_out[None]))


def halving_scatter(grad, axis_name):
    size = lax.axis_size(axis_name)
    me = lax.axis_index(axis_name)
    chunk = grad.shape[0] // size
    rest = grad.shape[1:]
    total = grad.astype(jnp.float32).reshape(size, chunk, *rest)
    bit = 1
    while bit < size:
        pairs = total.reshape(total.shape[0] // 2, 2, chunk, *rest)
        mine = (me // bit) % 2
        keep = lax.dynamic_index_in_dim(pairs, mine, axis=1, keepdims=False)
        give = lax.dynamic_index_in_dim(pairs, 1 - mine, axis=1, keepdims=False)
        got = lax.ppermute(
            give.astype(jnp.bfloat16), axis_name, [(i, i ^ bit) for i in range(size)]
        )
        total = keep + got.astype(jnp.float32)
        bit *= 2
    return total.reshape(chunk, *rest)


def doubling_sum(part, axis_name):
    size = lax.axis_size(axis_name)
    total = part.astype(jnp.float32)
    bit = 1
    while bit < size:
        own = lax.reduce_precision(total, exponent_bits=8, mantissa_bits=7)
        got = lax.ppermute(
            own.astype(jnp.bfloat16), axis_name, [(i, i ^ bit) for i in range(size)]
        )
        total = own + got.astype(jnp.float32)
        bit *= 2
    return total


def reduce_layer(layer_grads):
    g_gain, g_shift, g_qkv, g_proj, g_router, g_in, g_out = layer_grads
    qkv_cols = g_qkv.shape[1]
    proj_cols = g_proj.shape[1]
    small = jnp.concatenate([g_gain.T, g_shift.T, g_router], axis=1)
    shared = jnp.concatenate([g_qkv, g_proj, small], axis=1)
    shared = doubling_sum(halving_scatter(shared, "shard"), "expert")
    tail = shared[:, qkv_cols + proj_cols :]
    return [
        tail[:, 0:2].T,
        tail[:, 2:4].T,
        shared[:, :qkv_cols],
        shared[:, qkv_cols : qkv_cols + proj_cols],
        tail[:, 4:],
        halving_scatter(g_in[0], "shard")[None],
        halving_scatter(g_out[0], "shard")[None],
    ]


def local(
    tokens,
    routes,
    priority,
    norm_gain,
    norm_bias,
    w_qkv,
    w_proj,
    w_router,
    exp_in,
    exp_out,
    cotangent,
):
    experts = lax.axis_size("expert") * EXP_DEV
    capacity = max(8, (5 * TOK_MB // (2 * experts) + 7) // 8 * 8)
    tok_count = tokens.shape[0]
    blocks = tok_count // TOK_MB
    streams = []
    for block in range(blocks):
        rows = slice(block * TOK_MB, (block + 1) * TOK_MB)
        route_ids = routes[rows]
        tables = slot_onehot(route_ids, priority[rows], experts, capacity)
        route_hot = (
            route_ids[..., None] == jnp.arange(experts, dtype=jnp.int32)
        ).astype(jnp.float32)
        streams.append((rows, tables, route_hot))
    layer_count = norm_gain.shape[0]
    small = jnp.concatenate(
        [
            norm_gain.reshape(layer_count * 2, -1).T,
            norm_bias.reshape(layer_count * 2, -1).T,
            w_router.transpose(1, 0, 2).reshape(w_router.shape[1], -1),
        ],
        axis=1,
    )
    small = lax.all_gather(small, "shard", axis=0, tiled=True)
    qkv_cols = w_qkv.shape[2]
    all_weights = []
    for layer_index in range(LAYERS):
        attn = lax.all_gather(
            jnp.concatenate([w_qkv[layer_index], w_proj[layer_index]], axis=1),
            "shard",
            axis=0,
            tiled=True,
        )
        shift_at = 2 * layer_count + 2 * layer_index
        router_at = 4 * layer_count + experts * layer_index
        all_weights.append(
            (
                small[:, 2 * layer_index : 2 * layer_index + 2].T,
                small[:, shift_at : shift_at + 2].T,
                attn[:, :qkv_cols],
                attn[:, qkv_cols:],
                small[:, router_at : router_at + experts],
                lax.all_gather(exp_in[layer_index], "shard", axis=1, tiled=True),
                lax.all_gather(exp_out[layer_index], "shard", axis=1, tiled=True),
            )
        )
    residuals = [tokens[rows] for rows, _, _ in streams]
    saved = [[None] * LAYERS for _ in streams]
    for layer_index in range(LAYERS):
        for block, (rows, tables, route_hot) in enumerate(streams):
            residuals[block], saved[block][layer_index] = forward_layer(
                residuals[block], route_hot, tables, all_weights[layer_index], experts, capacity
            )
    activations = jnp.concatenate(residuals, axis=0)
    d_residuals = [cotangent[rows] for rows, _, _ in streams]
    reduced = [None] * LAYERS
    for layer_index in reversed(range(LAYERS)):
        layer_sum = None
        for block, (rows, tables, route_hot) in enumerate(streams):
            d_residuals[block], layer_grads = backward_layer(
                d_residuals[block],
                saved[block][layer_index],
                route_hot,
                tables,
                all_weights[layer_index],
                experts,
                capacity,
            )
            if layer_sum is None:
                layer_sum = layer_grads
            else:
                layer_sum = tuple(old + new for old, new in zip(layer_sum, layer_grads))
        reduced[layer_index] = reduce_layer(layer_sum)
    outs = [jnp.stack([reduced[l][k] for l in range(LAYERS)]) for k in range(7)]
    d_tokens = jnp.concatenate(d_residuals, axis=0)
    return (activations, d_tokens, *outs)


def solution(mesh):
    return jax.shard_map(
        local,
        mesh=mesh,
        in_specs=(
            P(("expert", "shard"), None),
            P(("expert", "shard"), None),
            P(("expert", "shard")),
            P(None, None, "shard"),
            P(None, None, "shard"),
            P(None, "shard", None),
            P(None, "shard", None),
            P(None, "shard", None),
            P(None, "expert", "shard", None),
            P(None, "expert", "shard", None),
            P(("expert", "shard"), None),
        ),
        out_specs=(
            P(("expert", "shard"), None),
            P(("expert", "shard"), None),
            P(None, None, "shard"),
            P(None, None, "shard"),
            P(None, "shard", None),
            P(None, "shard", None),
            P(None, "shard", None),
            P(None, "expert", "shard", None),
            P(None, "expert", "shard", None),
        ),
        check_vma=False,
    )
```

```python
import jax
import jax.numpy as jnp
from jax import lax
from jax.sharding import PartitionSpec as P

D = 512
HEADS = 8
HEAD = 64
HIDDEN_SIZE = 2048
EXP_DEV = 1
SEQ = 197
MICRO = 2
LAYERS = 2
TOP = 2
TOK_MB = 394


norm_eps = 1e-06


def layer_norm(values, norm_scale, norm_shift):
    centre = values - jnp.mean(values, axis=-1, keepdims=True)
    spread = jnp.mean(centre * centre, axis=-1, keepdims=True)
    return centre * lax.rsqrt(spread + norm_eps) * norm_scale + norm_shift


def gelu_tanh(values):
    return jax.nn.gelu(values, approximate=True)


def dot_first(left, right):
    return lax.dot_general(
        left, right, (((0,), (0,)), ((), ())), preferred_element_type=jnp.float32
    )


def dot_last(left, right):
    return lax.dot_general(
        left, right, (((1,), (1,)), ((), ())), preferred_element_type=jnp.float32
    )


def slot_onehot(route_ids, prio_rank, experts, capacity):
    tok_count = route_ids.shape[0]
    order_key = jnp.concatenate([prio_rank, prio_rank + tok_count])
    pair_expert = jnp.concatenate([route_ids[:, 0], route_ids[:, 1]])
    expert_hot = (pair_expert[:, None] == jnp.arange(experts, dtype=jnp.int32)[None, :]).astype(
        jnp.bfloat16
    )
    earlier = (order_key[:, None] < order_key[None, :]).astype(jnp.bfloat16)
    counts = dot_first(expert_hot, earlier)
    position = jnp.sum(counts.T * expert_hot.astype(jnp.float32), axis=1).astype(jnp.int32)
    kept_mask = position < capacity
    flat_slot = jnp.where(kept_mask, pair_expert * capacity + position, experts * capacity)
    pair_hot = (
        flat_slot[:, None] == jnp.arange(experts * capacity, dtype=jnp.int32)[None, :]
    ).astype(jnp.bfloat16)
    token_hot = pair_hot[:tok_count] + pair_hot[tok_count:]
    return pair_hot, token_hot, kept_mask


def forward_layer(residual, route_hot, tables, weights, experts, capacity):
    norm_gains, norm_shifts, qkv_w, proj_w, router_w, in_w, out_w = weights
    pair_hot, token_hot, kept_mask = tables
    tok_count = residual.shape[0]
    seq_count = tok_count // SEQ
    score_scale = HEAD ** (-0.5)
    norm_scale = norm_gains.astype(jnp.float32)
    norm_shift = norm_shifts.astype(jnp.float32)
    normed = layer_norm(residual, norm_scale[0], norm_shift[0]).astype(jnp.bfloat16)
    qkv_rows = jnp.dot(normed, qkv_w, preferred_element_type=jnp.float32).astype(jnp.bfloat16)
    heads = qkv_rows.reshape(seq_count, SEQ, 3, HEADS, HEAD)
    scores = (
        jnp.einsum(
            "sqhd,skhd->shqk", heads[:, :, 0], heads[:, :, 1], preferred_element_type=jnp.float32
        )
        * score_scale
    )
    row_top = jnp.max(scores, axis=-1, keepdims=True)
    scores_exp = jnp.exp(scores - row_top)
    row_total = jnp.sum(scores_exp, axis=-1, keepdims=True)
    soft_scores = scores_exp / row_total
    log_total = row_top + jnp.log(row_total)
    mixed_heads = jnp.einsum(
        "shqk,skhd->sqhd",
        soft_scores.astype(jnp.bfloat16),
        heads[:, :, 2],
        preferred_element_type=jnp.float32,
    )
    mixed_heads = mixed_heads.astype(jnp.bfloat16).reshape(tok_count, D)
    middle = residual + jnp.dot(mixed_heads, proj_w, preferred_element_type=jnp.float32)
    normed_two = layer_norm(middle, norm_scale[1], norm_shift[1]).astype(jnp.bfloat16)
    gate_probs = jax.nn.softmax(
        jnp.dot(normed_two, router_w, preferred_element_type=jnp.float32), axis=-1
    )
    sending = dot_first(token_hot, normed_two).astype(jnp.bfloat16)
    received = lax.all_to_all(
        sending.reshape(experts, capacity, D), "expert", split_axis=0, concat_axis=0, tiled=True
    )
    row_block = received.reshape(experts * capacity, D)
    hidden_pre = jnp.dot(row_block, in_w[0], preferred_element_type=jnp.float32)
    hidden_act = gelu_tanh(hidden_pre).astype(jnp.bfloat16)
    expert_rows = jnp.dot(hidden_act, out_w[0], preferred_element_type=jnp.float32).astype(
        jnp.bfloat16
    )
    returned = lax.all_to_all(
        expert_rows.reshape(experts, capacity, D),
        "expert",
        split_axis=0,
        concat_axis=0,
        tiled=True,
    )
    pair_rows = jnp.dot(
        pair_hot, returned.reshape(experts * capacity, D), preferred_element_type=jnp.float32
    ).reshape(TOP, tok_count, D)
    chosen = jnp.sum(route_hot * gate_probs[:, None, :], axis=-1)
    kept_gate = kept_mask.astype(jnp.float32).reshape(TOP, tok_count)
    weight_pair = kept_gate * chosen.T
    combined = jnp.sum(weight_pair[..., None] * pair_rows, axis=0)
    output = middle + combined
    saved_state = (
        residual,
        normed,
        heads,
        log_total,
        mixed_heads,
        middle,
        normed_two,
        gate_probs,
        kept_gate,
        weight_pair,
        pair_rows,
        row_block,
        hidden_pre,
    )
    return (output, saved_state)


def backward_layer(d_output, saved_state, route_hot, tables, weights, experts, capacity):
    (
        residual,
        normed,
        heads,
        log_total,
        mixed_heads,
        middle,
        normed_two,
        gate_probs,
        kept_gate,
        weight_pair,
        pair_rows,
        row_block,
        hidden_pre,
    ) = saved_state
    pair_hot, token_hot, kept_mask = tables
    norm_gains, norm_shifts, qkv_w, proj_w, router_w, in_w, out_w = weights
    tok_count = residual.shape[0]
    seq_count = tok_count // SEQ
    score_scale = HEAD ** (-0.5)
    norm_scale = norm_gains.astype(jnp.float32)
    norm_shift = norm_shifts.astype(jnp.float32)
    d_gate_pair = kept_gate * jnp.sum(d_output[None] * pair_rows, axis=-1)
    d_gates = jnp.sum(route_hot * d_gate_pair.T[:, :, None], axis=1)
    d_logits = (
        gate_probs * (d_gates - jnp.sum(gate_probs * d_gates, axis=-1, keepdims=True))
    ).astype(jnp.bfloat16)
    g_router = dot_first(normed_two, d_logits)
    d_normed_two = dot_last(d_logits, router_w)
    d_pairs = (
        (weight_pair[:, :, None] * d_output[None]).astype(jnp.bfloat16).reshape(TOP * tok_count, D)
    )
    d_slots = dot_first(pair_hot, d_pairs).astype(jnp.bfloat16).reshape(experts, capacity, D)
    d_expert_out = lax.all_to_all(d_slots, "expert", split_axis=0, concat_axis=0, tiled=True)
    flat_out = d_expert_out.reshape(experts * capacity, D)
    hidden_act = gelu_tanh(hidden_pre).astype(jnp.bfloat16)
    g_out = dot_first(hidden_act, flat_out)
    d_act = dot_last(flat_out, out_w[0])
    d_pre = jax.vjp(gelu_tanh, hidden_pre)[1](d_act)[0].astype(jnp.bfloat16)
    g_in = dot_first(row_block, d_pre)
    d_rows = dot_last(d_pre, in_w[0]).astype(jnp.bfloat16).reshape(experts, capacity, D)
    d_back = lax.all_to_all(d_rows, "expert", split_axis=0, concat_axis=0, tiled=True)
    d_pair_in = jnp.dot(
        pair_hot, d_back.reshape(experts * capacity, D), preferred_element_type=jnp.float32
    ).reshape(TOP, tok_count, D)
    d_normed_two = d_normed_two + jnp.sum(d_pair_in, axis=0)
    pulled_two = jax.vjp(layer_norm, middle, norm_scale[1], norm_shift[1])[1](d_normed_two)
    d_middle = d_output + pulled_two[0]
    d_branch = d_middle.astype(jnp.bfloat16)
    g_proj = dot_first(mixed_heads, d_branch)
    d_mixed = dot_last(d_branch, proj_w).astype(jnp.bfloat16).reshape(seq_count, SEQ, HEADS, HEAD)
    query_heads = heads[:, :, 0]
    key_heads = heads[:, :, 1]
    value_heads = heads[:, :, 2]
    scores = (
        jnp.einsum("sqhd,skhd->shqk", query_heads, key_heads, preferred_element_type=jnp.float32)
        * score_scale
    )
    soft_scores = jnp.exp(scores - log_total)
    d_soft = jnp.einsum("sqhd,skhd->shqk", d_mixed, value_heads, preferred_element_type=jnp.float32)
    d_values = jnp.einsum(
        "shqk,sqhd->skhd",
        soft_scores.astype(jnp.bfloat16),
        d_mixed,
        preferred_element_type=jnp.float32,
    )
    d_scores = (
        soft_scores * (d_soft - jnp.sum(soft_scores * d_soft, axis=-1, keepdims=True))
    ).astype(jnp.bfloat16)
    d_query = (
        jnp.einsum("shqk,skhd->sqhd", d_scores, key_heads, preferred_element_type=jnp.float32)
        * score_scale
    )
    d_keys = (
        jnp.einsum("shqk,sqhd->skhd", d_scores, query_heads, preferred_element_type=jnp.float32)
        * score_scale
    )
    d_qkv = (
        jnp.stack([d_query, d_keys, d_values], axis=2)
        .reshape(tok_count, 3 * D)
        .astype(jnp.bfloat16)
    )
    g_qkv = dot_first(normed, d_qkv)
    d_normed = dot_last(d_qkv, qkv_w)
    pulled_one = jax.vjp(layer_norm, residual, norm_scale[0], norm_shift[0])[1](d_normed)
    d_residual = d_middle + pulled_one[0]
    g_gain = jnp.stack([pulled_one[1], pulled_two[1]])
    g_shift = jnp.stack([pulled_one[2], pulled_two[2]])
    return (d_residual, (g_gain, g_shift, g_qkv, g_proj, g_router, g_in[None], g_out[None]))


def halving_scatter(grad, axis_name):
    size = lax.axis_size(axis_name)
    me = lax.axis_index(axis_name)
    chunk = grad.shape[0] // size
    rest = grad.shape[1:]
    total = grad.astype(jnp.float32).reshape(size, chunk, *rest)
    bit = 1
    while bit < size:
        pairs = total.reshape(total.shape[0] // 2, 2, chunk, *rest)
        mine = (me // bit) % 2
        keep = lax.dynamic_index_in_dim(pairs, mine, axis=1, keepdims=False)
        give = lax.dynamic_index_in_dim(pairs, 1 - mine, axis=1, keepdims=False)
        got = lax.ppermute(
            give.astype(jnp.bfloat16), axis_name, [(i, i ^ bit) for i in range(size)]
        )
        total = keep + got.astype(jnp.float32)
        bit *= 2
    return total.reshape(chunk, *rest)


def doubling_sum(part, axis_name):
    size = lax.axis_size(axis_name)
    total = part.astype(jnp.float32)
    bit = 1
    while bit < size:
        own = lax.reduce_precision(total, exponent_bits=8, mantissa_bits=7)
        got = lax.ppermute(
            own.astype(jnp.bfloat16), axis_name, [(i, i ^ bit) for i in range(size)]
        )
        total = own + got.astype(jnp.float32)
        bit *= 2
    return total


def doubling_gather(part, axis_name):
    size = lax.axis_size(axis_name)
    me = lax.axis_index(axis_name)
    held = part[None]
    bit = size // 2
    steps = 0
    while bit >= 1:
        got = lax.ppermute(held, axis_name, [(i, i ^ bit) for i in range(size)])
        low = (me // bit) % 2 == 0
        held = jnp.where(low, jnp.concatenate([held, got]), jnp.concatenate([got, held]))
        bit //= 2
        steps += 1
    held = held.reshape((2,) * steps + part.shape)
    held = held.transpose(tuple(reversed(range(steps))) + tuple(range(steps, held.ndim)))
    return held.reshape((size * part.shape[0],) + part.shape[1:])


def reduce_layer(layer_grads, late):
    g_gain, g_shift, g_qkv, g_proj, g_router, g_in, g_out = layer_grads
    qkv_cols = g_qkv.shape[1]
    proj_cols = g_proj.shape[1]
    small = jnp.concatenate([g_gain.T, g_shift.T, g_router], axis=1)
    shared = jnp.concatenate([g_qkv, g_proj, small], axis=1)
    shared = halving_scatter(shared, "shard")
    if late:
        owned = halving_scatter(shared, "expert")
        owned = lax.reduce_precision(owned, exponent_bits=8, mantissa_bits=7)
        shared = doubling_gather(owned.astype(jnp.bfloat16), "expert").astype(jnp.float32)
    else:
        shared = lax.psum(shared.astype(jnp.bfloat16), "expert").astype(jnp.float32)
    tail = shared[:, qkv_cols + proj_cols :]
    return [
        tail[:, 0:2].T,
        tail[:, 2:4].T,
        shared[:, :qkv_cols],
        shared[:, qkv_cols : qkv_cols + proj_cols],
        tail[:, 4:],
        halving_scatter(g_in[0], "shard")[None],
        halving_scatter(g_out[0], "shard")[None],
    ]


def local(
    tokens,
    routes,
    priority,
    norm_gain,
    norm_bias,
    w_qkv,
    w_proj,
    w_router,
    exp_in,
    exp_out,
    cotangent,
):
    experts = lax.axis_size("expert") * EXP_DEV
    capacity = max(8, (5 * TOK_MB // (2 * experts) + 7) // 8 * 8)
    tok_count = tokens.shape[0]
    blocks = tok_count // TOK_MB
    streams = []
    for block in range(blocks):
        rows = slice(block * TOK_MB, (block + 1) * TOK_MB)
        route_ids = routes[rows]
        tables = slot_onehot(route_ids, priority[rows], experts, capacity)
        route_hot = (
            route_ids[..., None] == jnp.arange(experts, dtype=jnp.int32)
        ).astype(jnp.float32)
        streams.append((rows, tables, route_hot))
    layer_count = norm_gain.shape[0]
    small = jnp.concatenate(
        [
            norm_gain.reshape(layer_count * 2, -1).T,
            norm_bias.reshape(layer_count * 2, -1).T,
            w_router.transpose(1, 0, 2).reshape(w_router.shape[1], -1),
        ],
        axis=1,
    )
    small = lax.all_gather(small, "shard", axis=0, tiled=True)
    qkv_cols = w_qkv.shape[2]
    all_weights = []
    for layer_index in range(LAYERS):
        attn = lax.all_gather(
            jnp.concatenate([w_qkv[layer_index], w_proj[layer_index]], axis=1),
            "shard",
            axis=0,
            tiled=True,
        )
        shift_at = 2 * layer_count + 2 * layer_index
        router_at = 4 * layer_count + experts * layer_index
        all_weights.append(
            (
                small[:, 2 * layer_index : 2 * layer_index + 2].T,
                small[:, shift_at : shift_at + 2].T,
                attn[:, :qkv_cols],
                attn[:, qkv_cols:],
                small[:, router_at : router_at + experts],
                lax.all_gather(exp_in[layer_index], "shard", axis=1, tiled=True),
                lax.all_gather(exp_out[layer_index], "shard", axis=1, tiled=True),
            )
        )
    residuals = [tokens[rows] for rows, _, _ in streams]
    saved = [[None] * LAYERS for _ in streams]
    for layer_index in range(LAYERS):
        for block, (rows, tables, route_hot) in enumerate(streams):
            residuals[block], saved[block][layer_index] = forward_layer(
                residuals[block], route_hot, tables, all_weights[layer_index], experts, capacity
            )
    activations = jnp.concatenate(residuals, axis=0)
    d_residuals = [cotangent[rows] for rows, _, _ in streams]
    reduced = [None] * LAYERS
    for layer_index in reversed(range(LAYERS)):
        layer_sum = None
        for block, (rows, tables, route_hot) in enumerate(streams):
            d_residuals[block], layer_grads = backward_layer(
                d_residuals[block],
                saved[block][layer_index],
                route_hot,
                tables,
                all_weights[layer_index],
                experts,
                capacity,
            )
            if layer_sum is None:
                layer_sum = layer_grads
            else:
                layer_sum = tuple(old + new for old, new in zip(layer_sum, layer_grads))
        reduced[layer_index] = reduce_layer(layer_sum, layer_index == 0)
    outs = [jnp.stack([reduced[l][k] for l in range(LAYERS)]) for k in range(7)]
    d_tokens = jnp.concatenate(d_residuals, axis=0)
    return (activations, d_tokens, *outs)


def solution(mesh):
    return jax.shard_map(
        local,
        mesh=mesh,
        in_specs=(
            P(("expert", "shard"), None),
            P(("expert", "shard"), None),
            P(("expert", "shard")),
            P(None, None, "shard"),
            P(None, None, "shard"),
            P(None, "shard", None),
            P(None, "shard", None),
            P(None, "shard", None),
            P(None, "expert", "shard", None),
            P(None, "expert", "shard", None),
            P(("expert", "shard"), None),
        ),
        out_specs=(
            P(("expert", "shard"), None),
            P(("expert", "shard"), None),
            P(None, None, "shard"),
            P(None, None, "shard"),
            P(None, "shard", None),
            P(None, "shard", None),
            P(None, "shard", None),
            P(None, "expert", "shard", None),
            P(None, "expert", "shard", None),
        ),
        check_vma=False,
    )
```

```python
import jax
import jax.numpy as jnp
from jax import lax
from jax.sharding import PartitionSpec as P


D = 512
HEADS = 8
HEAD = 64
EXP_DEV = 1
SEQ = 197
LAYERS = 2
TOP = 2
TOK_MB = 394


norm_eps = 1e-06


def layer_norm(values, norm_scale, norm_shift):
    centre = values - jnp.mean(values, axis=-1, keepdims=True)
    spread = jnp.mean(centre * centre, axis=-1, keepdims=True)
    return centre * lax.rsqrt(spread + norm_eps) * norm_scale + norm_shift


def gelu_tanh(values):
    return jax.nn.gelu(values, approximate=True)


def dot_first(left, right):
    return lax.dot_general(
        left, right, (((0,), (0,)), ((), ())), preferred_element_type=jnp.float32
    )


def dot_last(left, right):
    return lax.dot_general(
        left, right, (((1,), (1,)), ((), ())), preferred_element_type=jnp.float32
    )


def slot_onehot(route_ids, prio_rank, experts, capacity):
    tok_count = route_ids.shape[0]
    order_key = jnp.concatenate([prio_rank, prio_rank + tok_count])
    pair_expert = jnp.concatenate([route_ids[:, 0], route_ids[:, 1]])
    expert_hot = (pair_expert[:, None] == jnp.arange(experts, dtype=jnp.int32)[None, :]).astype(
        jnp.bfloat16
    )
    earlier = (order_key[:, None] < order_key[None, :]).astype(jnp.bfloat16)
    counts = dot_first(expert_hot, earlier)
    position = jnp.sum(counts.T * expert_hot.astype(jnp.float32), axis=1).astype(jnp.int32)
    kept_mask = position < capacity
    flat_slot = jnp.where(kept_mask, pair_expert * capacity + position, experts * capacity)
    pair_hot = (
        flat_slot[:, None] == jnp.arange(experts * capacity, dtype=jnp.int32)[None, :]
    ).astype(jnp.bfloat16)
    token_hot = pair_hot[:tok_count] + pair_hot[tok_count:]
    return pair_hot, token_hot, kept_mask


def exchange(blocks, axis_name):
    return lax.all_to_all(blocks, axis_name, split_axis=0, concat_axis=0, tiled=True)


def forward_attend(residual, tables, weights):
    norm_gains, norm_shifts, qkv_w, proj_w, router_w, _, _ = weights
    _, token_hot, _ = tables
    tok_count = residual.shape[0]
    seq_count = tok_count // SEQ
    score_scale = HEAD ** (-0.5)
    norm_scale = norm_gains.astype(jnp.float32)
    norm_shift = norm_shifts.astype(jnp.float32)
    normed = layer_norm(residual, norm_scale[0], norm_shift[0]).astype(jnp.bfloat16)
    qkv_rows = jnp.dot(normed, qkv_w, preferred_element_type=jnp.float32).astype(jnp.bfloat16)
    heads = qkv_rows.reshape(seq_count, SEQ, 3, HEADS, HEAD)
    scores = (
        jnp.einsum(
            "sqhd,skhd->shqk", heads[:, :, 0], heads[:, :, 1], preferred_element_type=jnp.float32
        )
        * score_scale
    )
    row_top = jnp.max(scores, axis=-1, keepdims=True)
    scores_exp = jnp.exp(scores - row_top)
    row_total = jnp.sum(scores_exp, axis=-1, keepdims=True)
    soft_scores = scores_exp / row_total
    log_total = row_top + jnp.log(row_total)
    mixed_heads = jnp.einsum(
        "shqk,skhd->sqhd",
        soft_scores.astype(jnp.bfloat16),
        heads[:, :, 2],
        preferred_element_type=jnp.float32,
    )
    mixed_heads = mixed_heads.astype(jnp.bfloat16).reshape(tok_count, D)
    middle = residual + jnp.dot(mixed_heads, proj_w, preferred_element_type=jnp.float32)
    normed_two = layer_norm(middle, norm_scale[1], norm_shift[1]).astype(jnp.bfloat16)
    gate_probs = jax.nn.softmax(
        jnp.dot(normed_two, router_w, preferred_element_type=jnp.float32), axis=-1
    )
    sending = dot_first(token_hot, normed_two).astype(jnp.bfloat16)
    carry = (residual, normed, heads, log_total, mixed_heads, middle, normed_two, gate_probs)
    return carry, sending


def forward_expert(carry, sending, route_hot, tables, weights, experts, capacity):
    _, _, _, _, _, in_w, out_w = weights
    received = exchange(sending.reshape(experts, capacity, D), "expert")
    row_block = received.reshape(experts * capacity, D)
    hidden_pre = jnp.dot(row_block, in_w[0], preferred_element_type=jnp.float32)
    hidden_act = gelu_tanh(hidden_pre).astype(jnp.bfloat16)
    expert_rows = jnp.dot(hidden_act, out_w[0], preferred_element_type=jnp.float32).astype(
        jnp.bfloat16
    )
    returned = exchange(expert_rows.reshape(experts, capacity, D), "expert")
    return forward_combine(
        carry, returned, row_block, hidden_pre, route_hot, tables, experts, capacity
    )


def forward_combine(carry, returned, row_block, hidden_pre, route_hot, tables, experts, capacity):
    residual, normed, heads, log_total, mixed_heads, middle, normed_two, gate_probs = carry
    pair_hot, _, kept_mask = tables
    tok_count = residual.shape[0]
    pair_rows = jnp.dot(
        pair_hot, returned.reshape(experts * capacity, D), preferred_element_type=jnp.float32
    ).reshape(TOP, tok_count, D)
    chosen = jnp.sum(route_hot * gate_probs[:, None, :], axis=-1)
    kept_gate = kept_mask.astype(jnp.float32).reshape(TOP, tok_count)
    weight_pair = kept_gate * chosen.T
    combined = jnp.sum(weight_pair[..., None] * pair_rows, axis=0)
    output = middle + combined
    saved_state = (
        residual,
        normed,
        heads,
        log_total,
        mixed_heads,
        middle,
        normed_two,
        gate_probs,
        kept_gate,
        weight_pair,
        pair_rows,
        row_block,
        hidden_pre,
    )
    return (output, saved_state)


def backward_layer(d_output, saved_state, route_hot, tables, weights, experts, capacity):
    (_, _, _, _, _, _, _, _, _, _, _, row_block, hidden_pre) = saved_state
    _, _, _, _, router_w, in_w, out_w = weights
    d_slots, g_router, d_normed_two = backward_route(
        d_output, saved_state, tables, route_hot, router_w, experts, capacity
    )
    d_expert_out = exchange(d_slots, "expert")
    flat_out = d_expert_out.reshape(experts * capacity, D)
    hidden_act = gelu_tanh(hidden_pre).astype(jnp.bfloat16)
    g_out = dot_first(hidden_act, flat_out)
    d_act = dot_last(flat_out, out_w[0])
    d_pre = jax.vjp(gelu_tanh, hidden_pre)[1](d_act)[0].astype(jnp.bfloat16)
    g_in = dot_first(row_block, d_pre)
    d_rows = dot_last(d_pre, in_w[0]).astype(jnp.bfloat16).reshape(experts, capacity, D)
    d_back = exchange(d_rows, "expert")
    d_residual, grads = backward_attend(
        d_output, saved_state, d_back, d_normed_two, tables, weights, experts, capacity
    )
    g_gain, g_shift, g_qkv, g_proj = grads
    return (d_residual, (g_gain, g_shift, g_qkv, g_proj, g_router, g_in[None], g_out[None]))


def backward_route(d_output, saved_state, tables, route_hot, router_w, experts, capacity):
    (
        residual, _, _, _, _, _, normed_two, gate_probs, kept_gate, weight_pair, pair_rows, _, _
    ) = saved_state
    pair_hot, _, _ = tables
    tok_count = residual.shape[0]
    d_gate_pair = kept_gate * jnp.sum(d_output[None] * pair_rows, axis=-1)
    d_gates = jnp.sum(route_hot * d_gate_pair.T[:, :, None], axis=1)
    d_logits = (
        gate_probs * (d_gates - jnp.sum(gate_probs * d_gates, axis=-1, keepdims=True))
    ).astype(jnp.bfloat16)
    g_router = dot_first(normed_two, d_logits)
    d_normed_two = dot_last(d_logits, router_w)
    d_pairs = (
        (weight_pair[:, :, None] * d_output[None]).astype(jnp.bfloat16).reshape(TOP * tok_count, D)
    )
    d_slots = dot_first(pair_hot, d_pairs).astype(jnp.bfloat16).reshape(experts, capacity, D)
    return d_slots, g_router, d_normed_two


def backward_attend(d_output, saved_state, d_back, d_normed_two, tables, weights, experts, capacity):
    (residual, normed, heads, log_total, mixed_heads, middle, _, _, _, _, _, _, _) = saved_state
    pair_hot, _, _ = tables
    norm_gains, norm_shifts, qkv_w, proj_w, _, _, _ = weights
    tok_count = residual.shape[0]
    seq_count = tok_count // SEQ
    score_scale = HEAD ** (-0.5)
    norm_scale = norm_gains.astype(jnp.float32)
    norm_shift = norm_shifts.astype(jnp.float32)
    d_pair_in = jnp.dot(
        pair_hot, d_back.reshape(experts * capacity, D), preferred_element_type=jnp.float32
    ).reshape(TOP, tok_count, D)
    d_normed_two = d_normed_two + jnp.sum(d_pair_in, axis=0)
    pulled_two = jax.vjp(layer_norm, middle, norm_scale[1], norm_shift[1])[1](d_normed_two)
    d_middle = d_output + pulled_two[0]
    d_branch = d_middle.astype(jnp.bfloat16)
    g_proj = dot_first(mixed_heads, d_branch)
    d_mixed = dot_last(d_branch, proj_w).astype(jnp.bfloat16).reshape(seq_count, SEQ, HEADS, HEAD)
    query_heads = heads[:, :, 0]
    key_heads = heads[:, :, 1]
    value_heads = heads[:, :, 2]
    scores = (
        jnp.einsum("sqhd,skhd->shqk", query_heads, key_heads, preferred_element_type=jnp.float32)
        * score_scale
    )
    soft_scores = jnp.exp(scores - log_total)
    d_soft = jnp.einsum("sqhd,skhd->shqk", d_mixed, value_heads, preferred_element_type=jnp.float32)
    d_values = jnp.einsum(
        "shqk,sqhd->skhd",
        soft_scores.astype(jnp.bfloat16),
        d_mixed,
        preferred_element_type=jnp.float32,
    )
    d_scores = (
        soft_scores * (d_soft - jnp.sum(soft_scores * d_soft, axis=-1, keepdims=True))
    ).astype(jnp.bfloat16)
    d_query = (
        jnp.einsum("shqk,skhd->sqhd", d_scores, key_heads, preferred_element_type=jnp.float32)
        * score_scale
    )
    d_keys = (
        jnp.einsum("shqk,sqhd->skhd", d_scores, query_heads, preferred_element_type=jnp.float32)
        * score_scale
    )
    d_qkv = (
        jnp.stack([d_query, d_keys, d_values], axis=2)
        .reshape(tok_count, 3 * D)
        .astype(jnp.bfloat16)
    )
    g_qkv = dot_first(normed, d_qkv)
    d_normed = dot_last(d_qkv, qkv_w)
    pulled_one = jax.vjp(layer_norm, residual, norm_scale[0], norm_shift[0])[1](d_normed)
    d_residual = d_middle + pulled_one[0]
    g_gain = jnp.stack([pulled_one[1], pulled_two[1]])
    g_shift = jnp.stack([pulled_one[2], pulled_two[2]])
    return d_residual, (g_gain, g_shift, g_qkv, g_proj)


def halving_scatter(grad, axis_name):
    size = lax.axis_size(axis_name)
    me = lax.axis_index(axis_name)
    chunk = grad.shape[0] // size
    rest = grad.shape[1:]
    total = grad.astype(jnp.float32).reshape(size, chunk, *rest)
    bit = 1
    while bit < size:
        pairs = total.reshape(total.shape[0] // 2, 2, chunk, *rest)
        mine = (me // bit) % 2
        keep = lax.dynamic_index_in_dim(pairs, mine, axis=1, keepdims=False)
        give = lax.dynamic_index_in_dim(pairs, 1 - mine, axis=1, keepdims=False)
        got = lax.ppermute(
            give.astype(jnp.bfloat16), axis_name, [(i, i ^ bit) for i in range(size)]
        )
        total = keep + got.astype(jnp.float32)
        bit *= 2
    return total.reshape(chunk, *rest)


def doubling_gather(part, axis_name):
    size = lax.axis_size(axis_name)
    me = lax.axis_index(axis_name)
    held = part[None]
    bit = size // 2
    steps = 0
    while bit >= 1:
        got = lax.ppermute(held, axis_name, [(i, i ^ bit) for i in range(size)])
        low = (me // bit) % 2 == 0
        held = jnp.where(low, jnp.concatenate([held, got]), jnp.concatenate([got, held]))
        bit //= 2
        steps += 1
    held = held.reshape((2,) * steps + part.shape)
    held = held.transpose(tuple(reversed(range(steps))) + tuple(range(steps, held.ndim)))
    return held.reshape((size * part.shape[0],) + part.shape[1:])


def reduce_layer(layer_grads, late):
    g_gain, g_shift, g_qkv, g_proj, g_router, g_in, g_out = layer_grads
    qkv_cols = g_qkv.shape[1]
    proj_cols = g_proj.shape[1]
    small = jnp.concatenate([g_gain.T, g_shift.T, g_router], axis=1)
    shared = jnp.concatenate([g_qkv, g_proj, small], axis=1)
    shared = halving_scatter(shared, "shard")
    if late:
        owned = halving_scatter(shared, "expert")
        owned = lax.reduce_precision(owned, exponent_bits=8, mantissa_bits=7)
        shared = doubling_gather(owned.astype(jnp.bfloat16), "expert").astype(jnp.float32)
    else:
        shared = lax.psum(shared.astype(jnp.bfloat16), "expert").astype(jnp.float32)
    tail = shared[:, qkv_cols + proj_cols :]
    return [
        tail[:, 0:2].T,
        tail[:, 2:4].T,
        shared[:, :qkv_cols],
        shared[:, qkv_cols : qkv_cols + proj_cols],
        tail[:, 4:],
        halving_scatter(g_in[0], "shard")[None],
        halving_scatter(g_out[0], "shard")[None],
    ]


def local(
    tokens,
    routes,
    priority,
    norm_gain,
    norm_bias,
    w_qkv,
    w_proj,
    w_router,
    exp_in,
    exp_out,
    cotangent,
):
    experts = lax.axis_size("expert") * EXP_DEV
    capacity = max(8, (5 * TOK_MB // (2 * experts) + 7) // 8 * 8)
    tok_count = tokens.shape[0]
    blocks = tok_count // TOK_MB
    streams = []
    for block in range(blocks):
        rows = slice(block * TOK_MB, (block + 1) * TOK_MB)
        route_ids = routes[rows]
        tables = slot_onehot(route_ids, priority[rows], experts, capacity)
        route_hot = (
            route_ids[..., None] == jnp.arange(experts, dtype=jnp.int32)
        ).astype(jnp.float32)
        streams.append((rows, tables, route_hot))
    layer_count = norm_gain.shape[0]
    small = jnp.concatenate(
        [
            norm_gain.reshape(layer_count * 2, -1).T,
            norm_bias.reshape(layer_count * 2, -1).T,
            w_router.transpose(1, 0, 2).reshape(w_router.shape[1], -1),
        ],
        axis=1,
    )
    small = lax.all_gather(small, "shard", axis=0, tiled=True)
    qkv_cols = w_qkv.shape[2]
    all_weights = []
    for layer_index in range(LAYERS):
        attn = lax.all_gather(
            jnp.concatenate([w_qkv[layer_index], w_proj[layer_index]], axis=1),
            "shard",
            axis=0,
            tiled=True,
        )
        shift_at = 2 * layer_count + 2 * layer_index
        router_at = 4 * layer_count + experts * layer_index
        all_weights.append(
            (
                small[:, 2 * layer_index : 2 * layer_index + 2].T,
                small[:, shift_at : shift_at + 2].T,
                attn[:, :qkv_cols],
                attn[:, qkv_cols:],
                small[:, router_at : router_at + experts],
                lax.all_gather(exp_in[layer_index], "shard", axis=1, tiled=True),
                lax.all_gather(exp_out[layer_index], "shard", axis=1, tiled=True),
            )
        )
    residuals = [tokens[rows] for rows, _, _ in streams]
    saved = [[None] * LAYERS for _ in streams]
    for layer_index in range(LAYERS):
        staged = []
        for block, (rows, tables, route_hot) in enumerate(streams):
            own_weights, own_rows = lax.optimization_barrier(
                (all_weights[layer_index], residuals[block])
            )
            staged.append(forward_attend(own_rows, tables, own_weights))
        for block, (rows, tables, route_hot) in enumerate(streams):
            carry, sending = staged[block]
            residuals[block], saved[block][layer_index] = forward_expert(
                carry, sending, route_hot, tables, all_weights[layer_index], experts, capacity
            )
    activations = jnp.concatenate(residuals, axis=0)
    d_residuals = [cotangent[rows] for rows, _, _ in streams]
    reduced = [None] * LAYERS
    for layer_index in reversed(range(LAYERS)):
        layer_sum = None
        for block, (rows, tables, route_hot) in enumerate(streams):
            d_residuals[block], layer_grads = backward_layer(
                d_residuals[block],
                saved[block][layer_index],
                route_hot,
                tables,
                all_weights[layer_index],
                experts,
                capacity,
            )
            if layer_sum is None:
                layer_sum = layer_grads
            else:
                layer_sum = tuple(old + new for old, new in zip(layer_sum, layer_grads))
        reduced[layer_index] = reduce_layer(layer_sum, layer_index == 0)
    outs = [jnp.stack([reduced[l][k] for l in range(LAYERS)]) for k in range(7)]
    d_tokens = jnp.concatenate(d_residuals, axis=0)
    return (activations, d_tokens, *outs)


def solution(mesh):
    return jax.shard_map(
        local,
        mesh=mesh,
        in_specs=(
            P(("expert", "shard"), None),
            P(("expert", "shard"), None),
            P(("expert", "shard")),
            P(None, None, "shard"),
            P(None, None, "shard"),
            P(None, "shard", None),
            P(None, "shard", None),
            P(None, "shard", None),
            P(None, "expert", "shard", None),
            P(None, "expert", "shard", None),
            P(("expert", "shard"), None),
        ),
        out_specs=(
            P(("expert", "shard"), None),
            P(("expert", "shard"), None),
            P(None, None, "shard"),
            P(None, None, "shard"),
            P(None, "shard", None),
            P(None, "shard", None),
            P(None, "shard", None),
            P(None, "expert", "shard", None),
            P(None, "expert", "shard", None),
        ),
        check_vma=False,
    )
```

```python
import jax
import jax.numpy as jnp
from jax import lax
from jax.sharding import PartitionSpec as P


D = 512
HEADS = 8
HEAD = 64
EXP_DEV = 1
SEQ = 197
LAYERS = 2
TOP = 2
TOK_MB = 394


norm_eps = 1e-06


def layer_norm(values, norm_scale, norm_shift):
    centre = values - jnp.mean(values, axis=-1, keepdims=True)
    spread = jnp.mean(centre * centre, axis=-1, keepdims=True)
    return centre * lax.rsqrt(spread + norm_eps) * norm_scale + norm_shift


def gelu_tanh(values):
    return jax.nn.gelu(values, approximate=True)


def dot_first(left, right):
    return lax.dot_general(
        left, right, (((0,), (0,)), ((), ())), preferred_element_type=jnp.float32
    )


def dot_last(left, right):
    return lax.dot_general(
        left, right, (((1,), (1,)), ((), ())), preferred_element_type=jnp.float32
    )


def slot_onehot(route_ids, prio_rank, experts, capacity):
    tok_count = route_ids.shape[0]
    order_key = jnp.concatenate([prio_rank, prio_rank + tok_count])
    pair_expert = jnp.concatenate([route_ids[:, 0], route_ids[:, 1]])
    expert_hot = (pair_expert[:, None] == jnp.arange(experts, dtype=jnp.int32)[None, :]).astype(
        jnp.bfloat16
    )
    earlier = (order_key[:, None] < order_key[None, :]).astype(jnp.bfloat16)
    counts = dot_first(expert_hot, earlier)
    position = jnp.sum(counts.T * expert_hot.astype(jnp.float32), axis=1).astype(jnp.int32)
    kept_mask = position < capacity
    flat_slot = jnp.where(kept_mask, pair_expert * capacity + position, experts * capacity)
    pair_hot = (
        flat_slot[:, None] == jnp.arange(experts * capacity, dtype=jnp.int32)[None, :]
    ).astype(jnp.bfloat16)
    token_hot = pair_hot[:tok_count] + pair_hot[tok_count:]
    return pair_hot, token_hot, kept_mask


def exchange(blocks, axis_name):
    return lax.all_to_all(blocks, axis_name, split_axis=0, concat_axis=0, tiled=True)


def forward_attend(residual, tables, weights):
    norm_gains, norm_shifts, qkv_w, proj_w, router_w, _, _ = weights
    _, token_hot, _ = tables
    tok_count = residual.shape[0]
    seq_count = tok_count // SEQ
    score_scale = HEAD ** (-0.5)
    norm_scale = norm_gains.astype(jnp.float32)
    norm_shift = norm_shifts.astype(jnp.float32)
    normed = layer_norm(residual, norm_scale[0], norm_shift[0]).astype(jnp.bfloat16)
    qkv_rows = jnp.dot(normed, qkv_w, preferred_element_type=jnp.float32).astype(jnp.bfloat16)
    heads = qkv_rows.reshape(seq_count, SEQ, 3, HEADS, HEAD)
    scores = (
        jnp.einsum(
            "sqhd,skhd->shqk", heads[:, :, 0], heads[:, :, 1], preferred_element_type=jnp.float32
        )
        * score_scale
    )
    row_top = jnp.max(scores, axis=-1, keepdims=True)
    scores_exp = jnp.exp(scores - row_top)
    row_total = jnp.sum(scores_exp, axis=-1, keepdims=True)
    soft_scores = scores_exp / row_total
    log_total = row_top + jnp.log(row_total)
    mixed_heads = jnp.einsum(
        "shqk,skhd->sqhd",
        soft_scores.astype(jnp.bfloat16),
        heads[:, :, 2],
        preferred_element_type=jnp.float32,
    )
    mixed_heads = mixed_heads.astype(jnp.bfloat16).reshape(tok_count, D)
    middle = residual + jnp.dot(mixed_heads, proj_w, preferred_element_type=jnp.float32)
    normed_two = layer_norm(middle, norm_scale[1], norm_shift[1]).astype(jnp.bfloat16)
    gate_probs = jax.nn.softmax(
        jnp.dot(normed_two, router_w, preferred_element_type=jnp.float32), axis=-1
    )
    sending = dot_first(token_hot, normed_two).astype(jnp.bfloat16)
    carry = (residual, normed, heads, log_total, mixed_heads, middle, normed_two, gate_probs)
    return carry, sending


def forward_expert(carry, sending, route_hot, tables, weights, experts, capacity):
    _, _, _, _, _, in_w, out_w = weights
    received = exchange(sending.reshape(experts, capacity, D), "expert")
    row_block = received.reshape(experts * capacity, D)
    hidden_pre = jnp.dot(row_block, in_w[0], preferred_element_type=jnp.float32)
    hidden_act = gelu_tanh(hidden_pre).astype(jnp.bfloat16)
    expert_rows = jnp.dot(hidden_act, out_w[0], preferred_element_type=jnp.float32).astype(
        jnp.bfloat16
    )
    returned = exchange(expert_rows.reshape(experts, capacity, D), "expert")
    return forward_combine(
        carry, returned, row_block, hidden_pre, route_hot, tables, experts, capacity
    )


def forward_combine(carry, returned, row_block, hidden_pre, route_hot, tables, experts, capacity):
    residual, normed, heads, log_total, mixed_heads, middle, normed_two, gate_probs = carry
    pair_hot, _, kept_mask = tables
    tok_count = residual.shape[0]
    pair_rows = jnp.dot(
        pair_hot, returned.reshape(experts * capacity, D), preferred_element_type=jnp.float32
    ).reshape(TOP, tok_count, D)
    chosen = jnp.sum(route_hot * gate_probs[:, None, :], axis=-1)
    kept_gate = kept_mask.astype(jnp.float32).reshape(TOP, tok_count)
    weight_pair = kept_gate * chosen.T
    combined = jnp.sum(weight_pair[..., None] * pair_rows, axis=0)
    output = middle + combined
    saved_state = (
        residual,
        normed,
        heads,
        log_total,
        mixed_heads,
        middle,
        normed_two,
        gate_probs,
        kept_gate,
        weight_pair,
        pair_rows,
        row_block,
        hidden_pre,
    )
    return (output, saved_state)


def backward_layer(d_output, saved_state, route_hot, tables, weights, experts, capacity):
    (_, _, _, _, _, _, _, _, _, _, _, row_block, hidden_pre) = saved_state
    _, _, _, _, router_w, in_w, out_w = weights
    d_slots, g_router, d_normed_two = backward_route(
        d_output, saved_state, tables, route_hot, router_w, experts, capacity
    )
    d_expert_out = exchange(d_slots, "expert")
    flat_out = d_expert_out.reshape(experts * capacity, D)
    hidden_act = gelu_tanh(hidden_pre).astype(jnp.bfloat16)
    g_out = dot_first(hidden_act, flat_out)
    d_act = dot_last(flat_out, out_w[0])
    d_pre = jax.vjp(gelu_tanh, hidden_pre)[1](d_act)[0].astype(jnp.bfloat16)
    g_in = dot_first(row_block, d_pre)
    d_rows = dot_last(d_pre, in_w[0]).astype(jnp.bfloat16).reshape(experts, capacity, D)
    d_back = exchange(d_rows, "expert")
    d_residual, grads = backward_attend(
        d_output, saved_state, d_back, d_normed_two, tables, weights, experts, capacity
    )
    g_gain, g_shift, g_qkv, g_proj = grads
    return (d_residual, (g_gain, g_shift, g_qkv, g_proj, g_router, g_in[None], g_out[None]))


def backward_route(d_output, saved_state, tables, route_hot, router_w, experts, capacity):
    (
        residual, _, _, _, _, _, normed_two, gate_probs, kept_gate, weight_pair, pair_rows, _, _
    ) = saved_state
    pair_hot, _, _ = tables
    tok_count = residual.shape[0]
    d_gate_pair = kept_gate * jnp.sum(d_output[None] * pair_rows, axis=-1)
    d_gates = jnp.sum(route_hot * d_gate_pair.T[:, :, None], axis=1)
    d_logits = (
        gate_probs * (d_gates - jnp.sum(gate_probs * d_gates, axis=-1, keepdims=True))
    ).astype(jnp.bfloat16)
    g_router = dot_first(normed_two, d_logits)
    d_normed_two = dot_last(d_logits, router_w)
    d_pairs = (
        (weight_pair[:, :, None] * d_output[None]).astype(jnp.bfloat16).reshape(TOP * tok_count, D)
    )
    d_slots = dot_first(pair_hot, d_pairs).astype(jnp.bfloat16).reshape(experts, capacity, D)
    return d_slots, g_router, d_normed_two


def backward_attend(d_output, saved_state, d_back, d_normed_two, tables, weights, experts, capacity):
    (residual, normed, heads, log_total, mixed_heads, middle, _, _, _, _, _, _, _) = saved_state
    pair_hot, _, _ = tables
    norm_gains, norm_shifts, qkv_w, proj_w, _, _, _ = weights
    tok_count = residual.shape[0]
    seq_count = tok_count // SEQ
    score_scale = HEAD ** (-0.5)
    norm_scale = norm_gains.astype(jnp.float32)
    norm_shift = norm_shifts.astype(jnp.float32)
    d_pair_in = jnp.dot(
        pair_hot, d_back.reshape(experts * capacity, D), preferred_element_type=jnp.float32
    ).reshape(TOP, tok_count, D)
    d_normed_two = d_normed_two + jnp.sum(d_pair_in, axis=0)
    pulled_two = jax.vjp(layer_norm, middle, norm_scale[1], norm_shift[1])[1](d_normed_two)
    d_middle = d_output + pulled_two[0]
    d_branch = d_middle.astype(jnp.bfloat16)
    g_proj = dot_first(mixed_heads, d_branch)
    d_mixed = dot_last(d_branch, proj_w).astype(jnp.bfloat16).reshape(seq_count, SEQ, HEADS, HEAD)
    query_heads = heads[:, :, 0]
    key_heads = heads[:, :, 1]
    value_heads = heads[:, :, 2]
    scores = (
        jnp.einsum("sqhd,skhd->shqk", query_heads, key_heads, preferred_element_type=jnp.float32)
        * score_scale
    )
    soft_scores = jnp.exp(scores - log_total)
    d_soft = jnp.einsum("sqhd,skhd->shqk", d_mixed, value_heads, preferred_element_type=jnp.float32)
    d_values = jnp.einsum(
        "shqk,sqhd->skhd",
        soft_scores.astype(jnp.bfloat16),
        d_mixed,
        preferred_element_type=jnp.float32,
    )
    d_scores = (
        soft_scores * (d_soft - jnp.sum(soft_scores * d_soft, axis=-1, keepdims=True))
    ).astype(jnp.bfloat16)
    d_query = (
        jnp.einsum("shqk,skhd->sqhd", d_scores, key_heads, preferred_element_type=jnp.float32)
        * score_scale
    )
    d_keys = (
        jnp.einsum("shqk,sqhd->skhd", d_scores, query_heads, preferred_element_type=jnp.float32)
        * score_scale
    )
    d_qkv = (
        jnp.stack([d_query, d_keys, d_values], axis=2)
        .reshape(tok_count, 3 * D)
        .astype(jnp.bfloat16)
    )
    g_qkv = dot_first(normed, d_qkv)
    d_normed = dot_last(d_qkv, qkv_w)
    pulled_one = jax.vjp(layer_norm, residual, norm_scale[0], norm_shift[0])[1](d_normed)
    d_residual = d_middle + pulled_one[0]
    g_gain = jnp.stack([pulled_one[1], pulled_two[1]])
    g_shift = jnp.stack([pulled_one[2], pulled_two[2]])
    return d_residual, (g_gain, g_shift, g_qkv, g_proj)


def halving_scatter(grad, axis_name):
    size = lax.axis_size(axis_name)
    me = lax.axis_index(axis_name)
    chunk = grad.shape[0] // size
    rest = grad.shape[1:]
    total = grad.astype(jnp.float32).reshape(size, chunk, *rest)
    bit = 1
    while bit < size:
        pairs = total.reshape(total.shape[0] // 2, 2, chunk, *rest)
        mine = (me // bit) % 2
        keep = lax.dynamic_index_in_dim(pairs, mine, axis=1, keepdims=False)
        give = lax.dynamic_index_in_dim(pairs, 1 - mine, axis=1, keepdims=False)
        got = lax.ppermute(
            give.astype(jnp.bfloat16), axis_name, [(i, i ^ bit) for i in range(size)]
        )
        total = keep + got.astype(jnp.float32)
        bit *= 2
    return total.reshape(chunk, *rest)


def doubling_gather(part, axis_name):
    size = lax.axis_size(axis_name)
    me = lax.axis_index(axis_name)
    held = part[None]
    bit = size // 2
    steps = 0
    while bit >= 1:
        got = lax.ppermute(held, axis_name, [(i, i ^ bit) for i in range(size)])
        low = (me // bit) % 2 == 0
        held = jnp.where(low, jnp.concatenate([held, got]), jnp.concatenate([got, held]))
        bit //= 2
        steps += 1
    held = held.reshape((2,) * steps + part.shape)
    held = held.transpose(tuple(reversed(range(steps))) + tuple(range(steps, held.ndim)))
    return held.reshape((size * part.shape[0],) + part.shape[1:])


def reduce_layer(layer_grads, late):
    g_gain, g_shift, g_qkv, g_proj, g_router, g_in, g_out = layer_grads
    qkv_cols = g_qkv.shape[1]
    proj_cols = g_proj.shape[1]
    small = jnp.concatenate([g_gain.T, g_shift.T, g_router], axis=1)
    shared = jnp.concatenate([g_qkv, g_proj, small], axis=1)
    shared = halving_scatter(shared, "shard")
    if late:
        owned = halving_scatter(shared, "expert")
        owned = lax.reduce_precision(owned, exponent_bits=8, mantissa_bits=7)
        shared = doubling_gather(owned.astype(jnp.bfloat16), "expert").astype(jnp.float32)
    else:
        shared = lax.psum(shared.astype(jnp.bfloat16), "expert").astype(jnp.float32)
    tail = shared[:, qkv_cols + proj_cols :]
    return [
        tail[:, 0:2].T,
        tail[:, 2:4].T,
        shared[:, :qkv_cols],
        shared[:, qkv_cols : qkv_cols + proj_cols],
        tail[:, 4:],
        halving_scatter(g_in[0], "shard")[None],
        halving_scatter(g_out[0], "shard")[None],
    ]


def local(
    tokens,
    routes,
    priority,
    norm_gain,
    norm_bias,
    w_qkv,
    w_proj,
    w_router,
    exp_in,
    exp_out,
    cotangent,
):
    experts = lax.axis_size("expert") * EXP_DEV
    capacity = max(8, (5 * TOK_MB // (2 * experts) + 7) // 8 * 8)
    tok_count = tokens.shape[0]
    blocks = tok_count // TOK_MB
    streams = []
    for block in range(blocks):
        rows = slice(block * TOK_MB, (block + 1) * TOK_MB)
        route_ids = routes[rows]
        tables = slot_onehot(route_ids, priority[rows], experts, capacity)
        route_hot = (
            route_ids[..., None] == jnp.arange(experts, dtype=jnp.int32)
        ).astype(jnp.float32)
        streams.append((rows, tables, route_hot))
    layer_count = norm_gain.shape[0]
    small = jnp.concatenate(
        [
            norm_gain.reshape(layer_count * 2, -1).T,
            norm_bias.reshape(layer_count * 2, -1).T,
            w_router.transpose(1, 0, 2).reshape(w_router.shape[1], -1),
        ],
        axis=1,
    )
    small = lax.all_gather(small, "shard", axis=0, tiled=True)
    qkv_cols = w_qkv.shape[2]
    all_weights = []
    for layer_index in range(LAYERS):
        attn = lax.all_gather(
            jnp.concatenate([w_qkv[layer_index], w_proj[layer_index]], axis=1),
            "shard",
            axis=0,
            tiled=True,
        )
        shift_at = 2 * layer_count + 2 * layer_index
        router_at = 4 * layer_count + experts * layer_index
        all_weights.append(
            (
                small[:, 2 * layer_index : 2 * layer_index + 2].T,
                small[:, shift_at : shift_at + 2].T,
                attn[:, :qkv_cols],
                attn[:, qkv_cols:],
                small[:, router_at : router_at + experts],
                lax.all_gather(exp_in[layer_index], "shard", axis=1, tiled=True),
                lax.all_gather(exp_out[layer_index], "shard", axis=1, tiled=True),
            )
        )
    residuals = [tokens[rows] for rows, _, _ in streams]
    saved = [[None] * LAYERS for _ in streams]
    for layer_index in range(LAYERS):
        staged = []
        for block, (rows, tables, route_hot) in enumerate(streams):
            attn_weights, own_rows = lax.optimization_barrier(
                (all_weights[layer_index][:5], residuals[block])
            )
            own_weights = tuple(attn_weights) + tuple(all_weights[layer_index][5:])
            staged.append(forward_attend(own_rows, tables, own_weights))
        for block, (rows, tables, route_hot) in enumerate(streams):
            carry, sending = staged[block]
            residuals[block], saved[block][layer_index] = forward_expert(
                carry, sending, route_hot, tables, all_weights[layer_index], experts, capacity
            )
    activations = jnp.concatenate(residuals, axis=0)
    d_residuals = [cotangent[rows] for rows, _, _ in streams]
    reduced = [None] * LAYERS
    for layer_index in reversed(range(LAYERS)):
        layer_sum = None
        for block, (rows, tables, route_hot) in enumerate(streams):
            d_residuals[block], layer_grads = backward_layer(
                d_residuals[block],
                saved[block][layer_index],
                route_hot,
                tables,
                all_weights[layer_index],
                experts,
                capacity,
            )
            if layer_sum is None:
                layer_sum = layer_grads
            else:
                layer_sum = tuple(old + new for old, new in zip(layer_sum, layer_grads))
        reduced[layer_index] = reduce_layer(layer_sum, layer_index == 0)
    outs = [jnp.stack([reduced[l][k] for l in range(LAYERS)]) for k in range(7)]
    d_tokens = jnp.concatenate(d_residuals, axis=0)
    return (activations, d_tokens, *outs)


def solution(mesh):
    return jax.shard_map(
        local,
        mesh=mesh,
        in_specs=(
            P(("expert", "shard"), None),
            P(("expert", "shard"), None),
            P(("expert", "shard")),
            P(None, None, "shard"),
            P(None, None, "shard"),
            P(None, "shard", None),
            P(None, "shard", None),
            P(None, "shard", None),
            P(None, "expert", "shard", None),
            P(None, "expert", "shard", None),
            P(("expert", "shard"), None),
        ),
        out_specs=(
            P(("expert", "shard"), None),
            P(("expert", "shard"), None),
            P(None, None, "shard"),
            P(None, None, "shard"),
            P(None, "shard", None),
            P(None, "shard", None),
            P(None, "shard", None),
            P(None, "expert", "shard", None),
            P(None, "expert", "shard", None),
        ),
        check_vma=False,
    )
```

```python
import jax
import jax.numpy as jnp
from jax import lax
from jax.sharding import PartitionSpec as P

D = 512
HEADS = 8
HEAD = 64
HIDDEN_SIZE = 2048
EXP_DEV = 1
SEQ = 197
MICRO = 2
LAYERS = 2
TOP = 2
TOK_MB = 394


norm_eps = 1e-06


def layer_norm(values, norm_scale, norm_shift):
    centre = values - jnp.mean(values, axis=-1, keepdims=True)
    spread = jnp.mean(centre * centre, axis=-1, keepdims=True)
    return centre * lax.rsqrt(spread + norm_eps) * norm_scale + norm_shift


def gelu_tanh(values):
    return jax.nn.gelu(values, approximate=True)


def dot_first(left, right):
    return lax.dot_general(
        left, right, (((0,), (0,)), ((), ())), preferred_element_type=jnp.float32
    )


def dot_last(left, right):
    return lax.dot_general(
        left, right, (((1,), (1,)), ((), ())), preferred_element_type=jnp.float32
    )


def slot_onehot(route_ids, prio_rank, experts, capacity):
    tok_count = route_ids.shape[0]
    order_key = jnp.concatenate([prio_rank, prio_rank + tok_count])
    pair_expert = jnp.concatenate([route_ids[:, 0], route_ids[:, 1]])
    expert_hot = (pair_expert[:, None] == jnp.arange(experts, dtype=jnp.int32)[None, :]).astype(
        jnp.bfloat16
    )
    earlier = (order_key[:, None] < order_key[None, :]).astype(jnp.bfloat16)
    counts = dot_first(expert_hot, earlier)
    position = jnp.sum(counts.T * expert_hot.astype(jnp.float32), axis=1).astype(jnp.int32)
    kept_mask = position < capacity
    flat_slot = jnp.where(kept_mask, pair_expert * capacity + position, experts * capacity)
    pair_hot = (
        flat_slot[:, None] == jnp.arange(experts * capacity, dtype=jnp.int32)[None, :]
    ).astype(jnp.bfloat16)
    token_hot = pair_hot[:tok_count] + pair_hot[tok_count:]
    return pair_hot, token_hot, kept_mask


def forward_layer(residual, route_hot, tables, weights, experts, capacity):
    norm_gains, norm_shifts, qkv_w, proj_w, router_w, in_w, out_w = weights
    pair_hot, token_hot, kept_mask = tables
    tok_count = residual.shape[0]
    seq_count = tok_count // SEQ
    score_scale = HEAD ** (-0.5)
    norm_scale = norm_gains.astype(jnp.float32)
    norm_shift = norm_shifts.astype(jnp.float32)
    normed = layer_norm(residual, norm_scale[0], norm_shift[0]).astype(jnp.bfloat16)
    qkv_rows = jnp.dot(normed, qkv_w, preferred_element_type=jnp.float32).astype(jnp.bfloat16)
    heads = qkv_rows.reshape(seq_count, SEQ, 3, HEADS, HEAD)
    scores = (
        jnp.einsum(
            "sqhd,skhd->shqk", heads[:, :, 0], heads[:, :, 1], preferred_element_type=jnp.float32
        )
        * score_scale
    )
    row_top = jnp.max(scores, axis=-1, keepdims=True)
    scores_exp = jnp.exp(scores - row_top)
    row_total = jnp.sum(scores_exp, axis=-1, keepdims=True)
    soft_scores = scores_exp / row_total
    log_total = row_top + jnp.log(row_total)
    mixed_heads = jnp.einsum(
        "shqk,skhd->sqhd",
        soft_scores.astype(jnp.bfloat16),
        heads[:, :, 2],
        preferred_element_type=jnp.float32,
    )
    mixed_heads = mixed_heads.astype(jnp.bfloat16).reshape(tok_count, D)
    middle = residual + jnp.dot(mixed_heads, proj_w, preferred_element_type=jnp.float32)
    normed_two = layer_norm(middle, norm_scale[1], norm_shift[1]).astype(jnp.bfloat16)
    gate_probs = jax.nn.softmax(
        jnp.dot(normed_two, router_w, preferred_element_type=jnp.float32), axis=-1
    )
    sending = dot_first(token_hot, normed_two).astype(jnp.bfloat16)
    received = lax.all_to_all(
        sending.reshape(experts, capacity, D), "expert", split_axis=0, concat_axis=0, tiled=True
    )
    row_block = received.reshape(experts * capacity, D)
    hidden_pre = jnp.dot(row_block, in_w[0], preferred_element_type=jnp.float32)
    hidden_act = gelu_tanh(hidden_pre).astype(jnp.bfloat16)
    slope = jax.vjp(gelu_tanh, hidden_pre)[1](jnp.ones_like(hidden_pre))[0].astype(jnp.bfloat16)
    expert_rows = jnp.dot(hidden_act, out_w[0], preferred_element_type=jnp.float32).astype(
        jnp.bfloat16
    )
    returned = lax.all_to_all(
        expert_rows.reshape(experts, capacity, D),
        "expert",
        split_axis=0,
        concat_axis=0,
        tiled=True,
    )
    pair_rows = jnp.dot(
        pair_hot, returned.reshape(experts * capacity, D), preferred_element_type=jnp.float32
    ).reshape(TOP, tok_count, D)
    chosen = jnp.sum(route_hot * gate_probs[:, None, :], axis=-1)
    kept_gate = kept_mask.astype(jnp.float32).reshape(TOP, tok_count)
    weight_pair = kept_gate * chosen.T
    combined = jnp.sum(weight_pair[..., None] * pair_rows, axis=0)
    output = middle + combined
    saved_state = (
        residual,
        normed,
        heads,
        log_total,
        mixed_heads,
        middle,
        normed_two,
        gate_probs,
        kept_gate,
        weight_pair,
        pair_rows,
        row_block,
        hidden_act,
        slope,
    )
    return (output, saved_state)


def backward_layer(d_output, saved_state, route_hot, tables, weights, experts, capacity):
    (
        residual,
        normed,
        heads,
        log_total,
        mixed_heads,
        middle,
        normed_two,
        gate_probs,
        kept_gate,
        weight_pair,
        pair_rows,
        row_block,
        hidden_act,
        slope,
    ) = saved_state
    pair_hot, token_hot, kept_mask = tables
    norm_gains, norm_shifts, qkv_w, proj_w, router_w, in_w, out_w = weights
    tok_count = residual.shape[0]
    seq_count = tok_count // SEQ
    score_scale = HEAD ** (-0.5)
    norm_scale = norm_gains.astype(jnp.float32)
    norm_shift = norm_shifts.astype(jnp.float32)
    d_gate_pair = kept_gate * jnp.sum(d_output[None] * pair_rows, axis=-1)
    d_gates = jnp.sum(route_hot * d_gate_pair.T[:, :, None], axis=1)
    d_logits = (
        gate_probs * (d_gates - jnp.sum(gate_probs * d_gates, axis=-1, keepdims=True))
    ).astype(jnp.bfloat16)
    g_router = dot_first(normed_two, d_logits)
    d_normed_two = dot_last(d_logits, router_w)
    d_pairs = (
        (weight_pair[:, :, None] * d_output[None]).astype(jnp.bfloat16).reshape(TOP * tok_count, D)
    )
    d_slots = dot_first(pair_hot, d_pairs).astype(jnp.bfloat16).reshape(experts, capacity, D)
    d_expert_out = lax.all_to_all(d_slots, "expert", split_axis=0, concat_axis=0, tiled=True)
    flat_out = d_expert_out.reshape(experts * capacity, D)
    g_out = dot_first(hidden_act, flat_out)
    d_act = dot_last(flat_out, out_w[0])
    d_pre = (d_act * slope.astype(jnp.float32)).astype(jnp.bfloat16)
    g_in = dot_first(row_block, d_pre)
    d_rows = dot_last(d_pre, in_w[0]).astype(jnp.bfloat16).reshape(experts, capacity, D)
    d_back = lax.all_to_all(d_rows, "expert", split_axis=0, concat_axis=0, tiled=True)
    d_pair_in = jnp.dot(
        pair_hot, d_back.reshape(experts * capacity, D), preferred_element_type=jnp.float32
    ).reshape(TOP, tok_count, D)
    d_normed_two = d_normed_two + jnp.sum(d_pair_in, axis=0)
    pulled_two = jax.vjp(layer_norm, middle, norm_scale[1], norm_shift[1])[1](d_normed_two)
    d_middle = d_output + pulled_two[0]
    d_branch = d_middle.astype(jnp.bfloat16)
    g_proj = dot_first(mixed_heads, d_branch)
    d_mixed = dot_last(d_branch, proj_w).astype(jnp.bfloat16).reshape(seq_count, SEQ, HEADS, HEAD)
    query_heads = heads[:, :, 0]
    key_heads = heads[:, :, 1]
    value_heads = heads[:, :, 2]
    scores = (
        jnp.einsum("sqhd,skhd->shqk", query_heads, key_heads, preferred_element_type=jnp.float32)
        * score_scale
    )
    soft_scores = jnp.exp(scores - log_total)
    d_soft = jnp.einsum("sqhd,skhd->shqk", d_mixed, value_heads, preferred_element_type=jnp.float32)
    d_values = jnp.einsum(
        "shqk,sqhd->skhd",
        soft_scores.astype(jnp.bfloat16),
        d_mixed,
        preferred_element_type=jnp.float32,
    )
    d_scores = (
        soft_scores * (d_soft - jnp.sum(soft_scores * d_soft, axis=-1, keepdims=True))
    ).astype(jnp.bfloat16)
    d_query = (
        jnp.einsum("shqk,skhd->sqhd", d_scores, key_heads, preferred_element_type=jnp.float32)
        * score_scale
    )
    d_keys = (
        jnp.einsum("shqk,sqhd->skhd", d_scores, query_heads, preferred_element_type=jnp.float32)
        * score_scale
    )
    d_qkv = (
        jnp.stack([d_query, d_keys, d_values], axis=2)
        .reshape(tok_count, 3 * D)
        .astype(jnp.bfloat16)
    )
    g_qkv = dot_first(normed, d_qkv)
    d_normed = dot_last(d_qkv, qkv_w)
    pulled_one = jax.vjp(layer_norm, residual, norm_scale[0], norm_shift[0])[1](d_normed)
    d_residual = d_middle + pulled_one[0]
    g_gain = jnp.stack([pulled_one[1], pulled_two[1]])
    g_shift = jnp.stack([pulled_one[2], pulled_two[2]])
    return (d_residual, (g_gain, g_shift, g_qkv, g_proj, g_router, g_in[None], g_out[None]))


def halving_scatter(grad, axis_name):
    size = lax.axis_size(axis_name)
    me = lax.axis_index(axis_name)
    chunk = grad.shape[0] // size
    rest = grad.shape[1:]
    total = grad.astype(jnp.float32).reshape(size, chunk, *rest)
    bit = 1
    while bit < size:
        pairs = total.reshape(total.shape[0] // 2, 2, chunk, *rest)
        mine = (me // bit) % 2
        keep = lax.dynamic_index_in_dim(pairs, mine, axis=1, keepdims=False)
        give = lax.dynamic_index_in_dim(pairs, 1 - mine, axis=1, keepdims=False)
        got = lax.ppermute(
            give.astype(jnp.bfloat16), axis_name, [(i, i ^ bit) for i in range(size)]
        )
        total = keep + got.astype(jnp.float32)
        bit *= 2
    return total.reshape(chunk, *rest)


def doubling_sum(part, axis_name):
    size = lax.axis_size(axis_name)
    total = part.astype(jnp.float32)
    bit = 1
    while bit < size:
        own = lax.reduce_precision(total, exponent_bits=8, mantissa_bits=7)
        got = lax.ppermute(
            own.astype(jnp.bfloat16), axis_name, [(i, i ^ bit) for i in range(size)]
        )
        total = own + got.astype(jnp.float32)
        bit *= 2
    return total


def doubling_gather(part, axis_name):
    size = lax.axis_size(axis_name)
    me = lax.axis_index(axis_name)
    held = part[None]
    bit = size // 2
    steps = 0
    while bit >= 1:
        got = lax.ppermute(held, axis_name, [(i, i ^ bit) for i in range(size)])
        low = (me // bit) % 2 == 0
        held = jnp.where(low, jnp.concatenate([held, got]), jnp.concatenate([got, held]))
        bit //= 2
        steps += 1
    held = held.reshape((2,) * steps + part.shape)
    held = held.transpose(tuple(reversed(range(steps))) + tuple(range(steps, held.ndim)))
    return held.reshape((size * part.shape[0],) + part.shape[1:])


def reduce_layer(layer_grads, late):
    g_gain, g_shift, g_qkv, g_proj, g_router, g_in, g_out = layer_grads
    qkv_cols = g_qkv.shape[1]
    proj_cols = g_proj.shape[1]
    small = jnp.concatenate([g_gain.T, g_shift.T, g_router], axis=1)
    shared = jnp.concatenate([g_qkv, g_proj, small], axis=1)
    shared = halving_scatter(shared, "shard")
    if late:
        owned = halving_scatter(shared, "expert")
        owned = lax.reduce_precision(owned, exponent_bits=8, mantissa_bits=7)
        shared = doubling_gather(owned.astype(jnp.bfloat16), "expert").astype(jnp.float32)
    else:
        shared = lax.psum(shared.astype(jnp.bfloat16), "expert").astype(jnp.float32)
    tail = shared[:, qkv_cols + proj_cols :]
    return [
        tail[:, 0:2].T,
        tail[:, 2:4].T,
        shared[:, :qkv_cols],
        shared[:, qkv_cols : qkv_cols + proj_cols],
        tail[:, 4:],
        halving_scatter(g_in[0], "shard")[None],
        halving_scatter(g_out[0], "shard")[None],
    ]


def local(
    tokens,
    routes,
    priority,
    norm_gain,
    norm_bias,
    w_qkv,
    w_proj,
    w_router,
    exp_in,
    exp_out,
    cotangent,
):
    experts = lax.axis_size("expert") * EXP_DEV
    capacity = max(8, (5 * TOK_MB // (2 * experts) + 7) // 8 * 8)
    tok_count = tokens.shape[0]
    blocks = tok_count // TOK_MB
    streams = []
    for block in range(blocks):
        rows = slice(block * TOK_MB, (block + 1) * TOK_MB)
        route_ids = routes[rows]
        tables = slot_onehot(route_ids, priority[rows], experts, capacity)
        route_hot = (
            route_ids[..., None] == jnp.arange(experts, dtype=jnp.int32)
        ).astype(jnp.float32)
        streams.append((rows, tables, route_hot))
    layer_count = norm_gain.shape[0]
    small = jnp.concatenate(
        [
            norm_gain.reshape(layer_count * 2, -1).T,
            norm_bias.reshape(layer_count * 2, -1).T,
            w_router.transpose(1, 0, 2).reshape(w_router.shape[1], -1),
        ],
        axis=1,
    )
    small = lax.all_gather(small, "shard", axis=0, tiled=True)
    qkv_cols = w_qkv.shape[2]
    all_weights = []
    for layer_index in range(LAYERS):
        attn = lax.all_gather(
            jnp.concatenate([w_qkv[layer_index], w_proj[layer_index]], axis=1),
            "shard",
            axis=0,
            tiled=True,
        )
        shift_at = 2 * layer_count + 2 * layer_index
        router_at = 4 * layer_count + experts * layer_index
        all_weights.append(
            (
                small[:, 2 * layer_index : 2 * layer_index + 2].T,
                small[:, shift_at : shift_at + 2].T,
                attn[:, :qkv_cols],
                attn[:, qkv_cols:],
                small[:, router_at : router_at + experts],
                lax.all_gather(exp_in[layer_index], "shard", axis=1, tiled=True),
                lax.all_gather(exp_out[layer_index], "shard", axis=1, tiled=True),
            )
        )
    residuals = [tokens[rows] for rows, _, _ in streams]
    saved = [[None] * LAYERS for _ in streams]
    for layer_index in range(LAYERS):
        for block, (rows, tables, route_hot) in enumerate(streams):
            residuals[block], saved[block][layer_index] = forward_layer(
                residuals[block], route_hot, tables, all_weights[layer_index], experts, capacity
            )
    activations = jnp.concatenate(residuals, axis=0)
    d_residuals = [cotangent[rows] for rows, _, _ in streams]
    reduced = [None] * LAYERS
    for layer_index in reversed(range(LAYERS)):
        layer_sum = None
        for block, (rows, tables, route_hot) in enumerate(streams):
            d_residuals[block], layer_grads = backward_layer(
                d_residuals[block],
                saved[block][layer_index],
                route_hot,
                tables,
                all_weights[layer_index],
                experts,
                capacity,
            )
            if layer_sum is None:
                layer_sum = layer_grads
            else:
                layer_sum = tuple(old + new for old, new in zip(layer_sum, layer_grads))
        reduced[layer_index] = reduce_layer(layer_sum, layer_index == 0)
    outs = [jnp.stack([reduced[l][k] for l in range(LAYERS)]) for k in range(7)]
    d_tokens = jnp.concatenate(d_residuals, axis=0)
    return (activations, d_tokens, *outs)


def solution(mesh):
    return jax.shard_map(
        local,
        mesh=mesh,
        in_specs=(
            P(("expert", "shard"), None),
            P(("expert", "shard"), None),
            P(("expert", "shard")),
            P(None, None, "shard"),
            P(None, None, "shard"),
            P(None, "shard", None),
            P(None, "shard", None),
            P(None, "shard", None),
            P(None, "expert", "shard", None),
            P(None, "expert", "shard", None),
            P(("expert", "shard"), None),
        ),
        out_specs=(
            P(("expert", "shard"), None),
            P(("expert", "shard"), None),
            P(None, None, "shard"),
            P(None, None, "shard"),
            P(None, "shard", None),
            P(None, "shard", None),
            P(None, "shard", None),
            P(None, "expert", "shard", None),
            P(None, "expert", "shard", None),
        ),
        check_vma=False,
    )
```

```python
import jax
import jax.numpy as jnp
from jax import lax
from jax.sharding import PartitionSpec as P

D = 512
HEADS = 8
HEAD = 64
HIDDEN_SIZE = 2048
EXP_DEV = 1
SEQ = 197
MICRO = 2
LAYERS = 2
TOP = 2
TOK_MB = 394


norm_eps = 1e-06


def layer_norm(values, norm_scale, norm_shift):
    centre = values - jnp.mean(values, axis=-1, keepdims=True)
    spread = jnp.mean(centre * centre, axis=-1, keepdims=True)
    return centre * lax.rsqrt(spread + norm_eps) * norm_scale + norm_shift


def gelu_tanh(values):
    return jax.nn.gelu(values, approximate=True)


def dot_first(left, right):
    return lax.dot_general(
        left, right, (((0,), (0,)), ((), ())), preferred_element_type=jnp.float32
    )


def dot_last(left, right):
    return lax.dot_general(
        left, right, (((1,), (1,)), ((), ())), preferred_element_type=jnp.float32
    )


def slot_onehot(route_ids, prio_rank, experts, capacity):
    tok_count = route_ids.shape[0]
    order_key = jnp.concatenate([prio_rank, prio_rank + tok_count])
    pair_expert = jnp.concatenate([route_ids[:, 0], route_ids[:, 1]])
    expert_hot = (pair_expert[:, None] == jnp.arange(experts, dtype=jnp.int32)[None, :]).astype(
        jnp.bfloat16
    )
    earlier = (order_key[:, None] < order_key[None, :]).astype(jnp.bfloat16)
    counts = dot_first(expert_hot, earlier)
    position = jnp.sum(counts.T * expert_hot.astype(jnp.float32), axis=1).astype(jnp.int32)
    kept_mask = position < capacity
    flat_slot = jnp.where(kept_mask, pair_expert * capacity + position, experts * capacity)
    pair_hot = (
        flat_slot[:, None] == jnp.arange(experts * capacity, dtype=jnp.int32)[None, :]
    ).astype(jnp.bfloat16)
    token_hot = pair_hot[:tok_count] + pair_hot[tok_count:]
    return pair_hot, token_hot, kept_mask


def forward_layer(residual, route_hot, tables, weights, experts, capacity):
    norm_gains, norm_shifts, qkv_w, proj_w, router_w, in_w, out_w = weights
    pair_hot, token_hot, kept_mask = tables
    tok_count = residual.shape[0]
    seq_count = tok_count // SEQ
    score_scale = HEAD ** (-0.5)
    norm_scale = norm_gains.astype(jnp.float32)
    norm_shift = norm_shifts.astype(jnp.float32)
    normed = layer_norm(residual, norm_scale[0], norm_shift[0]).astype(jnp.bfloat16)
    qkv_rows = jnp.dot(normed, qkv_w, preferred_element_type=jnp.float32).astype(jnp.bfloat16)
    heads = qkv_rows.reshape(seq_count, SEQ, 3, HEADS, HEAD)
    scores = (
        jnp.einsum(
            "sqhd,skhd->shqk", heads[:, :, 0], heads[:, :, 1], preferred_element_type=jnp.float32
        )
        * score_scale
    )
    row_top = jnp.max(scores, axis=-1, keepdims=True)
    scores_exp = jnp.exp(scores - row_top)
    row_total = jnp.sum(scores_exp, axis=-1, keepdims=True)
    soft_scores = scores_exp / row_total
    log_total = row_top + jnp.log(row_total)
    mixed_heads = jnp.einsum(
        "shqk,skhd->sqhd",
        soft_scores.astype(jnp.bfloat16),
        heads[:, :, 2],
        preferred_element_type=jnp.float32,
    )
    mixed_heads = mixed_heads.astype(jnp.bfloat16).reshape(tok_count, D)
    middle = residual + jnp.dot(mixed_heads, proj_w, preferred_element_type=jnp.float32)
    normed_two = layer_norm(middle, norm_scale[1], norm_shift[1]).astype(jnp.bfloat16)
    gate_probs = jax.nn.softmax(
        jnp.dot(normed_two, router_w, preferred_element_type=jnp.float32), axis=-1
    )
    sending = dot_first(token_hot, normed_two).astype(jnp.bfloat16)
    received = lax.all_to_all(
        sending.reshape(experts, capacity, D), "expert", split_axis=0, concat_axis=0, tiled=True
    )
    row_block = received.reshape(experts * capacity, D)
    hidden_pre = jnp.dot(row_block, in_w[0], preferred_element_type=jnp.float32)
    hidden_act = gelu_tanh(hidden_pre).astype(jnp.bfloat16)
    expert_rows = jnp.dot(hidden_act, out_w[0], preferred_element_type=jnp.float32).astype(
        jnp.bfloat16
    )
    returned = lax.all_to_all(
        expert_rows.reshape(experts, capacity, D),
        "expert",
        split_axis=0,
        concat_axis=0,
        tiled=True,
    )
    pair_rows = jnp.dot(
        pair_hot, returned.reshape(experts * capacity, D), preferred_element_type=jnp.float32
    ).reshape(TOP, tok_count, D)
    chosen = jnp.sum(route_hot * gate_probs[:, None, :], axis=-1)
    kept_gate = kept_mask.astype(jnp.float32).reshape(TOP, tok_count)
    weight_pair = kept_gate * chosen.T
    combined = jnp.sum(weight_pair[..., None] * pair_rows, axis=0)
    output = middle + combined
    saved_state = (
        residual,
        normed,
        heads,
        log_total,
        mixed_heads,
        middle,
        normed_two,
        gate_probs,
        kept_gate,
        weight_pair,
        pair_rows,
        row_block,
        hidden_pre,
    )
    return (output, saved_state)


def backward_layer(d_output, saved_state, route_hot, tables, weights, experts, capacity):
    (
        residual,
        normed,
        heads,
        log_total,
        mixed_heads,
        middle,
        normed_two,
        gate_probs,
        kept_gate,
        weight_pair,
        pair_rows,
        row_block,
        hidden_pre,
    ) = saved_state
    pair_hot, token_hot, kept_mask = tables
    norm_gains, norm_shifts, qkv_w, proj_w, router_w, in_w, out_w = weights
    tok_count = residual.shape[0]
    seq_count = tok_count // SEQ
    score_scale = HEAD ** (-0.5)
    norm_scale = norm_gains.astype(jnp.float32)
    norm_shift = norm_shifts.astype(jnp.float32)
    d_gate_pair = kept_gate * jnp.sum(d_output[None] * pair_rows, axis=-1)
    d_gates = jnp.sum(route_hot * d_gate_pair.T[:, :, None], axis=1)
    d_logits = (
        gate_probs * (d_gates - jnp.sum(gate_probs * d_gates, axis=-1, keepdims=True))
    ).astype(jnp.bfloat16)
    g_router = dot_first(normed_two, d_logits)
    d_normed_two = dot_last(d_logits, router_w)
    d_pairs = (
        (weight_pair[:, :, None] * d_output[None]).astype(jnp.bfloat16).reshape(TOP * tok_count, D)
    )
    d_slots = dot_first(pair_hot, d_pairs).astype(jnp.bfloat16).reshape(experts, capacity, D)
    d_expert_out = lax.all_to_all(d_slots, "expert", split_axis=0, concat_axis=0, tiled=True)
    flat_out = d_expert_out.reshape(experts * capacity, D)
    hidden_act = gelu_tanh(hidden_pre).astype(jnp.bfloat16)
    g_out = dot_first(hidden_act, flat_out)
    d_act = dot_last(flat_out, out_w[0])
    d_pre = jax.vjp(gelu_tanh, hidden_pre)[1](d_act)[0].astype(jnp.bfloat16)
    g_in = dot_first(row_block, d_pre)
    d_rows = dot_last(d_pre, in_w[0]).astype(jnp.bfloat16).reshape(experts, capacity, D)
    d_back = lax.all_to_all(d_rows, "expert", split_axis=0, concat_axis=0, tiled=True)
    d_pair_in = jnp.dot(
        pair_hot, d_back.reshape(experts * capacity, D), preferred_element_type=jnp.float32
    ).reshape(TOP, tok_count, D)
    d_normed_two = d_normed_two + jnp.sum(d_pair_in, axis=0)
    pulled_two = jax.vjp(layer_norm, middle, norm_scale[1], norm_shift[1])[1](d_normed_two)
    d_middle = d_output + pulled_two[0]
    d_branch = d_middle.astype(jnp.bfloat16)
    g_proj = dot_first(mixed_heads, d_branch)
    d_mixed = dot_last(d_branch, proj_w).astype(jnp.bfloat16).reshape(seq_count, SEQ, HEADS, HEAD)
    query_heads = heads[:, :, 0]
    key_heads = heads[:, :, 1]
    value_heads = heads[:, :, 2]
    scores = (
        jnp.einsum("sqhd,skhd->shqk", query_heads, key_heads, preferred_element_type=jnp.float32)
        * score_scale
    )
    soft_scores = jnp.exp(scores - log_total)
    d_soft = jnp.einsum("sqhd,skhd->shqk", d_mixed, value_heads, preferred_element_type=jnp.float32)
    d_values = jnp.einsum(
        "shqk,sqhd->skhd",
        soft_scores.astype(jnp.bfloat16),
        d_mixed,
        preferred_element_type=jnp.float32,
    )
    d_scores = (
        soft_scores * (d_soft - jnp.sum(soft_scores * d_soft, axis=-1, keepdims=True))
    ).astype(jnp.bfloat16)
    d_query = (
        jnp.einsum("shqk,skhd->sqhd", d_scores, key_heads, preferred_element_type=jnp.float32)
        * score_scale
    )
    d_keys = (
        jnp.einsum("shqk,sqhd->skhd", d_scores, query_heads, preferred_element_type=jnp.float32)
        * score_scale
    )
    d_qkv = (
        jnp.stack([d_query, d_keys, d_values], axis=2)
        .reshape(tok_count, 3 * D)
        .astype(jnp.bfloat16)
    )
    g_qkv = dot_first(normed, d_qkv)
    d_normed = dot_last(d_qkv, qkv_w)
    pulled_one = jax.vjp(layer_norm, residual, norm_scale[0], norm_shift[0])[1](d_normed)
    d_residual = d_middle + pulled_one[0]
    g_gain = jnp.stack([pulled_one[1], pulled_two[1]])
    g_shift = jnp.stack([pulled_one[2], pulled_two[2]])
    return (d_residual, (g_gain, g_shift, g_qkv, g_proj, g_router, g_in[None], g_out[None]))


def halving_scatter(grad, axis_name):
    size = lax.axis_size(axis_name)
    me = lax.axis_index(axis_name)
    chunk = grad.shape[0] // size
    rest = grad.shape[1:]
    total = grad.astype(jnp.float32).reshape(size, chunk, *rest)
    bit = 1
    while bit < size:
        pairs = total.reshape(total.shape[0] // 2, 2, chunk, *rest)
        mine = (me // bit) % 2
        keep = lax.dynamic_index_in_dim(pairs, mine, axis=1, keepdims=False)
        give = lax.dynamic_index_in_dim(pairs, 1 - mine, axis=1, keepdims=False)
        got = lax.ppermute(
            give.astype(jnp.bfloat16), axis_name, [(i, i ^ bit) for i in range(size)]
        )
        total = keep + got.astype(jnp.float32)
        bit *= 2
    return total.reshape(chunk, *rest)


def doubling_sum(part, axis_name):
    size = lax.axis_size(axis_name)
    total = part.astype(jnp.float32)
    bit = 1
    while bit < size:
        own = lax.reduce_precision(total, exponent_bits=8, mantissa_bits=7)
        got = lax.ppermute(
            own.astype(jnp.bfloat16), axis_name, [(i, i ^ bit) for i in range(size)]
        )
        total = own + got.astype(jnp.float32)
        bit *= 2
    return total


def doubling_gather(part, axis_name):
    size = lax.axis_size(axis_name)
    me = lax.axis_index(axis_name)
    held = part[None]
    bit = size // 2
    steps = 0
    while bit >= 1:
        got = lax.ppermute(held, axis_name, [(i, i ^ bit) for i in range(size)])
        low = (me // bit) % 2 == 0
        held = jnp.where(low, jnp.concatenate([held, got]), jnp.concatenate([got, held]))
        bit //= 2
        steps += 1
    held = held.reshape((2,) * steps + part.shape)
    held = held.transpose(tuple(reversed(range(steps))) + tuple(range(steps, held.ndim)))
    return held.reshape((size * part.shape[0],) + part.shape[1:])


def reduce_layer(layer_grads, late):
    g_gain, g_shift, g_qkv, g_proj, g_router, g_in, g_out = layer_grads
    qkv_cols = g_qkv.shape[1]
    proj_cols = g_proj.shape[1]
    small = jnp.concatenate([g_gain.T, g_shift.T, g_router], axis=1)
    shared = jnp.concatenate([g_qkv, g_proj, small], axis=1)
    shared = halving_scatter(shared, "shard")
    if late:
        owned = halving_scatter(shared, "expert")
        owned = lax.reduce_precision(owned, exponent_bits=8, mantissa_bits=7)
        shared = doubling_gather(owned.astype(jnp.bfloat16), "expert").astype(jnp.float32)
    else:
        shared = lax.psum(shared.astype(jnp.bfloat16), "expert").astype(jnp.float32)
    tail = shared[:, qkv_cols + proj_cols :]
    return [
        tail[:, 0:2].T,
        tail[:, 2:4].T,
        shared[:, :qkv_cols],
        shared[:, qkv_cols : qkv_cols + proj_cols],
        tail[:, 4:],
        halving_scatter(g_in[0], "shard")[None],
        halving_scatter(g_out[0], "shard")[None],
    ]


def local(
    tokens,
    routes,
    priority,
    norm_gain,
    norm_bias,
    w_qkv,
    w_proj,
    w_router,
    exp_in,
    exp_out,
    cotangent,
):
    experts = lax.axis_size("expert") * EXP_DEV
    capacity = max(8, (5 * TOK_MB // (2 * experts) + 7) // 8 * 8)
    tok_count = tokens.shape[0]
    blocks = tok_count // TOK_MB
    streams = []
    for block in range(blocks):
        rows = slice(block * TOK_MB, (block + 1) * TOK_MB)
        route_ids = routes[rows]
        tables = slot_onehot(route_ids, priority[rows], experts, capacity)
        route_hot = (
            route_ids[..., None] == jnp.arange(experts, dtype=jnp.int32)
        ).astype(jnp.float32)
        streams.append((rows, tables, route_hot))
    layer_count = norm_gain.shape[0]
    small = jnp.concatenate(
        [
            norm_gain.reshape(layer_count * 2, -1).T,
            norm_bias.reshape(layer_count * 2, -1).T,
            w_router.transpose(1, 0, 2).reshape(w_router.shape[1], -1),
        ],
        axis=1,
    )
    small = doubling_gather(small, "shard")
    qkv_cols = w_qkv.shape[2]
    all_weights = []
    for layer_index in range(LAYERS):
        attn = jnp.concatenate([w_qkv[layer_index], w_proj[layer_index]], axis=1)
        if layer_index == 0:
            attn = doubling_gather(attn, "shard")
        else:
            attn = lax.all_gather(attn, "shard", axis=0, tiled=True)
        shift_at = 2 * layer_count + 2 * layer_index
        router_at = 4 * layer_count + experts * layer_index
        all_weights.append(
            (
                small[:, 2 * layer_index : 2 * layer_index + 2].T,
                small[:, shift_at : shift_at + 2].T,
                attn[:, :qkv_cols],
                attn[:, qkv_cols:],
                small[:, router_at : router_at + experts],
                lax.all_gather(exp_in[layer_index], "shard", axis=1, tiled=True),
                lax.all_gather(exp_out[layer_index], "shard", axis=1, tiled=True),
            )
        )
    residuals = [tokens[rows] for rows, _, _ in streams]
    saved = [[None] * LAYERS for _ in streams]
    for layer_index in range(LAYERS):
        for block, (rows, tables, route_hot) in enumerate(streams):
            residuals[block], saved[block][layer_index] = forward_layer(
                residuals[block], route_hot, tables, all_weights[layer_index], experts, capacity
            )
    activations = jnp.concatenate(residuals, axis=0)
    d_residuals = [cotangent[rows] for rows, _, _ in streams]
    reduced = [None] * LAYERS
    for layer_index in reversed(range(LAYERS)):
        layer_sum = None
        for block, (rows, tables, route_hot) in enumerate(streams):
            d_residuals[block], layer_grads = backward_layer(
                d_residuals[block],
                saved[block][layer_index],
                route_hot,
                tables,
                all_weights[layer_index],
                experts,
                capacity,
            )
            if layer_sum is None:
                layer_sum = layer_grads
            else:
                layer_sum = tuple(old + new for old, new in zip(layer_sum, layer_grads))
        reduced[layer_index] = reduce_layer(layer_sum, layer_index == 0)
    outs = [jnp.stack([reduced[l][k] for l in range(LAYERS)]) for k in range(7)]
    d_tokens = jnp.concatenate(d_residuals, axis=0)
    return (activations, d_tokens, *outs)


def solution(mesh):
    return jax.shard_map(
        local,
        mesh=mesh,
        in_specs=(
            P(("expert", "shard"), None),
            P(("expert", "shard"), None),
            P(("expert", "shard")),
            P(None, None, "shard"),
            P(None, None, "shard"),
            P(None, "shard", None),
            P(None, "shard", None),
            P(None, "shard", None),
            P(None, "expert", "shard", None),
            P(None, "expert", "shard", None),
            P(("expert", "shard"), None),
        ),
        out_specs=(
            P(("expert", "shard"), None),
            P(("expert", "shard"), None),
            P(None, None, "shard"),
            P(None, None, "shard"),
            P(None, "shard", None),
            P(None, "shard", None),
            P(None, "shard", None),
            P(None, "expert", "shard", None),
            P(None, "expert", "shard", None),
        ),
        check_vma=False,
    )
```

```python
import jax
import jax.numpy as jnp
from jax import lax
from jax.sharding import PartitionSpec as P


D = 512
HEADS = 8
HEAD = 64
EXP_DEV = 1
SEQ = 197
LAYERS = 2
TOP = 2
TOK_MB = 394


norm_eps = 1e-06


def layer_norm(values, norm_scale, norm_shift):
    centre = values - jnp.mean(values, axis=-1, keepdims=True)
    spread = jnp.mean(centre * centre, axis=-1, keepdims=True)
    return centre * lax.rsqrt(spread + norm_eps) * norm_scale + norm_shift


def gelu_tanh(values):
    return jax.nn.gelu(values, approximate=True)


def dot_first(left, right):
    return lax.dot_general(
        left, right, (((0,), (0,)), ((), ())), preferred_element_type=jnp.float32
    )


def dot_last(left, right):
    return lax.dot_general(
        left, right, (((1,), (1,)), ((), ())), preferred_element_type=jnp.float32
    )


def slot_onehot(route_ids, prio_rank, experts, capacity):
    tok_count = route_ids.shape[0]
    order_key = jnp.concatenate([prio_rank, prio_rank + tok_count])
    pair_expert = jnp.concatenate([route_ids[:, 0], route_ids[:, 1]])
    expert_hot = (pair_expert[:, None] == jnp.arange(experts, dtype=jnp.int32)[None, :]).astype(
        jnp.bfloat16
    )
    earlier = (order_key[:, None] < order_key[None, :]).astype(jnp.bfloat16)
    counts = dot_first(expert_hot, earlier)
    position = jnp.sum(counts.T * expert_hot.astype(jnp.float32), axis=1).astype(jnp.int32)
    kept_mask = position < capacity
    flat_slot = jnp.where(kept_mask, pair_expert * capacity + position, experts * capacity)
    pair_hot = (
        flat_slot[:, None] == jnp.arange(experts * capacity, dtype=jnp.int32)[None, :]
    ).astype(jnp.bfloat16)
    token_hot = pair_hot[:tok_count] + pair_hot[tok_count:]
    return pair_hot, token_hot, kept_mask


def exchange(blocks, axis_name):
    return lax.all_to_all(blocks, axis_name, split_axis=0, concat_axis=0, tiled=True)


def forward_attend(residual, tables, weights):
    norm_gains, norm_shifts, qkv_w, proj_w, router_w, _, _ = weights
    _, token_hot, _ = tables
    tok_count = residual.shape[0]
    seq_count = tok_count // SEQ
    score_scale = HEAD ** (-0.5)
    norm_scale = norm_gains.astype(jnp.float32)
    norm_shift = norm_shifts.astype(jnp.float32)
    normed = layer_norm(residual, norm_scale[0], norm_shift[0]).astype(jnp.bfloat16)
    qkv_rows = jnp.dot(normed, qkv_w, preferred_element_type=jnp.float32).astype(jnp.bfloat16)
    heads = qkv_rows.reshape(seq_count, SEQ, 3, HEADS, HEAD)
    scores = (
        jnp.einsum(
            "sqhd,skhd->shqk", heads[:, :, 0], heads[:, :, 1], preferred_element_type=jnp.float32
        )
        * score_scale
    )
    row_top = jnp.max(scores, axis=-1, keepdims=True)
    scores_exp = jnp.exp(scores - row_top)
    row_total = jnp.sum(scores_exp, axis=-1, keepdims=True)
    soft_scores = scores_exp / row_total
    log_total = row_top + jnp.log(row_total)
    mixed_heads = jnp.einsum(
        "shqk,skhd->sqhd",
        soft_scores.astype(jnp.bfloat16),
        heads[:, :, 2],
        preferred_element_type=jnp.float32,
    )
    mixed_heads = mixed_heads.astype(jnp.bfloat16).reshape(tok_count, D)
    middle = residual + jnp.dot(mixed_heads, proj_w, preferred_element_type=jnp.float32)
    normed_two = layer_norm(middle, norm_scale[1], norm_shift[1]).astype(jnp.bfloat16)
    gate_probs = jax.nn.softmax(
        jnp.dot(normed_two, router_w, preferred_element_type=jnp.float32), axis=-1
    )
    sending = dot_first(token_hot, normed_two).astype(jnp.bfloat16)
    carry = (residual, normed, heads, log_total, mixed_heads, middle, normed_two, gate_probs)
    return carry, sending


def forward_expert(carry, sending, route_hot, tables, weights, experts, capacity):
    _, _, _, _, _, in_w, out_w = weights
    received = exchange(sending.reshape(experts, capacity, D), "expert")
    row_block = received.reshape(experts * capacity, D)
    hidden_pre = jnp.dot(row_block, in_w[0], preferred_element_type=jnp.float32)
    hidden_act = gelu_tanh(hidden_pre).astype(jnp.bfloat16)
    expert_rows = jnp.dot(hidden_act, out_w[0], preferred_element_type=jnp.float32).astype(
        jnp.bfloat16
    )
    returned = exchange(expert_rows.reshape(experts, capacity, D), "expert")
    return forward_combine(
        carry, returned, row_block, hidden_pre, route_hot, tables, experts, capacity
    )


def forward_combine(carry, returned, row_block, hidden_pre, route_hot, tables, experts, capacity):
    residual, normed, heads, log_total, mixed_heads, middle, normed_two, gate_probs = carry
    pair_hot, _, kept_mask = tables
    tok_count = residual.shape[0]
    pair_rows = jnp.dot(
        pair_hot, returned.reshape(experts * capacity, D), preferred_element_type=jnp.float32
    ).reshape(TOP, tok_count, D)
    chosen = jnp.sum(route_hot * gate_probs[:, None, :], axis=-1)
    kept_gate = kept_mask.astype(jnp.float32).reshape(TOP, tok_count)
    weight_pair = kept_gate * chosen.T
    combined = jnp.sum(weight_pair[..., None] * pair_rows, axis=0)
    output = middle + combined
    saved_state = (
        residual,
        normed,
        heads,
        log_total,
        mixed_heads,
        middle,
        normed_two,
        gate_probs,
        kept_gate,
        weight_pair,
        pair_rows,
        row_block,
        hidden_pre,
    )
    return (output, saved_state)


def backward_layer(d_output, saved_state, route_hot, tables, weights, experts, capacity):
    (_, _, _, _, _, _, _, _, _, _, _, row_block, hidden_pre) = saved_state
    _, _, _, _, router_w, in_w, out_w = weights
    d_slots, g_router, d_normed_two = backward_route(
        d_output, saved_state, tables, route_hot, router_w, experts, capacity
    )
    d_expert_out = exchange(d_slots, "expert")
    flat_out = d_expert_out.reshape(experts * capacity, D)
    hidden_act = gelu_tanh(hidden_pre).astype(jnp.bfloat16)
    g_out = dot_first(hidden_act, flat_out)
    d_act = dot_last(flat_out, out_w[0])
    d_pre = jax.vjp(gelu_tanh, hidden_pre)[1](d_act)[0].astype(jnp.bfloat16)
    g_in = dot_first(row_block, d_pre)
    d_rows = dot_last(d_pre, in_w[0]).astype(jnp.bfloat16).reshape(experts, capacity, D)
    d_back = exchange(d_rows, "expert")
    d_residual, grads = backward_attend(
        d_output, saved_state, d_back, d_normed_two, tables, weights, experts, capacity
    )
    g_gain, g_shift, g_qkv, g_proj = grads
    return (d_residual, (g_gain, g_shift, g_qkv, g_proj, g_router, g_in[None], g_out[None]))


def backward_route(d_output, saved_state, tables, route_hot, router_w, experts, capacity):
    (
        residual, _, _, _, _, _, normed_two, gate_probs, kept_gate, weight_pair, pair_rows, _, _
    ) = saved_state
    pair_hot, _, _ = tables
    tok_count = residual.shape[0]
    d_gate_pair = kept_gate * jnp.sum(d_output[None] * pair_rows, axis=-1)
    d_gates = jnp.sum(route_hot * d_gate_pair.T[:, :, None], axis=1)
    d_logits = (
        gate_probs * (d_gates - jnp.sum(gate_probs * d_gates, axis=-1, keepdims=True))
    ).astype(jnp.bfloat16)
    g_router = dot_first(normed_two, d_logits)
    d_normed_two = dot_last(d_logits, router_w)
    d_pairs = (
        (weight_pair[:, :, None] * d_output[None]).astype(jnp.bfloat16).reshape(TOP * tok_count, D)
    )
    d_slots = dot_first(pair_hot, d_pairs).astype(jnp.bfloat16).reshape(experts, capacity, D)
    return d_slots, g_router, d_normed_two


def backward_attend(d_output, saved_state, d_back, d_normed_two, tables, weights, experts, capacity):
    (residual, normed, heads, log_total, mixed_heads, middle, _, _, _, _, _, _, _) = saved_state
    pair_hot, _, _ = tables
    norm_gains, norm_shifts, qkv_w, proj_w, _, _, _ = weights
    tok_count = residual.shape[0]
    seq_count = tok_count // SEQ
    score_scale = HEAD ** (-0.5)
    norm_scale = norm_gains.astype(jnp.float32)
    norm_shift = norm_shifts.astype(jnp.float32)
    d_pair_in = jnp.dot(
        pair_hot, d_back.reshape(experts * capacity, D), preferred_element_type=jnp.float32
    ).reshape(TOP, tok_count, D)
    d_normed_two = d_normed_two + jnp.sum(d_pair_in, axis=0)
    pulled_two = jax.vjp(layer_norm, middle, norm_scale[1], norm_shift[1])[1](d_normed_two)
    d_middle = d_output + pulled_two[0]
    d_branch = d_middle.astype(jnp.bfloat16)
    g_proj = dot_first(mixed_heads, d_branch)
    d_mixed = dot_last(d_branch, proj_w).astype(jnp.bfloat16).reshape(seq_count, SEQ, HEADS, HEAD)
    query_heads = heads[:, :, 0]
    key_heads = heads[:, :, 1]
    value_heads = heads[:, :, 2]
    scores = (
        jnp.einsum("sqhd,skhd->shqk", query_heads, key_heads, preferred_element_type=jnp.float32)
        * score_scale
    )
    soft_scores = jnp.exp(scores - log_total)
    d_soft = jnp.einsum("sqhd,skhd->shqk", d_mixed, value_heads, preferred_element_type=jnp.float32)
    d_values = jnp.einsum(
        "shqk,sqhd->skhd",
        soft_scores.astype(jnp.bfloat16),
        d_mixed,
        preferred_element_type=jnp.float32,
    )
    d_scores = (
        soft_scores * (d_soft - jnp.sum(soft_scores * d_soft, axis=-1, keepdims=True))
    ).astype(jnp.bfloat16)
    d_query = (
        jnp.einsum("shqk,skhd->sqhd", d_scores, key_heads, preferred_element_type=jnp.float32)
        * score_scale
    )
    d_keys = (
        jnp.einsum("shqk,sqhd->skhd", d_scores, query_heads, preferred_element_type=jnp.float32)
        * score_scale
    )
    d_qkv = (
        jnp.stack([d_query, d_keys, d_values], axis=2)
        .reshape(tok_count, 3 * D)
        .astype(jnp.bfloat16)
    )
    g_qkv = dot_first(normed, d_qkv)
    d_normed = dot_last(d_qkv, qkv_w)
    pulled_one = jax.vjp(layer_norm, residual, norm_scale[0], norm_shift[0])[1](d_normed)
    d_residual = d_middle + pulled_one[0]
    g_gain = jnp.stack([pulled_one[1], pulled_two[1]])
    g_shift = jnp.stack([pulled_one[2], pulled_two[2]])
    return d_residual, (g_gain, g_shift, g_qkv, g_proj)


def halving_scatter(grad, axis_name):
    size = lax.axis_size(axis_name)
    me = lax.axis_index(axis_name)
    chunk = grad.shape[0] // size
    rest = grad.shape[1:]
    total = grad.astype(jnp.float32).reshape(size, chunk, *rest)
    bit = 1
    while bit < size:
        pairs = total.reshape(total.shape[0] // 2, 2, chunk, *rest)
        mine = (me // bit) % 2
        keep = lax.dynamic_index_in_dim(pairs, mine, axis=1, keepdims=False)
        give = lax.dynamic_index_in_dim(pairs, 1 - mine, axis=1, keepdims=False)
        got = lax.ppermute(
            give.astype(jnp.bfloat16), axis_name, [(i, i ^ bit) for i in range(size)]
        )
        total = keep + got.astype(jnp.float32)
        bit *= 2
    return total.reshape(chunk, *rest)


def doubling_gather(part, axis_name):
    size = lax.axis_size(axis_name)
    me = lax.axis_index(axis_name)
    held = part[None]
    bit = size // 2
    steps = 0
    while bit >= 1:
        got = lax.ppermute(held, axis_name, [(i, i ^ bit) for i in range(size)])
        low = (me // bit) % 2 == 0
        held = jnp.where(low, jnp.concatenate([held, got]), jnp.concatenate([got, held]))
        bit //= 2
        steps += 1
    held = held.reshape((2,) * steps + part.shape)
    held = held.transpose(tuple(reversed(range(steps))) + tuple(range(steps, held.ndim)))
    return held.reshape((size * part.shape[0],) + part.shape[1:])


def reduce_layer(layer_grads, late):
    g_gain, g_shift, g_qkv, g_proj, g_router, g_in, g_out = layer_grads
    qkv_cols = g_qkv.shape[1]
    proj_cols = g_proj.shape[1]
    small = jnp.concatenate([g_gain.T, g_shift.T, g_router], axis=1)
    shared = jnp.concatenate([g_qkv, g_proj, small], axis=1)
    shared = halving_scatter(shared, "shard")
    if late:
        owned = halving_scatter(shared, "expert")
        owned = lax.reduce_precision(owned, exponent_bits=8, mantissa_bits=7)
        shared = doubling_gather(owned.astype(jnp.bfloat16), "expert").astype(jnp.float32)
    else:
        shared = lax.psum(shared.astype(jnp.bfloat16), "expert").astype(jnp.float32)
    tail = shared[:, qkv_cols + proj_cols :]
    return [
        tail[:, 0:2].T,
        tail[:, 2:4].T,
        shared[:, :qkv_cols],
        shared[:, qkv_cols : qkv_cols + proj_cols],
        tail[:, 4:],
        halving_scatter(g_in[0], "shard")[None],
        halving_scatter(g_out[0], "shard")[None],
    ]


def local(
    tokens,
    routes,
    priority,
    norm_gain,
    norm_bias,
    w_qkv,
    w_proj,
    w_router,
    exp_in,
    exp_out,
    cotangent,
):
    experts = lax.axis_size("expert") * EXP_DEV
    capacity = max(8, (5 * TOK_MB // (2 * experts) + 7) // 8 * 8)
    tok_count = tokens.shape[0]
    blocks = tok_count // TOK_MB
    streams = []
    for block in range(blocks):
        rows = slice(block * TOK_MB, (block + 1) * TOK_MB)
        route_ids = routes[rows]
        tables = slot_onehot(route_ids, priority[rows], experts, capacity)
        route_hot = (
            route_ids[..., None] == jnp.arange(experts, dtype=jnp.int32)
        ).astype(jnp.float32)
        streams.append((rows, tables, route_hot))
    layer_count = norm_gain.shape[0]
    small = jnp.concatenate(
        [
            norm_gain.reshape(layer_count * 2, -1).T,
            norm_bias.reshape(layer_count * 2, -1).T,
            w_router.transpose(1, 0, 2).reshape(w_router.shape[1], -1),
        ],
        axis=1,
    )
    small = lax.all_gather(small, "shard", axis=0, tiled=True)
    qkv_cols = w_qkv.shape[2]
    all_weights = []
    for layer_index in range(LAYERS):
        attn = lax.all_gather(
            jnp.concatenate([w_qkv[layer_index], w_proj[layer_index]], axis=1),
            "shard",
            axis=0,
            tiled=True,
        )
        shift_at = 2 * layer_count + 2 * layer_index
        router_at = 4 * layer_count + experts * layer_index
        all_weights.append(
            (
                small[:, 2 * layer_index : 2 * layer_index + 2].T,
                small[:, shift_at : shift_at + 2].T,
                attn[:, :qkv_cols],
                attn[:, qkv_cols:],
                small[:, router_at : router_at + experts],
                lax.all_gather(exp_in[layer_index], "shard", axis=1, tiled=True),
                lax.all_gather(exp_out[layer_index], "shard", axis=1, tiled=True),
            )
        )
    residuals = [tokens[rows] for rows, _, _ in streams]
    saved = [[None] * LAYERS for _ in streams]
    for layer_index in range(LAYERS):
        staged = []
        for block, (rows, tables, route_hot) in enumerate(streams):
            attn_weights, own_rows = lax.optimization_barrier(
                (all_weights[layer_index][:5], residuals[block])
            )
            own_weights = tuple(attn_weights) + tuple(all_weights[layer_index][5:])
            staged.append(forward_attend(own_rows, tables, own_weights))
        for block, (rows, tables, route_hot) in enumerate(streams):
            carry, sending = staged[block]
            residuals[block], saved[block][layer_index] = forward_expert(
                carry, sending, route_hot, tables, all_weights[layer_index], experts, capacity
            )
    activations = jnp.concatenate(residuals, axis=0)
    d_residuals = [cotangent[rows] for rows, _, _ in streams]
    reduced = [None] * LAYERS
    for layer_index in reversed(range(LAYERS)):
        layer_sum = None
        for block, (rows, tables, route_hot) in enumerate(streams):
            d_residuals[block], layer_grads = backward_layer(
                d_residuals[block],
                saved[block][layer_index],
                route_hot,
                tables,
                all_weights[layer_index],
                experts,
                capacity,
            )
            if layer_sum is None:
                layer_sum = layer_grads
            else:
                layer_sum = tuple(old + new for old, new in zip(layer_sum, layer_grads))
        if layer_index == 0:
            reduced[layer_index] = reduce_layer(layer_sum, True)
        else:
            reduced[layer_index] = reduce_layer(layer_sum, False)
    outs = [jnp.stack([reduced[l][k] for l in range(LAYERS)]) for k in range(7)]
    d_tokens = jnp.concatenate(d_residuals, axis=0)
    return (activations, d_tokens, *outs)


def solution(mesh):
    return jax.shard_map(
        local,
        mesh=mesh,
        in_specs=(
            P(("expert", "shard"), None),
            P(("expert", "shard"), None),
            P(("expert", "shard")),
            P(None, None, "shard"),
            P(None, None, "shard"),
            P(None, "shard", None),
            P(None, "shard", None),
            P(None, "shard", None),
            P(None, "expert", "shard", None),
            P(None, "expert", "shard", None),
            P(("expert", "shard"), None),
        ),
        out_specs=(
            P(("expert", "shard"), None),
            P(("expert", "shard"), None),
            P(None, None, "shard"),
            P(None, None, "shard"),
            P(None, "shard", None),
            P(None, "shard", None),
            P(None, "shard", None),
            P(None, "expert", "shard", None),
            P(None, "expert", "shard", None),
        ),
        check_vma=False,
    )
```

```python
import jax
import jax.numpy as jnp
from jax import lax
from jax.sharding import PartitionSpec as P


D = 512
HEADS = 8
HEAD = 64
EXP_DEV = 1
SEQ = 197
LAYERS = 2
TOP = 2
TOK_MB = 394


norm_eps = 1e-06


def layer_norm(values, norm_scale, norm_shift):
    centre = values - jnp.mean(values, axis=-1, keepdims=True)
    spread = jnp.mean(centre * centre, axis=-1, keepdims=True)
    return centre * lax.rsqrt(spread + norm_eps) * norm_scale + norm_shift


def gelu_tanh(values):
    return jax.nn.gelu(values, approximate=True)


def dot_first(left, right):
    return lax.dot_general(
        left, right, (((0,), (0,)), ((), ())), preferred_element_type=jnp.float32
    )


def dot_last(left, right):
    return lax.dot_general(
        left, right, (((1,), (1,)), ((), ())), preferred_element_type=jnp.float32
    )


def slot_onehot(route_ids, prio_rank, experts, capacity):
    tok_count = route_ids.shape[0]
    order_key = jnp.concatenate([prio_rank, prio_rank + tok_count])
    pair_expert = jnp.concatenate([route_ids[:, 0], route_ids[:, 1]])
    expert_hot = (pair_expert[:, None] == jnp.arange(experts, dtype=jnp.int32)[None, :]).astype(
        jnp.bfloat16
    )
    earlier = (order_key[:, None] < order_key[None, :]).astype(jnp.bfloat16)
    counts = dot_first(expert_hot, earlier)
    position = jnp.sum(counts.T * expert_hot.astype(jnp.float32), axis=1).astype(jnp.int32)
    kept_mask = position < capacity
    flat_slot = jnp.where(kept_mask, pair_expert * capacity + position, experts * capacity)
    pair_hot = (
        flat_slot[:, None] == jnp.arange(experts * capacity, dtype=jnp.int32)[None, :]
    ).astype(jnp.bfloat16)
    token_hot = pair_hot[:tok_count] + pair_hot[tok_count:]
    return pair_hot, token_hot, kept_mask


def exchange(blocks, axis_name):
    return lax.all_to_all(blocks, axis_name, split_axis=0, concat_axis=0, tiled=True)


def forward_attend(residual, tables, weights):
    norm_gains, norm_shifts, qkv_w, proj_w, router_w, _, _ = weights
    _, token_hot, _ = tables
    tok_count = residual.shape[0]
    seq_count = tok_count // SEQ
    score_scale = HEAD ** (-0.5)
    norm_scale = norm_gains.astype(jnp.float32)
    norm_shift = norm_shifts.astype(jnp.float32)
    normed = layer_norm(residual, norm_scale[0], norm_shift[0]).astype(jnp.bfloat16)
    qkv_rows = jnp.dot(normed, qkv_w, preferred_element_type=jnp.float32).astype(jnp.bfloat16)
    heads = qkv_rows.reshape(seq_count, SEQ, 3, HEADS, HEAD)
    scores = (
        jnp.einsum(
            "sqhd,skhd->shqk", heads[:, :, 0], heads[:, :, 1], preferred_element_type=jnp.float32
        )
        * score_scale
    )
    row_top = jnp.max(scores, axis=-1, keepdims=True)
    scores_exp = jnp.exp(scores - row_top)
    row_total = jnp.sum(scores_exp, axis=-1, keepdims=True)
    soft_scores = scores_exp / row_total
    log_total = row_top + jnp.log(row_total)
    mixed_heads = jnp.einsum(
        "shqk,skhd->sqhd",
        soft_scores.astype(jnp.bfloat16),
        heads[:, :, 2],
        preferred_element_type=jnp.float32,
    )
    mixed_heads = mixed_heads.astype(jnp.bfloat16).reshape(tok_count, D)
    middle = residual + jnp.dot(mixed_heads, proj_w, preferred_element_type=jnp.float32)
    normed_two = layer_norm(middle, norm_scale[1], norm_shift[1]).astype(jnp.bfloat16)
    gate_probs = jax.nn.softmax(
        jnp.dot(normed_two, router_w, preferred_element_type=jnp.float32), axis=-1
    )
    sending = dot_first(token_hot, normed_two).astype(jnp.bfloat16)
    carry = (residual, normed, heads, log_total, mixed_heads, middle, normed_two, gate_probs)
    return carry, sending


def forward_expert(carry, sending, route_hot, tables, weights, experts, capacity):
    _, _, _, _, _, in_w, out_w = weights
    received = exchange(sending.reshape(experts, capacity, D), "expert")
    row_block = received.reshape(experts * capacity, D)
    hidden_pre = jnp.dot(row_block, in_w[0], preferred_element_type=jnp.float32)
    hidden_act = gelu_tanh(hidden_pre).astype(jnp.bfloat16)
    expert_rows = jnp.dot(hidden_act, out_w[0], preferred_element_type=jnp.float32).astype(
        jnp.bfloat16
    )
    returned = exchange(expert_rows.reshape(experts, capacity, D), "expert")
    return forward_combine(
        carry, returned, row_block, hidden_pre, route_hot, tables, experts, capacity
    )


def forward_combine(carry, returned, row_block, hidden_pre, route_hot, tables, experts, capacity):
    residual, normed, heads, log_total, mixed_heads, middle, normed_two, gate_probs = carry
    pair_hot, _, kept_mask = tables
    tok_count = residual.shape[0]
    pair_rows = jnp.dot(
        pair_hot, returned.reshape(experts * capacity, D), preferred_element_type=jnp.float32
    ).reshape(TOP, tok_count, D)
    chosen = jnp.sum(route_hot * gate_probs[:, None, :], axis=-1)
    kept_gate = kept_mask.astype(jnp.float32).reshape(TOP, tok_count)
    weight_pair = kept_gate * chosen.T
    combined = jnp.sum(weight_pair[..., None] * pair_rows, axis=0)
    output = middle + combined
    saved_state = (
        residual,
        normed,
        heads,
        log_total,
        mixed_heads,
        middle,
        normed_two,
        gate_probs,
        kept_gate,
        weight_pair,
        pair_rows,
        row_block,
        hidden_pre,
    )
    return (output, saved_state)


def backward_layer(d_output, saved_state, route_hot, tables, weights, experts, capacity):
    (_, _, _, _, _, _, _, _, _, _, _, row_block, hidden_pre) = saved_state
    _, _, _, _, router_w, in_w, out_w = weights
    d_slots, g_router, d_normed_two = backward_route(
        d_output, saved_state, tables, route_hot, router_w, experts, capacity
    )
    d_expert_out = exchange(d_slots, "expert")
    flat_out = d_expert_out.reshape(experts * capacity, D)
    hidden_act = gelu_tanh(hidden_pre).astype(jnp.bfloat16)
    g_out = dot_first(hidden_act, flat_out)
    d_act = dot_last(flat_out, out_w[0])
    d_pre = jax.vjp(gelu_tanh, hidden_pre)[1](d_act)[0].astype(jnp.bfloat16)
    g_in = dot_first(row_block, d_pre)
    d_rows = dot_last(d_pre, in_w[0]).astype(jnp.bfloat16).reshape(experts, capacity, D)
    d_back = exchange(d_rows, "expert")
    d_residual, grads = backward_attend(
        d_output, saved_state, d_back, d_normed_two, tables, weights, experts, capacity
    )
    g_gain, g_shift, g_qkv, g_proj = grads
    return (d_residual, (g_gain, g_shift, g_qkv, g_proj, g_router, g_in[None], g_out[None]))


def backward_route(d_output, saved_state, tables, route_hot, router_w, experts, capacity):
    (
        residual, _, _, _, _, _, normed_two, gate_probs, kept_gate, weight_pair, pair_rows, _, _
    ) = saved_state
    pair_hot, _, _ = tables
    tok_count = residual.shape[0]
    d_gate_pair = kept_gate * jnp.sum(d_output[None] * pair_rows, axis=-1)
    d_gates = jnp.sum(route_hot * d_gate_pair.T[:, :, None], axis=1)
    d_logits = (
        gate_probs * (d_gates - jnp.sum(gate_probs * d_gates, axis=-1, keepdims=True))
    ).astype(jnp.bfloat16)
    g_router = dot_first(normed_two, d_logits)
    d_normed_two = dot_last(d_logits, router_w)
    d_pairs = (
        (weight_pair[:, :, None] * d_output[None]).astype(jnp.bfloat16).reshape(TOP * tok_count, D)
    )
    d_slots = dot_first(pair_hot, d_pairs).astype(jnp.bfloat16).reshape(experts, capacity, D)
    return d_slots, g_router, d_normed_two


def backward_attend(d_output, saved_state, d_back, d_normed_two, tables, weights, experts, capacity):
    (residual, normed, heads, log_total, mixed_heads, middle, _, _, _, _, _, _, _) = saved_state
    pair_hot, _, _ = tables
    norm_gains, norm_shifts, qkv_w, proj_w, _, _, _ = weights
    tok_count = residual.shape[0]
    seq_count = tok_count // SEQ
    score_scale = HEAD ** (-0.5)
    norm_scale = norm_gains.astype(jnp.float32)
    norm_shift = norm_shifts.astype(jnp.float32)
    d_pair_in = jnp.dot(
        pair_hot, d_back.reshape(experts * capacity, D), preferred_element_type=jnp.float32
    ).reshape(TOP, tok_count, D)
    d_normed_two = d_normed_two + jnp.sum(d_pair_in, axis=0)
    pulled_two = jax.vjp(layer_norm, middle, norm_scale[1], norm_shift[1])[1](d_normed_two)
    d_middle = d_output + pulled_two[0]
    d_branch = d_middle.astype(jnp.bfloat16)
    g_proj = dot_first(mixed_heads, d_branch)
    d_mixed = dot_last(d_branch, proj_w).astype(jnp.bfloat16).reshape(seq_count, SEQ, HEADS, HEAD)
    query_heads = heads[:, :, 0]
    key_heads = heads[:, :, 1]
    value_heads = heads[:, :, 2]
    scores = (
        jnp.einsum("sqhd,skhd->shqk", query_heads, key_heads, preferred_element_type=jnp.float32)
        * score_scale
    )
    soft_scores = jnp.exp(scores - log_total)
    d_soft = jnp.einsum("sqhd,skhd->shqk", d_mixed, value_heads, preferred_element_type=jnp.float32)
    d_values = jnp.einsum(
        "shqk,sqhd->skhd",
        soft_scores.astype(jnp.bfloat16),
        d_mixed,
        preferred_element_type=jnp.float32,
    )
    d_scores = (
        soft_scores * (d_soft - jnp.sum(soft_scores * d_soft, axis=-1, keepdims=True))
    ).astype(jnp.bfloat16)
    d_query = (
        jnp.einsum("shqk,skhd->sqhd", d_scores, key_heads, preferred_element_type=jnp.float32)
        * score_scale
    )
    d_keys = (
        jnp.einsum("shqk,sqhd->skhd", d_scores, query_heads, preferred_element_type=jnp.float32)
        * score_scale
    )
    d_qkv = (
        jnp.stack([d_query, d_keys, d_values], axis=2)
        .reshape(tok_count, 3 * D)
        .astype(jnp.bfloat16)
    )
    g_qkv = dot_first(normed, d_qkv)
    d_normed = dot_last(d_qkv, qkv_w)
    pulled_one = jax.vjp(layer_norm, residual, norm_scale[0], norm_shift[0])[1](d_normed)
    d_residual = d_middle + pulled_one[0]
    g_gain = jnp.stack([pulled_one[1], pulled_two[1]])
    g_shift = jnp.stack([pulled_one[2], pulled_two[2]])
    return d_residual, (g_gain, g_shift, g_qkv, g_proj)


def halving_scatter(grad, axis_name):
    size = lax.axis_size(axis_name)
    me = lax.axis_index(axis_name)
    chunk = grad.shape[0] // size
    rest = grad.shape[1:]
    total = grad.reshape(size, chunk, *rest)
    bit = 1
    while bit < size:
        pairs = total.reshape(total.shape[0] // 2, 2, chunk, *rest)
        mine = (me // bit) % 2
        keep = lax.dynamic_index_in_dim(pairs, mine, axis=1, keepdims=False)
        give = lax.dynamic_index_in_dim(pairs, 1 - mine, axis=1, keepdims=False)
        got = lax.ppermute(
            give.astype(jnp.bfloat16), axis_name, [(i, i ^ bit) for i in range(size)]
        )
        total = keep.astype(jnp.float32) + got.astype(jnp.float32)
        bit *= 2
    return total.reshape(chunk, *rest)


def doubling_gather(part, axis_name):
    size = lax.axis_size(axis_name)
    me = lax.axis_index(axis_name)
    held = part[None]
    bit = size // 2
    steps = 0
    while bit >= 1:
        got = lax.ppermute(held, axis_name, [(i, i ^ bit) for i in range(size)])
        low = (me // bit) % 2 == 0
        held = jnp.where(low, jnp.concatenate([held, got]), jnp.concatenate([got, held]))
        bit //= 2
        steps += 1
    held = held.reshape((2,) * steps + part.shape)
    held = held.transpose(tuple(reversed(range(steps))) + tuple(range(steps, held.ndim)))
    return held.reshape((size * part.shape[0],) + part.shape[1:])


def expert_sum(part):
    owned = halving_scatter(part, "expert")
    owned = lax.reduce_precision(owned, exponent_bits=8, mantissa_bits=7)
    return doubling_gather(owned.astype(jnp.bfloat16), "expert").astype(jnp.float32)


def reduce_layer(layer_grads, late):
    g_gain, g_shift, g_qkv, g_proj, g_router, g_in, g_out = layer_grads
    qkv_cols = g_qkv.shape[1]
    proj_cols = g_proj.shape[1]
    small = jnp.concatenate([g_gain.T, g_shift.T, g_router], axis=1)
    if late:
        early = jnp.concatenate([g_proj, small], axis=1).astype(jnp.bfloat16)
        early = expert_sum(halving_scatter(early, "shard"))
        qkv = expert_sum(halving_scatter(g_qkv.astype(jnp.bfloat16), "shard"))
        proj = early[:, :proj_cols]
        tail = early[:, proj_cols:]
    else:
        shared = jnp.concatenate([g_qkv, g_proj, small], axis=1)
        shared = halving_scatter(shared, "shard")
        shared = lax.psum(shared.astype(jnp.bfloat16), "expert").astype(jnp.float32)
        qkv = shared[:, :qkv_cols]
        proj = shared[:, qkv_cols : qkv_cols + proj_cols]
        tail = shared[:, qkv_cols + proj_cols :]
    return [
        tail[:, 0:2].T,
        tail[:, 2:4].T,
        qkv,
        proj,
        tail[:, 4:],
        halving_scatter(g_in[0], "shard")[None],
        halving_scatter(g_out[0], "shard")[None],
    ]


def local(
    tokens,
    routes,
    priority,
    norm_gain,
    norm_bias,
    w_qkv,
    w_proj,
    w_router,
    exp_in,
    exp_out,
    cotangent,
):
    experts = lax.axis_size("expert") * EXP_DEV
    capacity = max(8, (5 * TOK_MB // (2 * experts) + 7) // 8 * 8)
    tok_count = tokens.shape[0]
    blocks = tok_count // TOK_MB
    streams = []
    for block in range(blocks):
        rows = slice(block * TOK_MB, (block + 1) * TOK_MB)
        route_ids = routes[rows]
        tables = slot_onehot(route_ids, priority[rows], experts, capacity)
        route_hot = (
            route_ids[..., None] == jnp.arange(experts, dtype=jnp.int32)
        ).astype(jnp.float32)
        streams.append((rows, tables, route_hot))
    layer_count = norm_gain.shape[0]
    small = jnp.concatenate(
        [
            norm_gain.reshape(layer_count * 2, -1).T,
            norm_bias.reshape(layer_count * 2, -1).T,
            w_router.transpose(1, 0, 2).reshape(w_router.shape[1], -1),
        ],
        axis=1,
    )
    small = lax.all_gather(small, "shard", axis=0, tiled=True)
    qkv_cols = w_qkv.shape[2]
    all_weights = []
    for layer_index in range(LAYERS):
        attn = lax.all_gather(
            jnp.concatenate([w_qkv[layer_index], w_proj[layer_index]], axis=1),
            "shard",
            axis=0,
            tiled=True,
        )
        shift_at = 2 * layer_count + 2 * layer_index
        router_at = 4 * layer_count + experts * layer_index
        all_weights.append(
            (
                small[:, 2 * layer_index : 2 * layer_index + 2].T,
                small[:, shift_at : shift_at + 2].T,
                attn[:, :qkv_cols],
                attn[:, qkv_cols:],
                small[:, router_at : router_at + experts],
                lax.all_gather(exp_in[layer_index], "shard", axis=1, tiled=True),
                lax.all_gather(exp_out[layer_index], "shard", axis=1, tiled=True),
            )
        )
    residuals = [tokens[rows] for rows, _, _ in streams]
    saved = [[None] * LAYERS for _ in streams]
    for layer_index in range(LAYERS):
        staged = []
        for block, (rows, tables, route_hot) in enumerate(streams):
            attn_weights, own_rows = lax.optimization_barrier(
                (all_weights[layer_index][:5], residuals[block])
            )
            own_weights = tuple(attn_weights) + tuple(all_weights[layer_index][5:])
            staged.append(forward_attend(own_rows, tables, own_weights))
        for block, (rows, tables, route_hot) in enumerate(streams):
            carry, sending = staged[block]
            residuals[block], saved[block][layer_index] = forward_expert(
                carry, sending, route_hot, tables, all_weights[layer_index], experts, capacity
            )
    activations = jnp.concatenate(residuals, axis=0)
    d_residuals = [cotangent[rows] for rows, _, _ in streams]
    reduced = [None] * LAYERS
    for layer_index in reversed(range(LAYERS)):
        layer_sum = None
        for block, (rows, tables, route_hot) in enumerate(streams):
            d_residuals[block], layer_grads = backward_layer(
                d_residuals[block],
                saved[block][layer_index],
                route_hot,
                tables,
                all_weights[layer_index],
                experts,
                capacity,
            )
            if layer_sum is None:
                layer_sum = layer_grads
            else:
                layer_sum = tuple(old + new for old, new in zip(layer_sum, layer_grads))
        if layer_index == 0:
            reduced[layer_index] = reduce_layer(layer_sum, True)
        else:
            reduced[layer_index] = reduce_layer(layer_sum, False)
    outs = [jnp.stack([reduced[l][k] for l in range(LAYERS)]) for k in range(7)]
    d_tokens = jnp.concatenate(d_residuals, axis=0)
    return (activations, d_tokens, *outs)


def solution(mesh):
    return jax.shard_map(
        local,
        mesh=mesh,
        in_specs=(
            P(("expert", "shard"), None),
            P(("expert", "shard"), None),
            P(("expert", "shard")),
            P(None, None, "shard"),
            P(None, None, "shard"),
            P(None, "shard", None),
            P(None, "shard", None),
            P(None, "shard", None),
            P(None, "expert", "shard", None),
            P(None, "expert", "shard", None),
            P(("expert", "shard"), None),
        ),
        out_specs=(
            P(("expert", "shard"), None),
            P(("expert", "shard"), None),
            P(None, None, "shard"),
            P(None, None, "shard"),
            P(None, "shard", None),
            P(None, "shard", None),
            P(None, "shard", None),
            P(None, "expert", "shard", None),
            P(None, "expert", "shard", None),
        ),
        check_vma=False,
    )
```

```python
import jax
import jax.numpy as jnp
from jax import lax
from jax.sharding import PartitionSpec as P


D = 512
HEADS = 8
HEAD = 64
EXP_DEV = 1
SEQ = 197
LAYERS = 2
TOP = 2
TOK_MB = 394


norm_eps = 1e-06


def layer_norm(values, norm_scale, norm_shift):
    centre = values - jnp.mean(values, axis=-1, keepdims=True)
    spread = jnp.mean(centre * centre, axis=-1, keepdims=True)
    return centre * lax.rsqrt(spread + norm_eps) * norm_scale + norm_shift


def gelu_tanh(values):
    return jax.nn.gelu(values, approximate=True)


def dot_first(left, right):
    return lax.dot_general(
        left, right, (((0,), (0,)), ((), ())), preferred_element_type=jnp.float32
    )


def dot_last(left, right):
    return lax.dot_general(
        left, right, (((1,), (1,)), ((), ())), preferred_element_type=jnp.float32
    )


def same_image(tok_count):
    image = jnp.arange(tok_count, dtype=jnp.int32) // SEQ
    return image[:, None] == image[None, :]


def slot_onehot(route_ids, prio_rank, experts, capacity):
    tok_count = route_ids.shape[0]
    order_key = jnp.concatenate([prio_rank, prio_rank + tok_count])
    pair_expert = jnp.concatenate([route_ids[:, 0], route_ids[:, 1]])
    expert_hot = (pair_expert[:, None] == jnp.arange(experts, dtype=jnp.int32)[None, :]).astype(
        jnp.bfloat16
    )
    earlier = (order_key[:, None] < order_key[None, :]).astype(jnp.bfloat16)
    counts = dot_first(expert_hot, earlier)
    position = jnp.sum(counts.T * expert_hot.astype(jnp.float32), axis=1).astype(jnp.int32)
    kept_mask = position < capacity
    flat_slot = jnp.where(kept_mask, pair_expert * capacity + position, experts * capacity)
    pair_hot = (
        flat_slot[:, None] == jnp.arange(experts * capacity, dtype=jnp.int32)[None, :]
    ).astype(jnp.bfloat16)
    token_hot = pair_hot[:tok_count] + pair_hot[tok_count:]
    return pair_hot, token_hot, kept_mask


def exchange(blocks, axis_name):
    return lax.all_to_all(blocks, axis_name, split_axis=0, concat_axis=0, tiled=True)


def forward_attend(residual, tables, weights):
    norm_gains, norm_shifts, qkv_w, proj_w, router_w, _, _ = weights
    _, token_hot, _ = tables
    tok_count = residual.shape[0]
    score_scale = HEAD ** (-0.5)
    norm_scale = norm_gains.astype(jnp.float32)
    norm_shift = norm_shifts.astype(jnp.float32)
    normed = layer_norm(residual, norm_scale[0], norm_shift[0]).astype(jnp.bfloat16)
    qkv_rows = jnp.dot(normed, qkv_w, preferred_element_type=jnp.float32).astype(jnp.bfloat16)
    heads = qkv_rows.reshape(tok_count, 3, HEADS, HEAD)
    scores = jnp.where(
        same_image(tok_count),
        jnp.einsum(
            "thd,shd->hts", heads[:, 0], heads[:, 1], preferred_element_type=jnp.float32
        )
        * score_scale,
        -jnp.inf,
    )
    row_top = jnp.max(scores, axis=-1, keepdims=True)
    scores_exp = jnp.exp(scores - row_top)
    row_total = jnp.sum(scores_exp, axis=-1, keepdims=True)
    soft_scores = scores_exp / row_total
    log_total = row_top + jnp.log(row_total)
    mixed_heads = jnp.einsum(
        "hts,shd->thd",
        soft_scores.astype(jnp.bfloat16),
        heads[:, 2],
        preferred_element_type=jnp.float32,
    )
    mixed_heads = mixed_heads.astype(jnp.bfloat16).reshape(tok_count, D)
    middle = residual + jnp.dot(mixed_heads, proj_w, preferred_element_type=jnp.float32)
    normed_two = layer_norm(middle, norm_scale[1], norm_shift[1]).astype(jnp.bfloat16)
    gate_probs = jax.nn.softmax(
        jnp.dot(normed_two, router_w, preferred_element_type=jnp.float32), axis=-1
    )
    sending = dot_first(token_hot, normed_two).astype(jnp.bfloat16)
    carry = (residual, normed, heads, log_total, mixed_heads, middle, normed_two, gate_probs)
    return carry, sending


def forward_expert(carry, sending, route_hot, tables, weights, experts, capacity):
    _, _, _, _, _, in_w, out_w = weights
    received = exchange(sending.reshape(experts, capacity, D), "expert")
    row_block = received.reshape(experts * capacity, D)
    hidden_pre = jnp.dot(row_block, in_w[0], preferred_element_type=jnp.float32)
    hidden_act = gelu_tanh(hidden_pre).astype(jnp.bfloat16)
    expert_rows = jnp.dot(hidden_act, out_w[0], preferred_element_type=jnp.float32).astype(
        jnp.bfloat16
    )
    returned = exchange(expert_rows.reshape(experts, capacity, D), "expert")
    return forward_combine(
        carry, returned, row_block, hidden_pre, route_hot, tables, experts, capacity
    )


def forward_combine(carry, returned, row_block, hidden_pre, route_hot, tables, experts, capacity):
    residual, normed, heads, log_total, mixed_heads, middle, normed_two, gate_probs = carry
    pair_hot, _, kept_mask = tables
    tok_count = residual.shape[0]
    pair_rows = jnp.dot(
        pair_hot, returned.reshape(experts * capacity, D), preferred_element_type=jnp.float32
    ).reshape(TOP, tok_count, D)
    chosen = jnp.sum(route_hot * gate_probs[:, None, :], axis=-1)
    kept_gate = kept_mask.astype(jnp.float32).reshape(TOP, tok_count)
    weight_pair = kept_gate * chosen.T
    combined = jnp.sum(weight_pair[..., None] * pair_rows, axis=0)
    output = middle + combined
    saved_state = (
        residual,
        normed,
        heads,
        log_total,
        mixed_heads,
        middle,
        normed_two,
        gate_probs,
        kept_gate,
        weight_pair,
        pair_rows,
        row_block,
        hidden_pre,
    )
    return (output, saved_state)


def backward_layer(d_output, saved_state, route_hot, tables, weights, experts, capacity):
    (_, _, _, _, _, _, _, _, _, _, _, row_block, hidden_pre) = saved_state
    _, _, _, _, router_w, in_w, out_w = weights
    d_slots, g_router, d_normed_two = backward_route(
        d_output, saved_state, tables, route_hot, router_w, experts, capacity
    )
    d_expert_out = exchange(d_slots, "expert")
    flat_out = d_expert_out.reshape(experts * capacity, D)
    hidden_act = gelu_tanh(hidden_pre).astype(jnp.bfloat16)
    g_out = dot_first(hidden_act, flat_out)
    d_act = dot_last(flat_out, out_w[0])
    d_pre = jax.vjp(gelu_tanh, hidden_pre)[1](d_act)[0].astype(jnp.bfloat16)
    g_in = dot_first(row_block, d_pre)
    d_rows = dot_last(d_pre, in_w[0]).astype(jnp.bfloat16).reshape(experts, capacity, D)
    d_back = exchange(d_rows, "expert")
    d_residual, grads = backward_attend(
        d_output, saved_state, d_back, d_normed_two, tables, weights, experts, capacity
    )
    g_gain, g_shift, g_qkv, g_proj = grads
    return (d_residual, (g_gain, g_shift, g_qkv, g_proj, g_router, g_in[None], g_out[None]))


def backward_route(d_output, saved_state, tables, route_hot, router_w, experts, capacity):
    (
        residual, _, _, _, _, _, normed_two, gate_probs, kept_gate, weight_pair, pair_rows, _, _
    ) = saved_state
    pair_hot, _, _ = tables
    tok_count = residual.shape[0]
    d_gate_pair = kept_gate * jnp.sum(d_output[None] * pair_rows, axis=-1)
    d_gates = jnp.sum(route_hot * d_gate_pair.T[:, :, None], axis=1)
    d_logits = (
        gate_probs * (d_gates - jnp.sum(gate_probs * d_gates, axis=-1, keepdims=True))
    ).astype(jnp.bfloat16)
    g_router = dot_first(normed_two, d_logits)
    d_normed_two = dot_last(d_logits, router_w)
    d_pairs = (
        (weight_pair[:, :, None] * d_output[None]).astype(jnp.bfloat16).reshape(TOP * tok_count, D)
    )
    d_slots = dot_first(pair_hot, d_pairs).astype(jnp.bfloat16).reshape(experts, capacity, D)
    return d_slots, g_router, d_normed_two


def backward_attend(d_output, saved_state, d_back, d_normed_two, tables, weights, experts, capacity):
    (residual, normed, heads, log_total, mixed_heads, middle, _, _, _, _, _, _, _) = saved_state
    pair_hot, _, _ = tables
    norm_gains, norm_shifts, qkv_w, proj_w, _, _, _ = weights
    tok_count = residual.shape[0]
    score_scale = HEAD ** (-0.5)
    norm_scale = norm_gains.astype(jnp.float32)
    norm_shift = norm_shifts.astype(jnp.float32)
    d_pair_in = jnp.dot(
        pair_hot, d_back.reshape(experts * capacity, D), preferred_element_type=jnp.float32
    ).reshape(TOP, tok_count, D)
    d_normed_two = d_normed_two + jnp.sum(d_pair_in, axis=0)
    pulled_two = jax.vjp(layer_norm, middle, norm_scale[1], norm_shift[1])[1](d_normed_two)
    d_middle = d_output + pulled_two[0]
    d_branch = d_middle.astype(jnp.bfloat16)
    g_proj = dot_first(mixed_heads, d_branch)
    d_mixed = dot_last(d_branch, proj_w).astype(jnp.bfloat16).reshape(tok_count, HEADS, HEAD)
    query_heads = heads[:, 0]
    key_heads = heads[:, 1]
    value_heads = heads[:, 2]
    scores = jnp.where(
        same_image(tok_count),
        jnp.einsum("thd,shd->hts", query_heads, key_heads, preferred_element_type=jnp.float32)
        * score_scale,
        -jnp.inf,
    )
    soft_scores = jnp.exp(scores - log_total)
    d_soft = jnp.einsum("thd,shd->hts", d_mixed, value_heads, preferred_element_type=jnp.float32)
    d_values = jnp.einsum(
        "hts,thd->shd",
        soft_scores.astype(jnp.bfloat16),
        d_mixed,
        preferred_element_type=jnp.float32,
    )
    d_scores = (
        soft_scores * (d_soft - jnp.sum(soft_scores * d_soft, axis=-1, keepdims=True))
    ).astype(jnp.bfloat16)
    d_query = (
        jnp.einsum("hts,shd->thd", d_scores, key_heads, preferred_element_type=jnp.float32)
        * score_scale
    )
    d_keys = (
        jnp.einsum("hts,thd->shd", d_scores, query_heads, preferred_element_type=jnp.float32)
        * score_scale
    )
    d_qkv = (
        jnp.stack([d_query, d_keys, d_values], axis=1)
        .reshape(tok_count, 3 * D)
        .astype(jnp.bfloat16)
    )
    g_qkv = dot_first(normed, d_qkv)
    d_normed = dot_last(d_qkv, qkv_w)
    pulled_one = jax.vjp(layer_norm, residual, norm_scale[0], norm_shift[0])[1](d_normed)
    d_residual = d_middle + pulled_one[0]
    g_gain = jnp.stack([pulled_one[1], pulled_two[1]])
    g_shift = jnp.stack([pulled_one[2], pulled_two[2]])
    return d_residual, (g_gain, g_shift, g_qkv, g_proj)


def halving_scatter(grad, axis_name):
    size = lax.axis_size(axis_name)
    me = lax.axis_index(axis_name)
    chunk = grad.shape[0] // size
    rest = grad.shape[1:]
    total = grad.reshape(size, chunk, *rest)
    bit = 1
    while bit < size:
        pairs = total.reshape(total.shape[0] // 2, 2, chunk, *rest)
        mine = (me // bit) % 2
        keep = lax.dynamic_index_in_dim(pairs, mine, axis=1, keepdims=False)
        give = lax.dynamic_index_in_dim(pairs, 1 - mine, axis=1, keepdims=False)
        got = lax.ppermute(
            give.astype(jnp.bfloat16), axis_name, [(i, i ^ bit) for i in range(size)]
        )
        total = keep.astype(jnp.float32) + got.astype(jnp.float32)
        bit *= 2
    return total.reshape(chunk, *rest)


def doubling_gather(part, axis_name):
    size = lax.axis_size(axis_name)
    me = lax.axis_index(axis_name)
    held = part[None]
    bit = size // 2
    steps = 0
    while bit >= 1:
        got = lax.ppermute(held, axis_name, [(i, i ^ bit) for i in range(size)])
        low = (me // bit) % 2 == 0
        held = jnp.where(low, jnp.concatenate([held, got]), jnp.concatenate([got, held]))
        bit //= 2
        steps += 1
    held = held.reshape((2,) * steps + part.shape)
    held = held.transpose(tuple(reversed(range(steps))) + tuple(range(steps, held.ndim)))
    return held.reshape((size * part.shape[0],) + part.shape[1:])


def expert_sum(part):
    owned = halving_scatter(part, "expert")
    owned = lax.reduce_precision(owned, exponent_bits=8, mantissa_bits=7)
    return doubling_gather(owned.astype(jnp.bfloat16), "expert").astype(jnp.float32)


def reduce_layer(layer_grads, late):
    g_gain, g_shift, g_qkv, g_proj, g_router, g_in, g_out = layer_grads
    qkv_cols = g_qkv.shape[1]
    proj_cols = g_proj.shape[1]
    small = jnp.concatenate([g_gain.T, g_shift.T, g_router], axis=1)
    if late:
        early = jnp.concatenate([g_proj, small], axis=1).astype(jnp.bfloat16)
        early = expert_sum(halving_scatter(early, "shard"))
        qkv = expert_sum(halving_scatter(g_qkv.astype(jnp.bfloat16), "shard"))
        proj = early[:, :proj_cols]
        tail = early[:, proj_cols:]
    else:
        shared = jnp.concatenate([g_qkv, g_proj, small], axis=1)
        shared = halving_scatter(shared, "shard")
        shared = lax.psum(shared.astype(jnp.bfloat16), "expert").astype(jnp.float32)
        qkv = shared[:, :qkv_cols]
        proj = shared[:, qkv_cols : qkv_cols + proj_cols]
        tail = shared[:, qkv_cols + proj_cols :]
    return [
        tail[:, 0:2].T,
        tail[:, 2:4].T,
        qkv,
        proj,
        tail[:, 4:],
        halving_scatter(g_in[0], "shard")[None],
        halving_scatter(g_out[0], "shard")[None],
    ]


def local(
    tokens,
    routes,
    priority,
    norm_gain,
    norm_bias,
    w_qkv,
    w_proj,
    w_router,
    exp_in,
    exp_out,
    cotangent,
):
    experts = lax.axis_size("expert") * EXP_DEV
    capacity = max(8, (5 * TOK_MB // (2 * experts) + 7) // 8 * 8)
    tok_count = tokens.shape[0]
    blocks = tok_count // TOK_MB
    streams = []
    for block in range(blocks):
        rows = slice(block * TOK_MB, (block + 1) * TOK_MB)
        route_ids = routes[rows]
        tables = slot_onehot(route_ids, priority[rows], experts, capacity)
        route_hot = (
            route_ids[..., None] == jnp.arange(experts, dtype=jnp.int32)
        ).astype(jnp.float32)
        streams.append((rows, tables, route_hot))
    layer_count = norm_gain.shape[0]
    small = jnp.concatenate(
        [
            norm_gain.reshape(layer_count * 2, -1).T,
            norm_bias.reshape(layer_count * 2, -1).T,
            w_router.transpose(1, 0, 2).reshape(w_router.shape[1], -1),
        ],
        axis=1,
    )
    small = lax.all_gather(small, "shard", axis=0, tiled=True)
    qkv_cols = w_qkv.shape[2]
    all_weights = []
    for layer_index in range(LAYERS):
        attn = lax.all_gather(
            jnp.concatenate([w_qkv[layer_index], w_proj[layer_index]], axis=1),
            "shard",
            axis=0,
            tiled=True,
        )
        shift_at = 2 * layer_count + 2 * layer_index
        router_at = 4 * layer_count + experts * layer_index
        all_weights.append(
            (
                small[:, 2 * layer_index : 2 * layer_index + 2].T,
                small[:, shift_at : shift_at + 2].T,
                attn[:, :qkv_cols],
                attn[:, qkv_cols:],
                small[:, router_at : router_at + experts],
                lax.all_gather(exp_in[layer_index], "shard", axis=1, tiled=True),
                lax.all_gather(exp_out[layer_index], "shard", axis=1, tiled=True),
            )
        )
    residuals = [tokens[rows] for rows, _, _ in streams]
    saved = [[None] * LAYERS for _ in streams]
    for layer_index in range(LAYERS):
        staged = []
        for block, (rows, tables, route_hot) in enumerate(streams):
            attn_weights, own_rows = lax.optimization_barrier(
                (all_weights[layer_index][:5], residuals[block])
            )
            own_weights = tuple(attn_weights) + tuple(all_weights[layer_index][5:])
            staged.append(forward_attend(own_rows, tables, own_weights))
        for block, (rows, tables, route_hot) in enumerate(streams):
            carry, sending = staged[block]
            residuals[block], saved[block][layer_index] = forward_expert(
                carry, sending, route_hot, tables, all_weights[layer_index], experts, capacity
            )
    activations = jnp.concatenate(residuals, axis=0)
    d_residuals = [cotangent[rows] for rows, _, _ in streams]
    reduced = [None] * LAYERS
    for layer_index in reversed(range(LAYERS)):
        layer_sum = None
        for block, (rows, tables, route_hot) in enumerate(streams):
            d_residuals[block], layer_grads = backward_layer(
                d_residuals[block],
                saved[block][layer_index],
                route_hot,
                tables,
                all_weights[layer_index],
                experts,
                capacity,
            )
            if layer_sum is None:
                layer_sum = layer_grads
            else:
                layer_sum = tuple(old + new for old, new in zip(layer_sum, layer_grads))
        if layer_index == 0:
            reduced[layer_index] = reduce_layer(layer_sum, True)
        else:
            reduced[layer_index] = reduce_layer(layer_sum, False)
    outs = [jnp.stack([reduced[l][k] for l in range(LAYERS)]) for k in range(7)]
    d_tokens = jnp.concatenate(d_residuals, axis=0)
    return (activations, d_tokens, *outs)


def solution(mesh):
    return jax.shard_map(
        local,
        mesh=mesh,
        in_specs=(
            P(("expert", "shard"), None),
            P(("expert", "shard"), None),
            P(("expert", "shard")),
            P(None, None, "shard"),
            P(None, None, "shard"),
            P(None, "shard", None),
            P(None, "shard", None),
            P(None, "shard", None),
            P(None, "expert", "shard", None),
            P(None, "expert", "shard", None),
            P(("expert", "shard"), None),
        ),
        out_specs=(
            P(("expert", "shard"), None),
            P(("expert", "shard"), None),
            P(None, None, "shard"),
            P(None, None, "shard"),
            P(None, "shard", None),
            P(None, "shard", None),
            P(None, "shard", None),
            P(None, "expert", "shard", None),
            P(None, "expert", "shard", None),
        ),
        check_vma=False,
    )
```

```python
import jax
import jax.numpy as jnp
from jax import lax
from jax.sharding import PartitionSpec as P


D = 512
HEADS = 8
HEAD = 64
EXP_DEV = 1
SEQ = 197
LAYERS = 2
TOP = 2
TOK_MB = 394


norm_eps = 1e-06


def layer_norm(values, norm_scale, norm_shift):
    centre = values - jnp.mean(values, axis=-1, keepdims=True)
    spread = jnp.mean(centre * centre, axis=-1, keepdims=True)
    return centre * lax.rsqrt(spread + norm_eps) * norm_scale + norm_shift


def gelu_tanh(values):
    return jax.nn.gelu(values, approximate=True)


def dot_first(left, right):
    return lax.dot_general(
        left, right, (((0,), (0,)), ((), ())), preferred_element_type=jnp.float32
    )


def dot_last(left, right):
    return lax.dot_general(
        left, right, (((1,), (1,)), ((), ())), preferred_element_type=jnp.float32
    )


def same_image(tok_count):
    image = jnp.arange(tok_count, dtype=jnp.int32) // SEQ
    return image[:, None] == image[None, :]


def slot_onehot(route_ids, prio_rank, experts, capacity):
    tok_count = route_ids.shape[0]
    order_key = jnp.concatenate([prio_rank, prio_rank + tok_count])
    pair_expert = jnp.concatenate([route_ids[:, 0], route_ids[:, 1]])
    expert_hot = (pair_expert[:, None] == jnp.arange(experts, dtype=jnp.int32)[None, :]).astype(
        jnp.bfloat16
    )
    earlier = (order_key[:, None] < order_key[None, :]).astype(jnp.bfloat16)
    counts = dot_first(expert_hot, earlier)
    position = jnp.sum(counts.T * expert_hot.astype(jnp.float32), axis=1).astype(jnp.int32)
    kept_mask = position < capacity
    flat_slot = jnp.where(kept_mask, pair_expert * capacity + position, experts * capacity)
    pair_hot = (
        flat_slot[:, None] == jnp.arange(experts * capacity, dtype=jnp.int32)[None, :]
    ).astype(jnp.bfloat16)
    token_hot = pair_hot[:tok_count] + pair_hot[tok_count:]
    return pair_hot, token_hot, kept_mask


def exchange(blocks, axis_name):
    return lax.all_to_all(blocks, axis_name, split_axis=0, concat_axis=0, tiled=True)


def forward_attend(residual, tables, weights):
    norm_gains, norm_shifts, qkv_w, proj_w, router_w, _, _ = weights
    _, token_hot, _ = tables
    tok_count = residual.shape[0]
    score_scale = HEAD ** (-0.5)
    norm_scale = norm_gains.astype(jnp.float32)
    norm_shift = norm_shifts.astype(jnp.float32)
    normed = layer_norm(residual, norm_scale[0], norm_shift[0]).astype(jnp.bfloat16)
    qkv_rows = jnp.dot(normed, qkv_w, preferred_element_type=jnp.float32).astype(jnp.bfloat16)
    heads = qkv_rows.reshape(tok_count, 3, HEADS, HEAD)
    scores = jnp.where(
        same_image(tok_count),
        jnp.einsum(
            "thd,shd->hts", heads[:, 0], heads[:, 1], preferred_element_type=jnp.float32
        )
        * score_scale,
        -jnp.inf,
    )
    row_top = jnp.max(scores, axis=-1, keepdims=True)
    scores_exp = jnp.exp(scores - row_top)
    row_total = jnp.sum(scores_exp, axis=-1, keepdims=True)
    soft_scores = scores_exp / row_total
    log_total = row_top + jnp.log(row_total)
    mixed_heads = jnp.einsum(
        "hts,shd->thd",
        soft_scores.astype(jnp.bfloat16),
        heads[:, 2],
        preferred_element_type=jnp.float32,
    )
    mixed_heads = mixed_heads.astype(jnp.bfloat16).reshape(tok_count, D)
    middle = residual + jnp.dot(mixed_heads, proj_w, preferred_element_type=jnp.float32)
    normed_two = layer_norm(middle, norm_scale[1], norm_shift[1]).astype(jnp.bfloat16)
    gate_probs = jax.nn.softmax(
        jnp.dot(normed_two, router_w, preferred_element_type=jnp.float32), axis=-1
    )
    sending = dot_first(token_hot, normed_two).astype(jnp.bfloat16)
    carry = (residual, normed, heads, log_total, mixed_heads, middle, normed_two, gate_probs)
    return carry, sending


def forward_expert(carry, sending, route_hot, tables, weights, experts, capacity):
    _, _, _, _, _, in_w, out_w = weights
    received = exchange(sending.reshape(experts, capacity, D), "expert")
    row_block = received.reshape(experts * capacity, D)
    hidden_pre = jnp.dot(row_block, in_w[0], preferred_element_type=jnp.float32)
    hidden_act = gelu_tanh(hidden_pre).astype(jnp.bfloat16)
    expert_rows = jnp.dot(hidden_act, out_w[0], preferred_element_type=jnp.float32).astype(
        jnp.bfloat16
    )
    returned = exchange(expert_rows.reshape(experts, capacity, D), "expert")
    return forward_combine(
        carry, returned, row_block, hidden_pre, route_hot, tables, experts, capacity
    )


def forward_combine(carry, returned, row_block, hidden_pre, route_hot, tables, experts, capacity):
    residual, normed, heads, log_total, mixed_heads, middle, normed_two, gate_probs = carry
    pair_hot, _, kept_mask = tables
    tok_count = residual.shape[0]
    pair_rows = jnp.dot(
        pair_hot, returned.reshape(experts * capacity, D), preferred_element_type=jnp.float32
    ).reshape(TOP, tok_count, D)
    chosen = jnp.sum(route_hot * gate_probs[:, None, :], axis=-1)
    kept_gate = kept_mask.astype(jnp.float32).reshape(TOP, tok_count)
    weight_pair = kept_gate * chosen.T
    combined = jnp.sum(weight_pair[..., None] * pair_rows, axis=0)
    output = middle + combined
    saved_state = (
        residual,
        normed,
        heads,
        log_total,
        mixed_heads,
        middle,
        normed_two,
        gate_probs,
        kept_gate,
        weight_pair,
        pair_rows,
        row_block,
        hidden_pre,
    )
    return (output, saved_state)


def backward_layer(d_output, saved_state, route_hot, tables, weights, experts, capacity):
    (_, _, _, _, _, _, _, _, _, _, _, row_block, hidden_pre) = saved_state
    _, _, _, _, router_w, in_w, out_w = weights
    d_slots, g_router, d_normed_two = backward_route(
        d_output, saved_state, tables, route_hot, router_w, experts, capacity
    )
    d_expert_out = exchange(d_slots, "expert")
    flat_out = d_expert_out.reshape(experts * capacity, D)
    hidden_act = gelu_tanh(hidden_pre).astype(jnp.bfloat16)
    g_out = dot_first(hidden_act, flat_out)
    d_act = dot_last(flat_out, out_w[0])
    d_pre = jax.vjp(gelu_tanh, hidden_pre)[1](d_act)[0].astype(jnp.bfloat16)
    g_in = dot_first(row_block, d_pre)
    d_rows = dot_last(d_pre, in_w[0]).astype(jnp.bfloat16).reshape(experts, capacity, D)
    d_back = exchange(d_rows, "expert")
    d_residual, grads = backward_attend(
        d_output, saved_state, d_back, d_normed_two, tables, weights, experts, capacity
    )
    g_gain, g_shift, g_qkv, g_proj = grads
    return (d_residual, (g_gain, g_shift, g_qkv, g_proj, g_router, g_in[None], g_out[None]))


def backward_route(d_output, saved_state, tables, route_hot, router_w, experts, capacity):
    (
        residual, _, _, _, _, _, normed_two, gate_probs, kept_gate, weight_pair, pair_rows, _, _
    ) = saved_state
    pair_hot, _, _ = tables
    tok_count = residual.shape[0]
    d_gate_pair = kept_gate * jnp.sum(d_output[None] * pair_rows, axis=-1)
    d_gates = jnp.sum(route_hot * d_gate_pair.T[:, :, None], axis=1)
    d_logits = (
        gate_probs * (d_gates - jnp.sum(gate_probs * d_gates, axis=-1, keepdims=True))
    ).astype(jnp.bfloat16)
    g_router = dot_first(normed_two, d_logits)
    d_normed_two = dot_last(d_logits, router_w)
    d_pairs = (
        (weight_pair[:, :, None] * d_output[None]).astype(jnp.bfloat16).reshape(TOP * tok_count, D)
    )
    d_slots = dot_first(pair_hot, d_pairs).astype(jnp.bfloat16).reshape(experts, capacity, D)
    return d_slots, g_router, d_normed_two


def backward_attend(d_output, saved_state, d_back, d_normed_two, tables, weights, experts, capacity):
    (residual, normed, heads, log_total, mixed_heads, middle, _, _, _, _, _, _, _) = saved_state
    pair_hot, _, _ = tables
    norm_gains, norm_shifts, qkv_w, proj_w, _, _, _ = weights
    tok_count = residual.shape[0]
    score_scale = HEAD ** (-0.5)
    norm_scale = norm_gains.astype(jnp.float32)
    norm_shift = norm_shifts.astype(jnp.float32)
    d_pair_in = jnp.dot(
        pair_hot, d_back.reshape(experts * capacity, D), preferred_element_type=jnp.float32
    ).reshape(TOP, tok_count, D)
    d_normed_two = d_normed_two + jnp.sum(d_pair_in, axis=0)
    pulled_two = jax.vjp(layer_norm, middle, norm_scale[1], norm_shift[1])[1](d_normed_two)
    d_middle = d_output + pulled_two[0]
    d_branch = d_middle.astype(jnp.bfloat16)
    g_proj = dot_first(mixed_heads, d_branch)
    d_mixed = dot_last(d_branch, proj_w).astype(jnp.bfloat16).reshape(tok_count, HEADS, HEAD)
    query_heads = heads[:, 0]
    key_heads = heads[:, 1]
    value_heads = heads[:, 2]
    scores = jnp.where(
        same_image(tok_count),
        jnp.einsum("thd,shd->hts", query_heads, key_heads, preferred_element_type=jnp.float32)
        * score_scale,
        -jnp.inf,
    )
    soft_scores = jnp.exp(scores - log_total)
    d_soft = jnp.einsum("thd,shd->hts", d_mixed, value_heads, preferred_element_type=jnp.float32)
    d_values = jnp.einsum(
        "hts,thd->shd",
        soft_scores.astype(jnp.bfloat16),
        d_mixed,
        preferred_element_type=jnp.float32,
    )
    d_scores = (
        soft_scores * (d_soft - jnp.sum(soft_scores * d_soft, axis=-1, keepdims=True))
    ).astype(jnp.bfloat16)
    d_query = (
        jnp.einsum("hts,shd->thd", d_scores, key_heads, preferred_element_type=jnp.float32)
        * score_scale
    )
    d_keys = (
        jnp.einsum("hts,thd->shd", d_scores, query_heads, preferred_element_type=jnp.float32)
        * score_scale
    )
    d_qkv = (
        jnp.stack([d_query, d_keys, d_values], axis=1)
        .reshape(tok_count, 3 * D)
        .astype(jnp.bfloat16)
    )
    g_qkv = dot_first(normed, d_qkv)
    d_normed = dot_last(d_qkv, qkv_w)
    pulled_one = jax.vjp(layer_norm, residual, norm_scale[0], norm_shift[0])[1](d_normed)
    d_residual = d_middle + pulled_one[0]
    g_gain = jnp.stack([pulled_one[1], pulled_two[1]])
    g_shift = jnp.stack([pulled_one[2], pulled_two[2]])
    return d_residual, (g_gain, g_shift, g_qkv, g_proj)


def halving_scatter(grad, axis_name):
    size = lax.axis_size(axis_name)
    me = lax.axis_index(axis_name)
    chunk = grad.shape[0] // size
    rest = grad.shape[1:]
    total = grad.reshape(size, chunk, *rest)
    bit = 1
    while bit < size:
        pairs = total.reshape(total.shape[0] // 2, 2, chunk, *rest)
        mine = (me // bit) % 2
        keep = lax.dynamic_index_in_dim(pairs, mine, axis=1, keepdims=False)
        give = lax.dynamic_index_in_dim(pairs, 1 - mine, axis=1, keepdims=False)
        got = lax.ppermute(
            give.astype(jnp.bfloat16), axis_name, [(i, i ^ bit) for i in range(size)]
        )
        total = keep.astype(jnp.float32) + got.astype(jnp.float32)
        bit *= 2
    return total.reshape(chunk, *rest)


def doubling_gather(part, axis_name):
    size = lax.axis_size(axis_name)
    me = lax.axis_index(axis_name)
    held = part[None]
    bit = size // 2
    steps = 0
    while bit >= 1:
        got = lax.ppermute(held, axis_name, [(i, i ^ bit) for i in range(size)])
        low = (me // bit) % 2 == 0
        held = jnp.where(low, jnp.concatenate([held, got]), jnp.concatenate([got, held]))
        bit //= 2
        steps += 1
    held = held.reshape((2,) * steps + part.shape)
    held = held.transpose(tuple(reversed(range(steps))) + tuple(range(steps, held.ndim)))
    return held.reshape((size * part.shape[0],) + part.shape[1:])


def expert_sum(part):
    owned = halving_scatter(part, "expert")
    owned = lax.reduce_precision(owned, exponent_bits=8, mantissa_bits=7)
    return doubling_gather(owned.astype(jnp.bfloat16), "expert").astype(jnp.float32)


def reduce_layer(layer_grads, late):
    g_gain, g_shift, g_qkv, g_proj, g_router, g_in, g_out = layer_grads
    qkv_cols = g_qkv.shape[1]
    proj_cols = g_proj.shape[1]
    small = jnp.concatenate([g_gain.T, g_shift.T, g_router], axis=1)
    if late:
        early = jnp.concatenate([g_proj, small], axis=1).astype(jnp.bfloat16)
        early = expert_sum(halving_scatter(early, "shard"))
        qkv = expert_sum(halving_scatter(g_qkv.astype(jnp.bfloat16), "shard"))
        proj = early[:, :proj_cols]
        tail = early[:, proj_cols:]
    else:
        shared = jnp.concatenate([g_qkv, g_proj, small], axis=1)
        shared = halving_scatter(shared, "shard")
        shared = lax.psum(shared.astype(jnp.bfloat16), "expert").astype(jnp.float32)
        qkv = shared[:, :qkv_cols]
        proj = shared[:, qkv_cols : qkv_cols + proj_cols]
        tail = shared[:, qkv_cols + proj_cols :]
    return [
        tail[:, 0:2].T,
        tail[:, 2:4].T,
        qkv,
        proj,
        tail[:, 4:],
        halving_scatter(g_in[0], "shard")[None],
        halving_scatter(g_out[0], "shard")[None],
    ]


def local(
    tokens,
    routes,
    priority,
    norm_gain,
    norm_bias,
    w_qkv,
    w_proj,
    w_router,
    exp_in,
    exp_out,
    cotangent,
):
    experts = lax.axis_size("expert") * EXP_DEV
    capacity = max(8, (5 * TOK_MB // (2 * experts) + 7) // 8 * 8)
    tok_count = tokens.shape[0]
    blocks = tok_count // TOK_MB
    streams = []
    for block in range(blocks):
        rows = slice(block * TOK_MB, (block + 1) * TOK_MB)
        route_ids = routes[rows]
        tables = slot_onehot(route_ids, priority[rows], experts, capacity)
        route_hot = (
            route_ids[..., None] == jnp.arange(experts, dtype=jnp.int32)
        ).astype(jnp.float32)
        streams.append((rows, tables, route_hot))
    layer_count = norm_gain.shape[0]
    small = jnp.concatenate(
        [
            norm_gain.reshape(layer_count * 2, -1).T,
            norm_bias.reshape(layer_count * 2, -1).T,
            w_router.transpose(1, 0, 2).reshape(w_router.shape[1], -1),
        ],
        axis=1,
    )
    qkv_cols = w_qkv.shape[2]
    attn_cols = qkv_cols + w_proj.shape[2]
    all_weights = []
    for layer_index in range(LAYERS):
        parts = [w_qkv[layer_index], w_proj[layer_index]] + ([small] if layer_index == 0 else [])
        attn = lax.all_gather(jnp.concatenate(parts, axis=1), "shard", axis=0, tiled=True)
        if layer_index == 0:
            small = attn[:, attn_cols:]
        shift_at = 2 * layer_count + 2 * layer_index
        router_at = 4 * layer_count + experts * layer_index
        all_weights.append(
            (
                small[:, 2 * layer_index : 2 * layer_index + 2].T,
                small[:, shift_at : shift_at + 2].T,
                attn[:, :qkv_cols],
                attn[:, qkv_cols:attn_cols],
                small[:, router_at : router_at + experts],
                lax.all_gather(exp_in[layer_index], "shard", axis=1, tiled=True),
                lax.all_gather(exp_out[layer_index], "shard", axis=1, tiled=True),
            )
        )
    residuals = [tokens[rows] for rows, _, _ in streams]
    saved = [[None] * LAYERS for _ in streams]
    for layer_index in range(LAYERS):
        staged = []
        for block, (rows, tables, route_hot) in enumerate(streams):
            attn_weights, own_rows = lax.optimization_barrier(
                (all_weights[layer_index][:5], residuals[block])
            )
            own_weights = tuple(attn_weights) + tuple(all_weights[layer_index][5:])
            staged.append(forward_attend(own_rows, tables, own_weights))
        for block, (rows, tables, route_hot) in enumerate(streams):
            carry, sending = staged[block]
            residuals[block], saved[block][layer_index] = forward_expert(
                carry, sending, route_hot, tables, all_weights[layer_index], experts, capacity
            )
    activations = jnp.concatenate(residuals, axis=0)
    d_residuals = [cotangent[rows] for rows, _, _ in streams]
    reduced = [None] * LAYERS
    for layer_index in reversed(range(LAYERS)):
        layer_sum = None
        for block, (rows, tables, route_hot) in enumerate(streams):
            d_residuals[block], layer_grads = backward_layer(
                d_residuals[block],
                saved[block][layer_index],
                route_hot,
                tables,
                all_weights[layer_index],
                experts,
                capacity,
            )
            if layer_sum is None:
                layer_sum = layer_grads
            else:
                layer_sum = tuple(old + new for old, new in zip(layer_sum, layer_grads))
        if layer_index == 0:
            reduced[layer_index] = reduce_layer(layer_sum, True)
        else:
            reduced[layer_index] = reduce_layer(layer_sum, False)
    outs = [jnp.stack([reduced[l][k] for l in range(LAYERS)]) for k in range(7)]
    d_tokens = jnp.concatenate(d_residuals, axis=0)
    return (activations, d_tokens, *outs)


def solution(mesh):
    return jax.shard_map(
        local,
        mesh=mesh,
        in_specs=(
            P(("expert", "shard"), None),
            P(("expert", "shard"), None),
            P(("expert", "shard")),
            P(None, None, "shard"),
            P(None, None, "shard"),
            P(None, "shard", None),
            P(None, "shard", None),
            P(None, "shard", None),
            P(None, "expert", "shard", None),
            P(None, "expert", "shard", None),
            P(("expert", "shard"), None),
        ),
        out_specs=(
            P(("expert", "shard"), None),
            P(("expert", "shard"), None),
            P(None, None, "shard"),
            P(None, None, "shard"),
            P(None, "shard", None),
            P(None, "shard", None),
            P(None, "shard", None),
            P(None, "expert", "shard", None),
            P(None, "expert", "shard", None),
        ),
        check_vma=False,
    )
```
